32 devices in a mesh: groups: 2 (over x), dom: 16 (over z, y, core).
Axes of the slice: x: 2, y: 2, z: 4, core: 2. Of those that a mesh axis runs over, the one named last changes fastest.
Arguments:
- image: bfloat16 [32, 64, 128, 128], P(('groups', 'dom')), parts along dimension 0, may hold values from -16 to 16
- adjoint_data: bfloat16 [32, 64, 128, 128], P(('groups', 'dom')), parts along dimension 0, may hold values from -8 to 8
- coil_maps: bfloat16 [32, 16, 128, 128], P(('groups', 'dom')), parts along dimension 0, may hold values from -1 to 1
- spoke_counts: int32 [32, 64], P(('groups', 'dom')), parts along dimension 0, may hold values from 1 to 6, as said below
- tile_map: int32 [32, 64, 6, 5, 2], P(('groups', 'dom')), parts along dimension 0, may hold values from 0 to 127
- blocks: bfloat16 [5, 2, 128, 128], replicated, may hold values from -0.39648438 to 0.39648438
- z_kernel: bfloat16 [3, 2, 64, 64], replicated, may hold values from -0.3125 to 0.3125
- rank_cap: int32 [1], replicated, may hold values from 2 to 32
Outputs:
- image_next: bfloat16 [32, 64, 128, 128], P(('groups', 'dom')), parts along dimension 0
The draws below stay inside these ranges and needn't reach their ends.
There are 2 independent parts, one for each index of `groups`. The reference program is written for one: setup_inputs(seed, part) draws one part's arguments, and reference() takes and returns one part's arrays. A program takes and returns all parts, laid end to end along the dimension named above; an argument that names none is the same for every part. Nothing has to cross between parts.
Inputs may be any that keep to these rules, and one draw needn't show every extreme that they name: `spoke_counts`: partitions less than 2 away from partition 16 // 2 take 6 - 1 or 6 spokes in every frame, all others 1 or 2; partition 16 // 2 takes 6 spokes in some frame.
All inputs are finite; a program needn't handle non-finite values.
Results may differ from the reference program's by a relative error of at most 0.0055.
Values may be sent and summed in bfloat16 or wider, within the bound.
No kernel may reach another device: no remote copies, remote signals or barrier semaphores. Data moves between devices by JAX's collectives and lax.ppermute only.
A program may use at most 128 MiB of HBM per device.

```python
import jax
import jax.numpy as jnp
from jax import lax

FR = 64
C = 16
PIX = 64
TILES = 128
SPT = 5
NNZ = 2
SMAX = 6
NZ = 16


def signal_field(key, salt_value):
    shared_keys = jax.random.split(jax.random.fold_in(key, 55), 5)
    own_keys = jax.random.split(jax.random.fold_in(key, salt_value), 4)
    comp_count = 8
    decay_rate = 0.72
    frame_pos = jnp.arange(FR, dtype=jnp.float32) / FR
    frequencies = jax.random.uniform(shared_keys[0], (comp_count,), jnp.float32, 0.3, 3.0)
    phases = jax.random.uniform(shared_keys[1], (comp_count,), jnp.float32, -jnp.pi, jnp.pi)
    slopes = jax.random.uniform(shared_keys[2], (comp_count,), jnp.float32, -2.0, 2.0)
    angle_values = 2.0 * jnp.pi * frequencies[:, None] * frame_pos[None, :] + phases[:, None]
    basis_real = jnp.cos(angle_values)
    basis_imag = jnp.sin(angle_values)
    frame_scale = jnp.exp(jax.random.uniform(shared_keys[4], (FR,), jnp.float32, -0.7, 0.7))
    ramp_values = jnp.arange(NZ, dtype=jnp.float32) / max(NZ - 1, 1)
    comp_weight = jnp.power(decay_rate, jnp.arange(comp_count, dtype=jnp.float32))
    jitter = jnp.exp(jax.random.uniform(own_keys[0], (comp_count, NZ), jnp.float32, -0.5, 0.5))
    plane_weight = comp_weight[:, None] * jnp.exp(slopes[:, None] * (ramp_values[None, :] - 0.5)) * jitter
    weight_norm = jnp.sqrt(jnp.sum(comp_weight * comp_weight))
    map_shape = (comp_count, NZ, TILES, PIX)
    noise_shape = (NZ, FR, TILES, 2 * PIX)
    map_real = jax.random.normal(own_keys[1], map_shape, jnp.float32)
    map_imag = jax.random.normal(own_keys[2], map_shape, jnp.float32)
    noise_field = jax.random.normal(own_keys[3], noise_shape, jnp.float32)
    field_real = jnp.zeros((NZ, FR, TILES, PIX), jnp.float32)
    field_imag = jnp.zeros((NZ, FR, TILES, PIX), jnp.float32)
    for comp_index in range(comp_count):
        scaled_real = plane_weight[comp_index][:, None, None, None] * map_real[comp_index][:, None, :, :]
        scaled_imag = plane_weight[comp_index][:, None, None, None] * map_imag[comp_index][:, None, :, :]
        time_real = basis_real[comp_index][None, :, None, None]
        time_imag = basis_imag[comp_index][None, :, None, None]
        field_real = field_real + scaled_real * time_real - scaled_imag * time_imag
        field_imag = field_imag + scaled_real * time_imag + scaled_imag * time_real
    signal = jnp.concatenate([field_real, field_imag], axis=-1) / weight_norm
    field_values = signal + 0.2 * noise_field
    plane_scale = 0.45 * jnp.power(10.0, 0.5 * ramp_values) * jnp.exp(jax.random.uniform(jax.random.fold_in(own_keys[0], 7), (NZ,), jnp.float32, -0.3, 0.3))
    field_values = field_values * plane_scale[:, None, None, None] * frame_scale[None, :, None, None]
    return jnp.clip(field_values, -16.0, 16.0)


def draw_image(key, part):
    return signal_field(key, 101).astype(jnp.bfloat16)


def draw_adjoint_data(key, part):
    return (0.5 * signal_field(key, 202)).astype(jnp.bfloat16)


def draw_coil_maps(key, part):
    subkeys = jax.random.split(jax.random.fold_in(key, 404), 2)
    common_shape = (NZ, 1, TILES, 2 * PIX)
    own_shape = (NZ, C, TILES, 2 * PIX)
    common_part = jax.random.normal(subkeys[0], common_shape, jnp.float32)
    own_part = jax.random.normal(subkeys[1], own_shape, jnp.float32)
    return jnp.clip(0.13 * (common_part + own_part), -1.0, 1.0).astype(jnp.bfloat16)


def draw_spoke_counts(key, part):
    subkeys = jax.random.split(jax.random.fold_in(key, 303), 3)
    plane_ids = jnp.arange(NZ, dtype=jnp.int32)[:, None]
    distance = jnp.abs(plane_ids - NZ // 2)
    centre = distance < NZ // 8
    heavy = SMAX - jax.random.randint(subkeys[0], (NZ, FR), 0, 2)
    light = jax.random.randint(subkeys[1], (NZ, FR), 1, 3)
    counts = jnp.where(centre, heavy, light)
    chosen_frame = jax.random.randint(subkeys[2], (), 0, FR)
    counts = counts.at[NZ // 2, chosen_frame].set(SMAX)
    return counts.astype(jnp.int32)


def touch_ends(result, own_key, smallest, high):
    extent = result.shape
    index_at = [jax.random.randint(jax.random.fold_in(own_key, axis), (), 0, extent[axis]) for axis in range(len(extent))]
    result = result.at[tuple(index_at)].set(smallest)
    longest = extent.index(max(extent))
    index_at[longest] = (index_at[longest] + 1) % extent[longest]
    return result.at[tuple(index_at)].set(high)


def noise(key, extent, deviation, most, held_as=jnp.bfloat16):
    return jnp.clip(deviation * jax.random.normal(key, extent, jnp.float32), -most, most).astype(held_as)


def setup_inputs(seed: int = 0, part: int = 0) -> dict:
    key_of = jax.random.split(jax.random.key(seed), 9)
    part_splits = jax.random.split(jax.random.fold_in(key_of[8], part), 9)
    image = draw_image(jax.random.fold_in(jax.random.fold_in(key_of[8], part), 71), part)
    adjoint_data = draw_adjoint_data(jax.random.fold_in(jax.random.fold_in(key_of[8], part), 71), part)
    coil_maps = draw_coil_maps(jax.random.fold_in(jax.random.fold_in(key_of[8], part), 71), part)
    spoke_counts = draw_spoke_counts(jax.random.fold_in(jax.random.fold_in(key_of[8], part), 71), part)
    tile_map = touch_ends(jax.random.randint(part_splits[4], (NZ, FR, SMAX, SPT, NNZ), 0, TILES), jax.random.fold_in(part_splits[4], 1), 0, TILES - 1).astype(jnp.int32)
    blocks = noise(key_of[5], (SPT, NNZ, 2 * PIX, 2 * PIX), (1.13 * (2 * PIX) ** -0.5), 0.39648438)
    z_kernel = noise(key_of[6], (3, 2, FR, FR), (6 * FR) ** -0.5, 0.3125)
    rank_cap = jax.random.randint(key_of[7], (1,), 2, 33).astype(jnp.int32)
    return {"image": image, "adjoint_data": adjoint_data, "coil_maps": coil_maps, "spoke_counts": spoke_counts, "tile_map": tile_map, "blocks": blocks, "z_kernel": z_kernel, "rank_cap": rank_cap}


SOFT_CUT = 0.25

def rotate(field_values):
    half_width = field_values.shape[-1] // 2
    return jnp.concatenate([-field_values[..., half_width:], field_values[..., :half_width]], axis=-1)

def complex_times(left_value, right_value):
    half_width = left_value.shape[-1] // 2
    left_real, left_imag = (left_value[..., :half_width], left_value[..., half_width:])
    right_real, right_imag = (right_value[..., :half_width], right_value[..., half_width:])
    return jnp.concatenate([left_real * right_real - left_imag * right_imag, left_real * right_imag + left_imag * right_real], axis=-1)

def conj_times(left_value, right_value):
    half_width = left_value.shape[-1] // 2
    left_real, left_imag = (left_value[..., :half_width], left_value[..., half_width:])
    right_real, right_imag = (right_value[..., :half_width], right_value[..., half_width:])
    return jnp.concatenate([left_real * right_real + left_imag * right_imag, left_real * right_imag - left_imag * right_real], axis=-1)

def round_keep(values):
    held = lax.optimization_barrier(values.astype(jnp.bfloat16))
    return held.astype(jnp.float32)

def partition_gradient(inputs, blocks_wide):
    image_plane, plane_maps, counts, plane_map = inputs
    frame_count, tile_count, lane_width = image_plane.shape
    image_wide = image_plane.astype(jnp.float32)
    maps_wide = plane_maps.astype(jnp.float32)
    frame_ids = jnp.arange(frame_count, dtype=jnp.int32)[:, None, None]
    accum = jnp.zeros((frame_count * tile_count, lane_width), jnp.float32)
    for spoke_slot in range(SMAX):
        tile_index = plane_map[:, spoke_slot]
        image_picked = image_wide[frame_ids, tile_index]
        maps_picked = maps_wide[:, tile_index]
        coil_tiles = round_keep(complex_times(maps_picked, image_picked[None]))
        samples = jnp.einsum('ctqji,qjio->ctqo', coil_tiles, blocks_wide)
        live_mask = (counts > spoke_slot).astype(jnp.float32)[None, :, None, None]
        samples = round_keep(samples * live_mask)
        spread = jnp.einsum('ctqo,qjio->ctqji', samples, blocks_wide)
        back_sum = lax.optimization_barrier(jnp.sum(conj_times(maps_picked, spread), axis=0))
        flat_index = (frame_ids * tile_count + tile_index).reshape(-1).astype(jnp.int32)
        accum = accum.at[flat_index].add(back_sum.reshape(-1, lane_width))
    return accum.reshape(frame_count, tile_count, lane_width)

def apply_frames(mix_real, mix_imag, field_values):
    wide_field = field_values.astype(jnp.float32)
    direct = jnp.einsum('fg,zftw->zgtw', mix_real.astype(jnp.float32), wide_field)
    turned = jnp.einsum('fg,zftw->zgtw', mix_imag.astype(jnp.float32), rotate(wide_field))
    return direct + turned

def soft_shrink(filtered):
    half_width = filtered.shape[-1] // 2
    real_part, imag_part = (filtered[..., :half_width], filtered[..., half_width:])
    magnitude = jnp.sqrt(real_part * real_part + imag_part * imag_part)
    scale_values = jnp.maximum(magnitude - SOFT_CUT, 0.0) / jnp.maximum(magnitude, SOFT_CUT)
    return filtered * jnp.concatenate([scale_values, scale_values], axis=-1)

def reference(image, adjoint_data, coil_maps, spoke_counts, tile_map, blocks, z_kernel, rank_cap):
    blocks_wide = blocks.astype(jnp.float32)
    gradient = lax.map(lambda inputs: partition_gradient(inputs, blocks_wide), (image, coil_maps, spoke_counts, tile_map))
    fresh = (image.astype(jnp.float32) - (gradient - adjoint_data.astype(jnp.float32))).astype(jnp.bfloat16)
    rows_real = jnp.moveaxis(fresh, 1, 0).reshape(FR, -1)
    rows_turned = jnp.moveaxis(rotate(fresh), 1, 0).reshape(FR, -1)
    gram_real = jnp.dot(rows_real.astype(jnp.float32), rows_real.T.astype(jnp.float32), preferred_element_type=jnp.float32)
    gram_imag = jnp.dot(rows_turned.astype(jnp.float32), rows_real.T.astype(jnp.float32), preferred_element_type=jnp.float32)
    threshold_sq = jnp.trace(gram_real) / rank_cap[0].astype(jnp.float32)
    stacked = jnp.block([[gram_real, -gram_imag], [gram_imag, gram_real]])
    unit_matrix = jnp.eye(2 * FR, dtype=jnp.float32)
    chol_factor = jnp.linalg.cholesky(stacked + threshold_sq * unit_matrix)
    shrink = jax.scipy.linalg.cho_solve((chol_factor, True), stacked)
    shrink_real = shrink[:FR, :FR].astype(jnp.bfloat16)
    shrink_imag = shrink[FR:, :FR].astype(jnp.bfloat16)
    low_rank = apply_frames(shrink_real, shrink_imag, fresh)
    remainder = (fresh.astype(jnp.float32) - low_rank).astype(jnp.bfloat16)
    padded = jnp.pad(remainder, ((1, 1), (0, 0), (0, 0), (0, 0)))
    filtered = apply_frames(z_kernel[0, 0], z_kernel[0, 1], padded[0:NZ])
    for offset in range(1, 3):
        filtered = filtered + apply_frames(z_kernel[offset, 0], z_kernel[offset, 1], padded[offset:offset + NZ])
    sparse = soft_shrink(filtered)
    return (low_rank + sparse).astype(jnp.bfloat16)
```

```python
import jax
import jax.numpy as jnp
from jax import lax
from jax.sharding import PartitionSpec as P
import functools
from jax.experimental import pallas as pl
from jax.experimental.pallas import tpu as pltpu

SOFT_CUT = 0.25


def padded_2(block, sides, width):
    for axis, dim in sides:
        count = lax.axis_size(axis)
        forward = [(i, i + 1) for i in range(count - 1)]
        backward = [(target, source) for source, target in forward]
        low = lax.ppermute(
            lax.slice_in_dim(block, block.shape[dim] - width, None, axis=dim), axis, forward
        )
        high = lax.ppermute(lax.slice_in_dim(block, 0, width, axis=dim), axis, backward)
        block = jnp.concatenate([low, block, high], axis=dim)
    return block


def rotate(field_values):
    half_width = field_values.shape[-1] // 2
    return jnp.concatenate(
        [-field_values[..., half_width:], field_values[..., :half_width]], axis=-1
    )


def complex_times(left_value, right_value):
    half_width = left_value.shape[-1] // 2
    left_real, left_imag = (left_value[..., :half_width], left_value[..., half_width:])
    right_real, right_imag = (right_value[..., :half_width], right_value[..., half_width:])
    return jnp.concatenate(
        [
            left_real * right_real - left_imag * right_imag,
            left_real * right_imag + left_imag * right_real,
        ],
        axis=-1,
    )


def conj_times(left_value, right_value):
    half_width = left_value.shape[-1] // 2
    left_real, left_imag = (left_value[..., :half_width], left_value[..., half_width:])
    right_real, right_imag = (right_value[..., :half_width], right_value[..., half_width:])
    return jnp.concatenate(
        [
            left_real * right_real + left_imag * right_imag,
            left_real * right_imag - left_imag * right_real,
        ],
        axis=-1,
    )


def grid_gradient(image_plane, plane_maps, counts, plane_map, blocks):
    frame_count, tile_count, lane_width = image_plane.shape
    read_tiles, link_count = (plane_map.shape[2], plane_map.shape[3])
    coil_count = plane_maps.shape[0]
    tile_ids = jnp.arange(tile_count, dtype=jnp.int32)

    def one_slot(spoke_slot, accum):
        tile_index = lax.dynamic_index_in_dim(plane_map, spoke_slot, axis=1, keepdims=False)
        flat_index = tile_index.reshape(frame_count, read_tiles * link_count)
        image_picked = jnp.take_along_axis(image_plane, flat_index[:, :, None], axis=1)
        image_picked = image_picked.reshape(frame_count, read_tiles, link_count, lane_width)
        maps_picked = jnp.take(plane_maps, flat_index.reshape(-1), axis=1)
        maps_picked = maps_picked.reshape(
            coil_count, frame_count, read_tiles, link_count, lane_width
        ).astype(jnp.float32)
        coil_tiles = complex_times(maps_picked, image_picked.astype(jnp.float32)[None]).astype(
            jnp.bfloat16
        )
        samples = jnp.einsum(
            "ctqji,qjio->ctqo", coil_tiles, blocks, preferred_element_type=jnp.float32
        )
        live_mask = (counts > spoke_slot).astype(jnp.float32)[None, :, None, None]
        samples = (samples * live_mask).astype(jnp.bfloat16)
        spread = jnp.einsum("ctqo,qjio->ctqji", samples, blocks, preferred_element_type=jnp.float32)
        back_sum = jnp.sum(conj_times(maps_picked, spread), axis=0)
        back_sum = back_sum.reshape(frame_count, read_tiles * link_count, lane_width)
        onehot = (flat_index[:, :, None] == tile_ids).astype(jnp.float32)
        return accum + jnp.einsum("tkn,tkw->tnw", onehot, back_sum, precision=lax.Precision.HIGHEST)

    most_spokes = jnp.max(counts)
    start_value = jnp.zeros((frame_count, tile_count, lane_width), jnp.float32)
    return lax.fori_loop(0, most_spokes, one_slot, start_value)


def gradient_kernel(idx_ref, cnt_ref, nsl_ref, img_ref, adj_ref, mrr_ref, mii_ref,
                    bf_ref, bt_ref, btr_ref, out_ref, x_scr, rx_scr, g_scr,
                    lhs_scr, y_scr, ry_scr, *, fb, slots, links, coils):
    b = pl.program_id(0)
    reads = links // 2
    img = img_ref[...].astype(jnp.float32)
    x_scr[...] = img
    half = img.shape[-1] // 2
    lane = lax.broadcasted_iota(jnp.int32, img.shape, 2)
    sign = jnp.where(lane < half, -1.0, 1.0).astype(jnp.float32)
    rx_scr[...] = pltpu.roll(img, half, 2) * sign
    g_scr[...] = jnp.zeros_like(g_scr)
    lhs_scr[...] = jnp.zeros_like(lhs_scr)

    def slot_body(s, carry):
        for q in range(reads):
            def gather_t(t, c):
                frame = b * fb + t
                live = cnt_ref[frame] > s
                base = (frame * slots + s) * links + q * 2
                row = pl.multiple_of(t * coils, coils)

                @pl.when(live)
                def _():
                    for j in range(2):
                        p = idx_ref[base + j]
                        xv = x_scr[t, pl.ds(p, 1), :]
                        rxv = rx_scr[t, pl.ds(p, 1), :]
                        ct = mrr_ref[p] * xv + mii_ref[p] * rxv
                        lhs_scr[pl.ds(row, coils), pl.ds(j * 128, 128)] = ct.astype(jnp.bfloat16)
                return c

            lax.fori_loop(0, fb, gather_t, 0)
            samples = jnp.dot(lhs_scr[...], bf_ref[q], preferred_element_type=jnp.float32)
            samples = samples.astype(jnp.bfloat16)
            y_scr[...] = jnp.dot(samples, bt_ref[q], preferred_element_type=jnp.float32)
            ry_scr[...] = jnp.dot(samples, btr_ref[q], preferred_element_type=jnp.float32)

            def scatter_t(t, c):
                frame = b * fb + t
                live = cnt_ref[frame] > s
                base = (frame * slots + s) * links + q * 2
                row = pl.multiple_of(t * coils, coils)

                @pl.when(live)
                def _():
                    for j in range(2):
                        p = idx_ref[base + j]
                        yv = y_scr[pl.ds(row, coils), pl.ds(j * 128, 128)]
                        ryv = ry_scr[pl.ds(row, coils), pl.ds(j * 128, 128)]
                        v = mrr_ref[p] * yv - mii_ref[p] * ryv
                        back = jnp.sum(v, axis=0, keepdims=True)
                        g_scr[t, pl.ds(p, 1), :] = g_scr[t, pl.ds(p, 1), :] + back
                return c

            lax.fori_loop(0, fb, scatter_t, 0)
        return carry

    lax.fori_loop(0, nsl_ref[b], slot_body, 0)
    out_ref[...] = (x_scr[...] - (g_scr[...] - adj_ref[...].astype(jnp.float32))).astype(out_ref.dtype)


def fresh_image_of(image_plane, adjoint_plane, plane_maps, counts, plane_map, blocks):
    frame_count, tile_count, lane_width = image_plane.shape
    slots, reads, links = plane_map.shape[1], plane_map.shape[2], plane_map.shape[3]
    coils = plane_maps.shape[0]
    fb = 16 if frame_count % 16 == 0 else frame_count
    nblocks = frame_count // fb
    half = lane_width // 2
    maps_t = jnp.swapaxes(plane_maps.astype(jnp.float32), 0, 1)
    mrr = jnp.concatenate([maps_t[..., :half], maps_t[..., :half]], axis=-1)
    mii = jnp.concatenate([maps_t[..., half:], maps_t[..., half:]], axis=-1)
    bf = blocks.reshape(reads, links * lane_width, lane_width)
    bt4 = jnp.transpose(blocks, (0, 3, 1, 2))
    bt = bt4.reshape(reads, lane_width, links * lane_width)
    btr = rotate(bt4).reshape(reads, lane_width, links * lane_width)
    idx = plane_map.reshape(-1).astype(jnp.int32)
    cnt = counts.astype(jnp.int32)
    nsl = jnp.minimum(jnp.max(cnt.reshape(nblocks, fb), axis=1), slots).astype(jnp.int32)
    kernel = functools.partial(
        gradient_kernel, fb=fb, slots=slots, links=reads * links, coils=coils
    )
    plane_spec = pl.BlockSpec((fb, tile_count, lane_width), lambda b, *_: (b, 0, 0))
    whole3 = lambda shape: pl.BlockSpec(shape, lambda b, *_: (0, 0, 0))
    flops = 2 * frame_count * slots * reads * coils * (links * lane_width) * lane_width * 3
    return pl.pallas_call(
        kernel,
        out_shape=jax.ShapeDtypeStruct(image_plane.shape, jnp.bfloat16),
        grid_spec=pltpu.PrefetchScalarGridSpec(
            num_scalar_prefetch=3,
            grid=(nblocks,),
            in_specs=[
                plane_spec,
                plane_spec,
                whole3(mrr.shape),
                whole3(mii.shape),
                whole3(bf.shape),
                whole3(bt.shape),
                whole3(btr.shape),
            ],
            out_specs=plane_spec,
            scratch_shapes=[
                pltpu.VMEM((fb, tile_count, lane_width), jnp.float32),
                pltpu.VMEM((fb, tile_count, lane_width), jnp.float32),
                pltpu.VMEM((fb, tile_count, lane_width), jnp.float32),
                pltpu.VMEM((fb * coils, links * lane_width), jnp.bfloat16),
                pltpu.VMEM((fb * coils, links * lane_width), jnp.float32),
                pltpu.VMEM((fb * coils, links * lane_width), jnp.float32),
            ],
        ),
        compiler_params=pltpu.CompilerParams(dimension_semantics=("arbitrary",)),
        cost_estimate=pl.CostEstimate(
            flops=flops, transcendentals=0, bytes_accessed=image_plane.size * 6 + mrr.size * 8
        ),
    )(idx, cnt, nsl, image_plane, adjoint_plane, mrr, mii, bf, bt, btr)


def apply_frames(mix_real, mix_imag, field_values):
    direct = jnp.einsum("fg,zftw->zgtw", mix_real, field_values, preferred_element_type=jnp.float32)
    turned = jnp.einsum(
        "fg,zftw->zgtw", mix_imag, rotate(field_values), preferred_element_type=jnp.float32
    )
    return direct + turned


def soft_shrink(filtered):
    half_width = filtered.shape[-1] // 2
    real_part, imag_part = (filtered[..., :half_width], filtered[..., half_width:])
    magnitude = jnp.sqrt(real_part * real_part + imag_part * imag_part)
    scale_values = jnp.maximum(magnitude - SOFT_CUT, 0.0) / jnp.maximum(magnitude, SOFT_CUT)
    return filtered * jnp.concatenate([scale_values, scale_values], axis=-1)


def local(image, adjoint_data, coil_maps, spoke_counts, tile_map, blocks, z_kernel, rank_cap):
    plane_count = image.shape[0]
    frame_count = image.shape[1]
    fresh_image = fresh_image_of(
        image[0], adjoint_data[0], coil_maps[0], spoke_counts[0], tile_map[0], blocks
    )[None]
    rows_real = jnp.moveaxis(fresh_image, 1, 0).reshape(frame_count, -1)
    rows_turned = jnp.moveaxis(rotate(fresh_image), 1, 0).reshape(frame_count, -1)
    gram_real = jnp.einsum("fn,gn->fg", rows_real, rows_real, preferred_element_type=jnp.float32)
    gram_imag = jnp.einsum("fn,gn->fg", rows_turned, rows_real, preferred_element_type=jnp.float32)
    gram_real, gram_imag = lax.psum((gram_real, gram_imag), "dom")
    stacked = jnp.block([[gram_real, -gram_imag], [gram_imag, gram_real]])
    threshold_sq = jnp.trace(stacked[:frame_count, :frame_count]) / rank_cap[0].astype(jnp.float32)
    unit_matrix = jnp.eye(2 * frame_count, dtype=jnp.float32)
    chol_factor = jnp.linalg.cholesky(stacked + threshold_sq * unit_matrix)
    shrink = jax.scipy.linalg.cho_solve((chol_factor, True), stacked)
    shrink_real = shrink[:frame_count, :frame_count].astype(jnp.bfloat16)
    shrink_imag = shrink[frame_count:, :frame_count].astype(jnp.bfloat16)
    low_part = apply_frames(shrink_real, shrink_imag, fresh_image)
    remainder = (fresh_image.astype(jnp.float32) - low_part).astype(jnp.bfloat16)
    padded = padded_2(remainder, (("dom", 0),), 1)
    filtered = apply_frames(z_kernel[0, 0], z_kernel[0, 1], padded[0:plane_count])
    for offset in range(1, 3):
        filtered = filtered + apply_frames(
            z_kernel[offset, 0], z_kernel[offset, 1], padded[offset : offset + plane_count]
        )
    sparse = soft_shrink(filtered)
    return (low_part + sparse).astype(jnp.bfloat16)


def solution(mesh):
    return jax.shard_map(
        local,
        mesh=mesh,
        in_specs=(
            P(("groups", "dom"), None, None, None),
            P(("groups", "dom"), None, None, None),
            P(("groups", "dom"), None, None, None),
            P(("groups", "dom"), None),
            P(("groups", "dom"), None, None, None, None),
            P(),
            P(),
            P(),
        ),
        out_specs=P(("groups", "dom"), None, None, None),
        check_vma=False,
    )
```

```python
import jax
import jax.numpy as jnp
from jax import lax
from jax.sharding import PartitionSpec as P
import functools
from jax.experimental import pallas as pl
from jax.experimental.pallas import tpu as pltpu

SOFT_CUT = 0.25


def padded_2(block, sides, width):
    for axis, dim in sides:
        count = lax.axis_size(axis)
        forward = [(i, i + 1) for i in range(count - 1)]
        backward = [(target, source) for source, target in forward]
        low = lax.ppermute(
            lax.slice_in_dim(block, block.shape[dim] - width, None, axis=dim), axis, forward
        )
        high = lax.ppermute(lax.slice_in_dim(block, 0, width, axis=dim), axis, backward)
        block = jnp.concatenate([low, block, high], axis=dim)
    return block


def rotate(field_values):
    half_width = field_values.shape[-1] // 2
    return jnp.concatenate(
        [-field_values[..., half_width:], field_values[..., :half_width]], axis=-1
    )


def complex_times(left_value, right_value):
    half_width = left_value.shape[-1] // 2
    left_real, left_imag = (left_value[..., :half_width], left_value[..., half_width:])
    right_real, right_imag = (right_value[..., :half_width], right_value[..., half_width:])
    return jnp.concatenate(
        [
            left_real * right_real - left_imag * right_imag,
            left_real * right_imag + left_imag * right_real,
        ],
        axis=-1,
    )


def conj_times(left_value, right_value):
    half_width = left_value.shape[-1] // 2
    left_real, left_imag = (left_value[..., :half_width], left_value[..., half_width:])
    right_real, right_imag = (right_value[..., :half_width], right_value[..., half_width:])
    return jnp.concatenate(
        [
            left_real * right_real + left_imag * right_imag,
            left_real * right_imag - left_imag * right_real,
        ],
        axis=-1,
    )


def grid_gradient(image_plane, plane_maps, counts, plane_map, blocks):
    frame_count, tile_count, lane_width = image_plane.shape
    read_tiles, link_count = (plane_map.shape[2], plane_map.shape[3])
    coil_count = plane_maps.shape[0]
    tile_ids = jnp.arange(tile_count, dtype=jnp.int32)

    def one_slot(spoke_slot, accum):
        tile_index = lax.dynamic_index_in_dim(plane_map, spoke_slot, axis=1, keepdims=False)
        flat_index = tile_index.reshape(frame_count, read_tiles * link_count)
        image_picked = jnp.take_along_axis(image_plane, flat_index[:, :, None], axis=1)
        image_picked = image_picked.reshape(frame_count, read_tiles, link_count, lane_width)
        maps_picked = jnp.take(plane_maps, flat_index.reshape(-1), axis=1)
        maps_picked = maps_picked.reshape(
            coil_count, frame_count, read_tiles, link_count, lane_width
        ).astype(jnp.float32)
        coil_tiles = complex_times(maps_picked, image_picked.astype(jnp.float32)[None]).astype(
            jnp.bfloat16
        )
        samples = jnp.einsum(
            "ctqji,qjio->ctqo", coil_tiles, blocks, preferred_element_type=jnp.float32
        )
        live_mask = (counts > spoke_slot).astype(jnp.float32)[None, :, None, None]
        samples = (samples * live_mask).astype(jnp.bfloat16)
        spread = jnp.einsum("ctqo,qjio->ctqji", samples, blocks, preferred_element_type=jnp.float32)
        back_sum = jnp.sum(conj_times(maps_picked, spread), axis=0)
        back_sum = back_sum.reshape(frame_count, read_tiles * link_count, lane_width)
        onehot = (flat_index[:, :, None] == tile_ids).astype(jnp.float32)
        return accum + jnp.einsum("tkn,tkw->tnw", onehot, back_sum, precision=lax.Precision.HIGHEST)

    most_spokes = jnp.max(counts)
    start_value = jnp.zeros((frame_count, tile_count, lane_width), jnp.float32)
    return lax.fori_loop(0, most_spokes, one_slot, start_value)


def gradient_kernel(idx_ref, cnt_ref, nsl_ref, img_ref, adj_ref, mrr_ref, mii_ref,
                    bf_ref, bt_ref, btr_ref, out_ref, x_scr, rx_scr, g_scr,
                    lhs_scr, y_scr, ry_scr, *, fb, slots, links, coils):
    b = pl.program_id(0)
    reads = links // 2
    img = img_ref[...].astype(jnp.float32)
    x_scr[...] = img
    half = img.shape[-1] // 2
    lane = lax.broadcasted_iota(jnp.int32, img.shape, 2)
    sign = jnp.where(lane < half, -1.0, 1.0).astype(jnp.float32)
    rx_scr[...] = pltpu.roll(img, half, 2) * sign
    g_scr[...] = jnp.zeros_like(g_scr)
    lhs_scr[...] = jnp.zeros_like(lhs_scr)

    def slot_body(s, carry):
        for q in range(reads):
            def gather_t(t, c):
                frame = b * fb + t
                live = cnt_ref[frame] > s
                base = (frame * slots + s) * links + q * 2
                row = pl.multiple_of(t * coils, coils)

                @pl.when(live)
                def _():
                    for j in range(2):
                        p = idx_ref[base + j]
                        xv = x_scr[t, pl.ds(p, 1), :]
                        rxv = rx_scr[t, pl.ds(p, 1), :]
                        ct = mrr_ref[p] * xv + mii_ref[p] * rxv
                        lhs_scr[pl.ds(row, coils), pl.ds(j * 128, 128)] = ct.astype(jnp.bfloat16)
                return c

            lax.fori_loop(0, fb, gather_t, 0)
            samples = jnp.dot(lhs_scr[...], bf_ref[q], preferred_element_type=jnp.float32)
            samples = samples.astype(jnp.bfloat16)
            y_scr[...] = jnp.dot(samples, bt_ref[q], preferred_element_type=jnp.float32)
            ry_scr[...] = jnp.dot(samples, btr_ref[q], preferred_element_type=jnp.float32)

            def scatter_t(t, c):
                frame = b * fb + t
                live = cnt_ref[frame] > s
                base = (frame * slots + s) * links + q * 2
                row = pl.multiple_of(t * coils, coils)

                @pl.when(live)
                def _():
                    for j in range(2):
                        p = idx_ref[base + j]
                        yv = y_scr[pl.ds(row, coils), pl.ds(j * 128, 128)]
                        ryv = ry_scr[pl.ds(row, coils), pl.ds(j * 128, 128)]
                        v = mrr_ref[p] * yv - mii_ref[p] * ryv
                        back = jnp.sum(v, axis=0, keepdims=True)
                        g_scr[t, pl.ds(p, 1), :] = g_scr[t, pl.ds(p, 1), :] + back
                return c

            lax.fori_loop(0, fb, scatter_t, 0)
        return carry

    lax.fori_loop(0, nsl_ref[b], slot_body, 0)
    out_ref[...] = (x_scr[...] - (g_scr[...] - adj_ref[...].astype(jnp.float32))).astype(out_ref.dtype)


def fresh_image_of(image_plane, adjoint_plane, plane_maps, counts, plane_map, blocks):
    frame_count, tile_count, lane_width = image_plane.shape
    slots, reads, links = plane_map.shape[1], plane_map.shape[2], plane_map.shape[3]
    coils = plane_maps.shape[0]
    fb = 16 if frame_count % 16 == 0 else frame_count
    nblocks = frame_count // fb
    half = lane_width // 2
    maps_t = jnp.swapaxes(plane_maps.astype(jnp.float32), 0, 1)
    mrr = jnp.concatenate([maps_t[..., :half], maps_t[..., :half]], axis=-1)
    mii = jnp.concatenate([maps_t[..., half:], maps_t[..., half:]], axis=-1)
    bf = blocks.reshape(reads, links * lane_width, lane_width)
    bt4 = jnp.transpose(blocks, (0, 3, 1, 2))
    bt = bt4.reshape(reads, lane_width, links * lane_width)
    btr = rotate(bt4).reshape(reads, lane_width, links * lane_width)
    idx = plane_map.reshape(-1).astype(jnp.int32)
    cnt = counts.astype(jnp.int32)
    nsl = jnp.minimum(jnp.max(cnt.reshape(nblocks, fb), axis=1), slots).astype(jnp.int32)
    kernel = functools.partial(
        gradient_kernel, fb=fb, slots=slots, links=reads * links, coils=coils
    )
    plane_spec = pl.BlockSpec((fb, tile_count, lane_width), lambda b, *_: (b, 0, 0))
    whole3 = lambda shape: pl.BlockSpec(shape, lambda b, *_: (0, 0, 0))
    flops = 2 * frame_count * slots * reads * coils * (links * lane_width) * lane_width * 3
    return pl.pallas_call(
        kernel,
        out_shape=jax.ShapeDtypeStruct(image_plane.shape, jnp.bfloat16),
        grid_spec=pltpu.PrefetchScalarGridSpec(
            num_scalar_prefetch=3,
            grid=(nblocks,),
            in_specs=[
                plane_spec,
                plane_spec,
                whole3(mrr.shape),
                whole3(mii.shape),
                whole3(bf.shape),
                whole3(bt.shape),
                whole3(btr.shape),
            ],
            out_specs=plane_spec,
            scratch_shapes=[
                pltpu.VMEM((fb, tile_count, lane_width), jnp.float32),
                pltpu.VMEM((fb, tile_count, lane_width), jnp.float32),
                pltpu.VMEM((fb, tile_count, lane_width), jnp.float32),
                pltpu.VMEM((fb * coils, links * lane_width), jnp.bfloat16),
                pltpu.VMEM((fb * coils, links * lane_width), jnp.float32),
                pltpu.VMEM((fb * coils, links * lane_width), jnp.float32),
            ],
        ),
        compiler_params=pltpu.CompilerParams(dimension_semantics=("arbitrary",)),
        cost_estimate=pl.CostEstimate(
            flops=flops, transcendentals=0, bytes_accessed=image_plane.size * 6 + mrr.size * 8
        ),
    )(idx, cnt, nsl, image_plane, adjoint_plane, mrr, mii, bf, bt, btr)


def apply_frames(mix_real, mix_imag, field_values):
    direct = jnp.einsum("fg,zftw->zgtw", mix_real, field_values, preferred_element_type=jnp.float32)
    turned = jnp.einsum(
        "fg,zftw->zgtw", mix_imag, rotate(field_values), preferred_element_type=jnp.float32
    )
    return direct + turned


def soft_shrink(filtered):
    half_width = filtered.shape[-1] // 2
    real_part, imag_part = (filtered[..., :half_width], filtered[..., half_width:])
    magnitude = jnp.sqrt(real_part * real_part + imag_part * imag_part)
    scale_values = jnp.maximum(magnitude - SOFT_CUT, 0.0) / jnp.maximum(magnitude, SOFT_CUT)
    return filtered * jnp.concatenate([scale_values, scale_values], axis=-1)


def tree_sum(value, axis):
    count = lax.axis_size(axis)
    if count & (count - 1):
        return lax.psum(value, axis)
    step = 1
    while step < count:
        pairs = [(i, i ^ step) for i in range(count)]
        value = value + lax.ppermute(value, axis, pairs)
        step *= 2
    return value


def mix_frames(weights, field_values):
    half = weights.shape[1] // 2
    mixed = jnp.einsum("kh,ktw->htw", weights, field_values, preferred_element_type=jnp.float32)
    return mixed[:half] + rotate(mixed[half:])


def local(image, adjoint_data, coil_maps, spoke_counts, tile_map, blocks, z_kernel, rank_cap):
    frame_count = image.shape[1]
    fresh = fresh_image_of(
        image[0], adjoint_data[0], coil_maps[0], spoke_counts[0], tile_map[0], blocks
    )
    count = lax.axis_size("dom")
    forward = [(i, i + 1) for i in range(count - 1)]
    backward = [(target, source) for source, target in forward]
    fresh_before = lax.ppermute(fresh, "dom", forward)
    fresh_after = lax.ppermute(fresh, "dom", backward)
    rows_real = fresh.reshape(frame_count, -1)
    rows_turned = rotate(fresh).reshape(frame_count, -1)
    gram_real = jnp.einsum("fn,gn->fg", rows_real, rows_real, preferred_element_type=jnp.float32)
    gram_imag = jnp.einsum("fn,gn->fg", rows_turned, rows_real, preferred_element_type=jnp.float32)
    gram_real, gram_imag = tree_sum(jnp.stack([gram_real, gram_imag]), "dom")
    stacked = jnp.block([[gram_real, -gram_imag], [gram_imag, gram_real]])
    threshold_sq = jnp.trace(gram_real) / rank_cap[0].astype(jnp.float32)
    unit_matrix = jnp.eye(2 * frame_count, dtype=jnp.float32)
    chol_factor = jnp.linalg.cholesky(stacked + threshold_sq * unit_matrix)
    shrink = jax.scipy.linalg.cho_solve((chol_factor, True), stacked)
    shrink_real = shrink[:frame_count, :frame_count].astype(jnp.bfloat16)
    shrink_imag = shrink[frame_count:, :frame_count].astype(jnp.bfloat16)
    low_weights = jnp.concatenate([shrink_real, shrink_imag], axis=1)

    def remainder_of(plane):
        return (plane.astype(jnp.float32) - mix_frames(low_weights, plane)).astype(jnp.bfloat16)

    low_part = mix_frames(low_weights, fresh)
    remainder = (fresh.astype(jnp.float32) - low_part).astype(jnp.bfloat16)
    stacked_planes = jnp.concatenate(
        [remainder_of(fresh_before), remainder, remainder_of(fresh_after)], axis=0
    )
    taps = z_kernel.shape[0]
    filter_weights = jnp.concatenate([z_kernel[:, 0], z_kernel[:, 1]], axis=-1)
    filter_weights = filter_weights.reshape(taps * frame_count, 2 * frame_count)
    filtered = mix_frames(filter_weights, stacked_planes)
    sparse = soft_shrink(filtered)
    return (low_part + sparse).astype(jnp.bfloat16)[None]


def solution(mesh):
    return jax.shard_map(
        local,
        mesh=mesh,
        in_specs=(
            P(("groups", "dom"), None, None, None),
            P(("groups", "dom"), None, None, None),
            P(("groups", "dom"), None, None, None),
            P(("groups", "dom"), None),
            P(("groups", "dom"), None, None, None, None),
            P(),
            P(),
            P(),
        ),
        out_specs=P(("groups", "dom"), None, None, None),
        check_vma=False,
    )
```

```python
import jax
import jax.numpy as jnp
from jax import lax
from jax.sharding import PartitionSpec as P
import functools
from jax.experimental import pallas as pl
from jax.experimental.pallas import tpu as pltpu

SOFT_CUT = 0.25


def padded_2(block, sides, width):
    for axis, dim in sides:
        count = lax.axis_size(axis)
        forward = [(i, i + 1) for i in range(count - 1)]
        backward = [(target, source) for source, target in forward]
        low = lax.ppermute(
            lax.slice_in_dim(block, block.shape[dim] - width, None, axis=dim), axis, forward
        )
        high = lax.ppermute(lax.slice_in_dim(block, 0, width, axis=dim), axis, backward)
        block = jnp.concatenate([low, block, high], axis=dim)
    return block


def rotate(field_values):
    half_width = field_values.shape[-1] // 2
    return jnp.concatenate(
        [-field_values[..., half_width:], field_values[..., :half_width]], axis=-1
    )


def complex_times(left_value, right_value):
    half_width = left_value.shape[-1] // 2
    left_real, left_imag = (left_value[..., :half_width], left_value[..., half_width:])
    right_real, right_imag = (right_value[..., :half_width], right_value[..., half_width:])
    return jnp.concatenate(
        [
            left_real * right_real - left_imag * right_imag,
            left_real * right_imag + left_imag * right_real,
        ],
        axis=-1,
    )


def conj_times(left_value, right_value):
    half_width = left_value.shape[-1] // 2
    left_real, left_imag = (left_value[..., :half_width], left_value[..., half_width:])
    right_real, right_imag = (right_value[..., :half_width], right_value[..., half_width:])
    return jnp.concatenate(
        [
            left_real * right_real + left_imag * right_imag,
            left_real * right_imag - left_imag * right_real,
        ],
        axis=-1,
    )


def grid_gradient(image_plane, plane_maps, counts, plane_map, blocks):
    frame_count, tile_count, lane_width = image_plane.shape
    read_tiles, link_count = (plane_map.shape[2], plane_map.shape[3])
    coil_count = plane_maps.shape[0]
    tile_ids = jnp.arange(tile_count, dtype=jnp.int32)

    def one_slot(spoke_slot, accum):
        tile_index = lax.dynamic_index_in_dim(plane_map, spoke_slot, axis=1, keepdims=False)
        flat_index = tile_index.reshape(frame_count, read_tiles * link_count)
        image_picked = jnp.take_along_axis(image_plane, flat_index[:, :, None], axis=1)
        image_picked = image_picked.reshape(frame_count, read_tiles, link_count, lane_width)
        maps_picked = jnp.take(plane_maps, flat_index.reshape(-1), axis=1)
        maps_picked = maps_picked.reshape(
            coil_count, frame_count, read_tiles, link_count, lane_width
        ).astype(jnp.float32)
        coil_tiles = complex_times(maps_picked, image_picked.astype(jnp.float32)[None]).astype(
            jnp.bfloat16
        )
        samples = jnp.einsum(
            "ctqji,qjio->ctqo", coil_tiles, blocks, preferred_element_type=jnp.float32
        )
        live_mask = (counts > spoke_slot).astype(jnp.float32)[None, :, None, None]
        samples = (samples * live_mask).astype(jnp.bfloat16)
        spread = jnp.einsum("ctqo,qjio->ctqji", samples, blocks, preferred_element_type=jnp.float32)
        back_sum = jnp.sum(conj_times(maps_picked, spread), axis=0)
        back_sum = back_sum.reshape(frame_count, read_tiles * link_count, lane_width)
        onehot = (flat_index[:, :, None] == tile_ids).astype(jnp.float32)
        return accum + jnp.einsum("tkn,tkw->tnw", onehot, back_sum, precision=lax.Precision.HIGHEST)

    most_spokes = jnp.max(counts)
    start_value = jnp.zeros((frame_count, tile_count, lane_width), jnp.float32)
    return lax.fori_loop(0, most_spokes, one_slot, start_value)


def gradient_kernel(idx_ref, cnt_ref, nsl_ref, img_ref, adj_ref, mrr_ref, mii_ref,
                    bf_ref, bt_ref, btr_ref, out_ref, x_scr, rx_scr, g_scr,
                    lhs_scr, y_scr, ry_scr, *, fb, slots, links, coils):
    b = pl.program_id(0)
    reads = links // 2
    img = img_ref[...].astype(jnp.float32)
    x_scr[...] = img
    half = img.shape[-1] // 2
    lane = lax.broadcasted_iota(jnp.int32, img.shape, 2)
    sign = jnp.where(lane < half, -1.0, 1.0).astype(jnp.float32)
    rx_scr[...] = pltpu.roll(img, half, 2) * sign
    g_scr[...] = jnp.zeros_like(g_scr)
    lhs_scr[...] = jnp.zeros_like(lhs_scr)

    def slot_body(s, carry):
        for q in range(reads):
            def gather_t(t, c):
                frame = b * fb + t
                live = cnt_ref[frame] > s
                base = (frame * slots + s) * links + q * 2
                row = pl.multiple_of(t * coils, coils)

                @pl.when(live)
                def _():
                    for j in range(2):
                        p = idx_ref[base + j]
                        xv = x_scr[t, pl.ds(p, 1), :]
                        rxv = rx_scr[t, pl.ds(p, 1), :]
                        ct = mrr_ref[p] * xv + mii_ref[p] * rxv
                        lhs_scr[pl.ds(row, coils), pl.ds(j * 128, 128)] = ct.astype(jnp.bfloat16)
                return c

            lax.fori_loop(0, fb, gather_t, 0)
            samples = jnp.dot(lhs_scr[...], bf_ref[q], preferred_element_type=jnp.float32)
            samples = samples.astype(jnp.bfloat16)
            y_scr[...] = jnp.dot(samples, bt_ref[q], preferred_element_type=jnp.float32)
            ry_scr[...] = jnp.dot(samples, btr_ref[q], preferred_element_type=jnp.float32)

            def scatter_t(t, c):
                frame = b * fb + t
                live = cnt_ref[frame] > s
                base = (frame * slots + s) * links + q * 2
                row = pl.multiple_of(t * coils, coils)

                @pl.when(live)
                def _():
                    for j in range(2):
                        p = idx_ref[base + j]
                        yv = y_scr[pl.ds(row, coils), pl.ds(j * 128, 128)]
                        ryv = ry_scr[pl.ds(row, coils), pl.ds(j * 128, 128)]
                        v = mrr_ref[p] * yv - mii_ref[p] * ryv
                        back = jnp.sum(v, axis=0, keepdims=True)
                        g_scr[t, pl.ds(p, 1), :] = g_scr[t, pl.ds(p, 1), :] + back
                return c

            lax.fori_loop(0, fb, scatter_t, 0)
        return carry

    lax.fori_loop(0, nsl_ref[b], slot_body, 0)
    out_ref[...] = (x_scr[...] - (g_scr[...] - adj_ref[...].astype(jnp.float32))).astype(out_ref.dtype)


def fresh_image_of(image_plane, adjoint_plane, plane_maps, counts, plane_map, blocks):
    frame_count, tile_count, lane_width = image_plane.shape
    slots, reads, links = plane_map.shape[1], plane_map.shape[2], plane_map.shape[3]
    coils = plane_maps.shape[0]
    fb = 16 if frame_count % 16 == 0 else frame_count
    nblocks = frame_count // fb
    half = lane_width // 2
    maps_t = jnp.swapaxes(plane_maps.astype(jnp.float32), 0, 1)
    mrr = jnp.concatenate([maps_t[..., :half], maps_t[..., :half]], axis=-1)
    mii = jnp.concatenate([maps_t[..., half:], maps_t[..., half:]], axis=-1)
    bf = blocks.reshape(reads, links * lane_width, lane_width)
    bt4 = jnp.transpose(blocks, (0, 3, 1, 2))
    bt = bt4.reshape(reads, lane_width, links * lane_width)
    btr = rotate(bt4).reshape(reads, lane_width, links * lane_width)
    idx = plane_map.reshape(-1).astype(jnp.int32)
    cnt = counts.astype(jnp.int32)
    nsl = jnp.minimum(jnp.max(cnt.reshape(nblocks, fb), axis=1), slots).astype(jnp.int32)
    kernel = functools.partial(
        gradient_kernel, fb=fb, slots=slots, links=reads * links, coils=coils
    )
    plane_spec = pl.BlockSpec((fb, tile_count, lane_width), lambda b, *_: (b, 0, 0))
    whole3 = lambda shape: pl.BlockSpec(shape, lambda b, *_: (0, 0, 0))
    flops = 2 * frame_count * slots * reads * coils * (links * lane_width) * lane_width * 3
    return pl.pallas_call(
        kernel,
        out_shape=jax.ShapeDtypeStruct(image_plane.shape, jnp.bfloat16),
        grid_spec=pltpu.PrefetchScalarGridSpec(
            num_scalar_prefetch=3,
            grid=(nblocks,),
            in_specs=[
                plane_spec,
                plane_spec,
                whole3(mrr.shape),
                whole3(mii.shape),
                whole3(bf.shape),
                whole3(bt.shape),
                whole3(btr.shape),
            ],
            out_specs=plane_spec,
            scratch_shapes=[
                pltpu.VMEM((fb, tile_count, lane_width), jnp.float32),
                pltpu.VMEM((fb, tile_count, lane_width), jnp.float32),
                pltpu.VMEM((fb, tile_count, lane_width), jnp.float32),
                pltpu.VMEM((fb * coils, links * lane_width), jnp.bfloat16),
                pltpu.VMEM((fb * coils, links * lane_width), jnp.float32),
                pltpu.VMEM((fb * coils, links * lane_width), jnp.float32),
            ],
        ),
        compiler_params=pltpu.CompilerParams(dimension_semantics=("arbitrary",)),
        cost_estimate=pl.CostEstimate(
            flops=flops, transcendentals=0, bytes_accessed=image_plane.size * 6 + mrr.size * 8
        ),
    )(idx, cnt, nsl, image_plane, adjoint_plane, mrr, mii, bf, bt, btr)


def post_kernel(x_ref, xb_ref, xa_ref, wl_ref, wz_ref, out_ref, *, cut):
    frames, width = x_ref.shape
    lane = lax.broadcasted_iota(jnp.int32, (frames, width), 1) % 128
    low_lane = lane < 64

    def turn(v):
        return jnp.where(low_lane, -pltpu.roll(v, width - 64, 1), pltpu.roll(v, 64, 1))

    def pair(v):
        return jnp.where(low_lane, pltpu.roll(v, width - 64, 1), pltpu.roll(v, 64, 1))

    def low_of(plane):
        mixed = jnp.dot(wl_ref[...], plane, preferred_element_type=jnp.float32)
        return mixed[:frames] + turn(mixed[frames:])

    def remainder_of(plane):
        return (plane.astype(jnp.float32) - low_of(plane)).astype(jnp.bfloat16)

    x = x_ref[...]
    low = low_of(x)
    rem = (x.astype(jnp.float32) - low).astype(jnp.bfloat16)
    planes = jnp.concatenate([remainder_of(xb_ref[...]), rem, remainder_of(xa_ref[...])], axis=0)
    mixed = jnp.dot(wz_ref[...], planes, preferred_element_type=jnp.float32)
    filtered = mixed[:frames] + turn(mixed[frames:])
    square = filtered * filtered
    magnitude = jnp.sqrt(square + pair(square))
    scale = jnp.maximum(magnitude - cut, 0.0) / jnp.maximum(magnitude, cut)
    out_ref[...] = (low + filtered * scale).astype(out_ref.dtype)


def post_of(plane, before, after, low_t, filter_t):
    frames, width = plane.shape
    nb = 2048 if width % 2048 == 0 else width
    lane_spec = pl.BlockSpec((frames, nb), lambda i: (0, i))
    whole2 = lambda shape: pl.BlockSpec(shape, lambda i: (0, 0))
    return pl.pallas_call(
        functools.partial(post_kernel, cut=SOFT_CUT),
        out_shape=jax.ShapeDtypeStruct(plane.shape, jnp.bfloat16),
        grid=(width // nb,),
        in_specs=[lane_spec, lane_spec, lane_spec, whole2(low_t.shape), whole2(filter_t.shape)],
        out_specs=lane_spec,
        compiler_params=pltpu.CompilerParams(dimension_semantics=("arbitrary",)),
        cost_estimate=pl.CostEstimate(
            flops=2 * width * frames * (2 * frames) * 6, transcendentals=width * frames,
            bytes_accessed=plane.size * 8,
        ),
    )(plane, before, after, low_t, filter_t)


def apply_frames(mix_real, mix_imag, field_values):
    direct = jnp.einsum("fg,zftw->zgtw", mix_real, field_values, preferred_element_type=jnp.float32)
    turned = jnp.einsum(
        "fg,zftw->zgtw", mix_imag, rotate(field_values), preferred_element_type=jnp.float32
    )
    return direct + turned


def soft_shrink(filtered):
    half_width = filtered.shape[-1] // 2
    real_part, imag_part = (filtered[..., :half_width], filtered[..., half_width:])
    magnitude = jnp.sqrt(real_part * real_part + imag_part * imag_part)
    scale_values = jnp.maximum(magnitude - SOFT_CUT, 0.0) / jnp.maximum(magnitude, SOFT_CUT)
    return filtered * jnp.concatenate([scale_values, scale_values], axis=-1)


def tree_sum(value, axis):
    count = lax.axis_size(axis)
    if count & (count - 1):
        return lax.psum(value, axis)
    step = 1
    while step < count:
        pairs = [(i, i ^ step) for i in range(count)]
        value = value + lax.ppermute(value, axis, pairs)
        step *= 2
    return value


def mix_frames(weights, field_values):
    half = weights.shape[1] // 2
    mixed = jnp.einsum("kh,ktw->htw", weights, field_values, preferred_element_type=jnp.float32)
    return mixed[:half] + rotate(mixed[half:])


def local(image, adjoint_data, coil_maps, spoke_counts, tile_map, blocks, z_kernel, rank_cap):
    frame_count = image.shape[1]
    fresh = fresh_image_of(
        image[0], adjoint_data[0], coil_maps[0], spoke_counts[0], tile_map[0], blocks
    )
    count = lax.axis_size("dom")
    forward = [(i, i + 1) for i in range(count - 1)]
    backward = [(target, source) for source, target in forward]
    flat = fresh.reshape(frame_count, -1)
    fresh_before = lax.ppermute(flat, "dom", forward)
    fresh_after = lax.ppermute(flat, "dom", backward)
    rows_real = flat
    rows_turned = rotate(fresh).reshape(frame_count, -1)
    gram_real = jnp.einsum("fn,gn->fg", rows_real, rows_real, preferred_element_type=jnp.float32)
    gram_imag = jnp.einsum("fn,gn->fg", rows_turned, rows_real, preferred_element_type=jnp.float32)
    gram_real, gram_imag = tree_sum(jnp.stack([gram_real, gram_imag]), "dom")
    stacked = jnp.block([[gram_real, -gram_imag], [gram_imag, gram_real]])
    threshold_sq = jnp.trace(gram_real) / rank_cap[0].astype(jnp.float32)
    unit_matrix = jnp.eye(2 * frame_count, dtype=jnp.float32)
    chol_factor = jnp.linalg.cholesky(stacked + threshold_sq * unit_matrix)
    shrink = jax.scipy.linalg.cho_solve((chol_factor, True), stacked)
    shrink_real = shrink[:frame_count, :frame_count].astype(jnp.bfloat16)
    shrink_imag = shrink[frame_count:, :frame_count].astype(jnp.bfloat16)
    low_t = jnp.concatenate([shrink_real, shrink_imag], axis=1).T
    taps = z_kernel.shape[0]
    filter_weights = jnp.concatenate([z_kernel[:, 0], z_kernel[:, 1]], axis=-1)
    filter_t = filter_weights.reshape(taps * frame_count, 2 * frame_count).T
    out = post_of(flat, fresh_before, fresh_after, low_t, filter_t)
    return out.reshape(image.shape)


def solution(mesh):
    return jax.shard_map(
        local,
        mesh=mesh,
        in_specs=(
            P(("groups", "dom"), None, None, None),
            P(("groups", "dom"), None, None, None),
            P(("groups", "dom"), None, None, None),
            P(("groups", "dom"), None),
            P(("groups", "dom"), None, None, None, None),
            P(),
            P(),
            P(),
        ),
        out_specs=P(("groups", "dom"), None, None, None),
        check_vma=False,
    )
```

```python
import jax
import jax.numpy as jnp
from jax import lax
from jax.sharding import PartitionSpec as P
import functools
from jax.experimental import pallas as pl
from jax.experimental.pallas import tpu as pltpu

SOFT_CUT = 0.25


def padded_2(block, sides, width):
    for axis, dim in sides:
        count = lax.axis_size(axis)
        forward = [(i, i + 1) for i in range(count - 1)]
        backward = [(target, source) for source, target in forward]
        low = lax.ppermute(
            lax.slice_in_dim(block, block.shape[dim] - width, None, axis=dim), axis, forward
        )
        high = lax.ppermute(lax.slice_in_dim(block, 0, width, axis=dim), axis, backward)
        block = jnp.concatenate([low, block, high], axis=dim)
    return block


def rotate(field_values):
    half_width = field_values.shape[-1] // 2
    return jnp.concatenate(
        [-field_values[..., half_width:], field_values[..., :half_width]], axis=-1
    )


def complex_times(left_value, right_value):
    half_width = left_value.shape[-1] // 2
    left_real, left_imag = (left_value[..., :half_width], left_value[..., half_width:])
    right_real, right_imag = (right_value[..., :half_width], right_value[..., half_width:])
    return jnp.concatenate(
        [
            left_real * right_real - left_imag * right_imag,
            left_real * right_imag + left_imag * right_real,
        ],
        axis=-1,
    )


def conj_times(left_value, right_value):
    half_width = left_value.shape[-1] // 2
    left_real, left_imag = (left_value[..., :half_width], left_value[..., half_width:])
    right_real, right_imag = (right_value[..., :half_width], right_value[..., half_width:])
    return jnp.concatenate(
        [
            left_real * right_real + left_imag * right_imag,
            left_real * right_imag - left_imag * right_real,
        ],
        axis=-1,
    )


def grid_gradient(image_plane, plane_maps, counts, plane_map, blocks):
    frame_count, tile_count, lane_width = image_plane.shape
    read_tiles, link_count = (plane_map.shape[2], plane_map.shape[3])
    coil_count = plane_maps.shape[0]
    tile_ids = jnp.arange(tile_count, dtype=jnp.int32)

    def one_slot(spoke_slot, accum):
        tile_index = lax.dynamic_index_in_dim(plane_map, spoke_slot, axis=1, keepdims=False)
        flat_index = tile_index.reshape(frame_count, read_tiles * link_count)
        image_picked = jnp.take_along_axis(image_plane, flat_index[:, :, None], axis=1)
        image_picked = image_picked.reshape(frame_count, read_tiles, link_count, lane_width)
        maps_picked = jnp.take(plane_maps, flat_index.reshape(-1), axis=1)
        maps_picked = maps_picked.reshape(
            coil_count, frame_count, read_tiles, link_count, lane_width
        ).astype(jnp.float32)
        coil_tiles = complex_times(maps_picked, image_picked.astype(jnp.float32)[None]).astype(
            jnp.bfloat16
        )
        samples = jnp.einsum(
            "ctqji,qjio->ctqo", coil_tiles, blocks, preferred_element_type=jnp.float32
        )
        live_mask = (counts > spoke_slot).astype(jnp.float32)[None, :, None, None]
        samples = (samples * live_mask).astype(jnp.bfloat16)
        spread = jnp.einsum("ctqo,qjio->ctqji", samples, blocks, preferred_element_type=jnp.float32)
        back_sum = jnp.sum(conj_times(maps_picked, spread), axis=0)
        back_sum = back_sum.reshape(frame_count, read_tiles * link_count, lane_width)
        onehot = (flat_index[:, :, None] == tile_ids).astype(jnp.float32)
        return accum + jnp.einsum("tkn,tkw->tnw", onehot, back_sum, precision=lax.Precision.HIGHEST)

    most_spokes = jnp.max(counts)
    start_value = jnp.zeros((frame_count, tile_count, lane_width), jnp.float32)
    return lax.fori_loop(0, most_spokes, one_slot, start_value)


def gradient_kernel(idx_ref, cnt_ref, nsl_ref, img_ref, adj_ref, mrr_ref, mii_ref,
                    bf_ref, bt_ref, btr_ref, out_ref, x_scr, rx_scr, g_scr,
                    lhs_scr, y_scr, ry_scr, *, fb, slots, links, coils):
    b = pl.program_id(0)
    reads = links // 2
    img = img_ref[...].astype(jnp.float32)
    x_scr[...] = img
    half = img.shape[-1] // 2
    lane = lax.broadcasted_iota(jnp.int32, img.shape, 2)
    sign = jnp.where(lane < half, -1.0, 1.0).astype(jnp.float32)
    rx_scr[...] = pltpu.roll(img, half, 2) * sign
    g_scr[...] = jnp.zeros_like(g_scr)
    lhs_scr[...] = jnp.zeros_like(lhs_scr)

    def slot_body(s, carry):
        for q in range(reads):
            def gather_t(t, c):
                frame = b * fb + t
                base = (frame * slots + s) * links + q * 2
                row = pl.multiple_of(t * coils, coils)
                for j in range(2):
                    p = idx_ref[base + j]
                    xv = x_scr[t, pl.ds(p, 1), :]
                    rxv = rx_scr[t, pl.ds(p, 1), :]
                    ct = mrr_ref[p] * xv + mii_ref[p] * rxv
                    lhs_scr[pl.ds(row, coils), pl.ds(j * 128, 128)] = ct.astype(jnp.bfloat16)
                return c

            lax.fori_loop(0, fb, gather_t, 0, unroll=True)
            samples = jnp.dot(lhs_scr[...], bf_ref[q], preferred_element_type=jnp.float32)
            samples = samples.astype(jnp.bfloat16)
            y_scr[...] = jnp.dot(samples, bt_ref[q], preferred_element_type=jnp.float32)
            ry_scr[...] = jnp.dot(samples, btr_ref[q], preferred_element_type=jnp.float32)

            def scatter_t(t, c):
                frame = b * fb + t
                live = cnt_ref[frame] > s
                base = (frame * slots + s) * links + q * 2
                row = pl.multiple_of(t * coils, coils)

                keep = live.astype(jnp.float32)
                for j in range(2):
                    p = idx_ref[base + j]
                    yv = y_scr[pl.ds(row, coils), pl.ds(j * 128, 128)]
                    ryv = ry_scr[pl.ds(row, coils), pl.ds(j * 128, 128)]
                    v = mrr_ref[p] * yv - mii_ref[p] * ryv
                    back = jnp.sum(v, axis=0, keepdims=True) * keep
                    g_scr[t, pl.ds(p, 1), :] = g_scr[t, pl.ds(p, 1), :] + back
                return c

            lax.fori_loop(0, fb, scatter_t, 0, unroll=True)
        return carry

    lax.fori_loop(0, nsl_ref[b], slot_body, 0)
    out_ref[...] = (x_scr[...] - (g_scr[...] - adj_ref[...].astype(jnp.float32))).astype(out_ref.dtype)


def fresh_image_of(image_plane, adjoint_plane, plane_maps, counts, plane_map, blocks):
    frame_count, tile_count, lane_width = image_plane.shape
    slots, reads, links = plane_map.shape[1], plane_map.shape[2], plane_map.shape[3]
    coils = plane_maps.shape[0]
    fb = 16 if frame_count % 16 == 0 else frame_count
    nblocks = frame_count // fb
    half = lane_width // 2
    maps_t = jnp.swapaxes(plane_maps.astype(jnp.float32), 0, 1)
    mrr = jnp.concatenate([maps_t[..., :half], maps_t[..., :half]], axis=-1)
    mii = jnp.concatenate([maps_t[..., half:], maps_t[..., half:]], axis=-1)
    bf = blocks.reshape(reads, links * lane_width, lane_width)
    bt4 = jnp.transpose(blocks, (0, 3, 1, 2))
    bt = bt4.reshape(reads, lane_width, links * lane_width)
    btr = rotate(bt4).reshape(reads, lane_width, links * lane_width)
    idx = plane_map.reshape(-1).astype(jnp.int32)
    cnt = counts.astype(jnp.int32)
    nsl = jnp.minimum(jnp.max(cnt.reshape(nblocks, fb), axis=1), slots).astype(jnp.int32)
    kernel = functools.partial(
        gradient_kernel, fb=fb, slots=slots, links=reads * links, coils=coils
    )
    plane_spec = pl.BlockSpec((fb, tile_count, lane_width), lambda b, *_: (b, 0, 0))
    whole3 = lambda shape: pl.BlockSpec(shape, lambda b, *_: (0, 0, 0))
    flops = 2 * frame_count * slots * reads * coils * (links * lane_width) * lane_width * 3
    return pl.pallas_call(
        kernel,
        out_shape=jax.ShapeDtypeStruct(image_plane.shape, jnp.bfloat16),
        grid_spec=pltpu.PrefetchScalarGridSpec(
            num_scalar_prefetch=3,
            grid=(nblocks,),
            in_specs=[
                plane_spec,
                plane_spec,
                whole3(mrr.shape),
                whole3(mii.shape),
                whole3(bf.shape),
                whole3(bt.shape),
                whole3(btr.shape),
            ],
            out_specs=plane_spec,
            scratch_shapes=[
                pltpu.VMEM((fb, tile_count, lane_width), jnp.float32),
                pltpu.VMEM((fb, tile_count, lane_width), jnp.float32),
                pltpu.VMEM((fb, tile_count, lane_width), jnp.float32),
                pltpu.VMEM((fb * coils, links * lane_width), jnp.bfloat16),
                pltpu.VMEM((fb * coils, links * lane_width), jnp.float32),
                pltpu.VMEM((fb * coils, links * lane_width), jnp.float32),
            ],
        ),
        compiler_params=pltpu.CompilerParams(dimension_semantics=("arbitrary",)),
        cost_estimate=pl.CostEstimate(
            flops=flops, transcendentals=0, bytes_accessed=image_plane.size * 6 + mrr.size * 8
        ),
    )(idx, cnt, nsl, image_plane, adjoint_plane, mrr, mii, bf, bt, btr)


def post_kernel(x_ref, xb_ref, xa_ref, wl_ref, wz_ref, out_ref, *, cut):
    frames, width = x_ref.shape
    lane = lax.broadcasted_iota(jnp.int32, (frames, width), 1) % 128
    low_lane = lane < 64

    def turn(v):
        return jnp.where(low_lane, -pltpu.roll(v, width - 64, 1), pltpu.roll(v, 64, 1))

    def pair(v):
        return jnp.where(low_lane, pltpu.roll(v, width - 64, 1), pltpu.roll(v, 64, 1))

    def low_of(plane):
        mixed = jnp.dot(wl_ref[...], plane, preferred_element_type=jnp.float32)
        return mixed[:frames] + turn(mixed[frames:])

    def remainder_of(plane):
        return (plane.astype(jnp.float32) - low_of(plane)).astype(jnp.bfloat16)

    x = x_ref[...]
    low = low_of(x)
    rem = (x.astype(jnp.float32) - low).astype(jnp.bfloat16)
    planes = jnp.concatenate([remainder_of(xb_ref[...]), rem, remainder_of(xa_ref[...])], axis=0)
    mixed = jnp.dot(wz_ref[...], planes, preferred_element_type=jnp.float32)
    filtered = mixed[:frames] + turn(mixed[frames:])
    square = filtered * filtered
    magnitude = jnp.sqrt(square + pair(square))
    scale = jnp.maximum(magnitude - cut, 0.0) / jnp.maximum(magnitude, cut)
    out_ref[...] = (low + filtered * scale).astype(out_ref.dtype)


def post_of(plane, before, after, low_t, filter_t):
    frames, width = plane.shape
    nb = 2048 if width % 2048 == 0 else width
    lane_spec = pl.BlockSpec((frames, nb), lambda i: (0, i))
    whole2 = lambda shape: pl.BlockSpec(shape, lambda i: (0, 0))
    return pl.pallas_call(
        functools.partial(post_kernel, cut=SOFT_CUT),
        out_shape=jax.ShapeDtypeStruct(plane.shape, jnp.bfloat16),
        grid=(width // nb,),
        in_specs=[lane_spec, lane_spec, lane_spec, whole2(low_t.shape), whole2(filter_t.shape)],
        out_specs=lane_spec,
        compiler_params=pltpu.CompilerParams(dimension_semantics=("arbitrary",)),
        cost_estimate=pl.CostEstimate(
            flops=2 * width * frames * (2 * frames) * 6, transcendentals=width * frames,
            bytes_accessed=plane.size * 8,
        ),
    )(plane, before, after, low_t, filter_t)


def apply_frames(mix_real, mix_imag, field_values):
    direct = jnp.einsum("fg,zftw->zgtw", mix_real, field_values, preferred_element_type=jnp.float32)
    turned = jnp.einsum(
        "fg,zftw->zgtw", mix_imag, rotate(field_values), preferred_element_type=jnp.float32
    )
    return direct + turned


def soft_shrink(filtered):
    half_width = filtered.shape[-1] // 2
    real_part, imag_part = (filtered[..., :half_width], filtered[..., half_width:])
    magnitude = jnp.sqrt(real_part * real_part + imag_part * imag_part)
    scale_values = jnp.maximum(magnitude - SOFT_CUT, 0.0) / jnp.maximum(magnitude, SOFT_CUT)
    return filtered * jnp.concatenate([scale_values, scale_values], axis=-1)


def tree_sum(value, axis):
    count = lax.axis_size(axis)
    if count & (count - 1):
        return lax.psum(value, axis)
    step = 1
    while step < count:
        pairs = [(i, i ^ step) for i in range(count)]
        value = value + lax.ppermute(value, axis, pairs)
        step *= 2
    return value


def mix_frames(weights, field_values):
    half = weights.shape[1] // 2
    mixed = jnp.einsum("kh,ktw->htw", weights, field_values, preferred_element_type=jnp.float32)
    return mixed[:half] + rotate(mixed[half:])


def local(image, adjoint_data, coil_maps, spoke_counts, tile_map, blocks, z_kernel, rank_cap):
    frame_count = image.shape[1]
    fresh = fresh_image_of(
        image[0], adjoint_data[0], coil_maps[0], spoke_counts[0], tile_map[0], blocks
    )
    count = lax.axis_size("dom")
    forward = [(i, i + 1) for i in range(count - 1)]
    backward = [(target, source) for source, target in forward]
    flat = fresh.reshape(frame_count, -1)
    rows_real = flat
    rows_turned = rotate(fresh).reshape(frame_count, -1)
    gram_real = jnp.einsum("fn,gn->fg", rows_real, rows_real, preferred_element_type=jnp.float32)
    gram_imag = jnp.einsum("fn,gn->fg", rows_turned, rows_real, preferred_element_type=jnp.float32)
    gram_real, gram_imag = tree_sum(jnp.stack([gram_real, gram_imag]), "dom")
    flat, gram_real, gram_imag = lax.optimization_barrier((flat, gram_real, gram_imag))
    fresh_before = lax.ppermute(flat, "dom", forward)
    fresh_after = lax.ppermute(flat, "dom", backward)
    stacked = jnp.block([[gram_real, -gram_imag], [gram_imag, gram_real]])
    threshold_sq = jnp.trace(gram_real) / rank_cap[0].astype(jnp.float32)
    unit_matrix = jnp.eye(2 * frame_count, dtype=jnp.float32)
    chol_factor = jnp.linalg.cholesky(stacked + threshold_sq * unit_matrix)
    shrink = jax.scipy.linalg.cho_solve((chol_factor, True), stacked)
    shrink_real = shrink[:frame_count, :frame_count].astype(jnp.bfloat16)
    shrink_imag = shrink[frame_count:, :frame_count].astype(jnp.bfloat16)
    low_t = jnp.concatenate([shrink_real, shrink_imag], axis=1).T
    taps = z_kernel.shape[0]
    filter_weights = jnp.concatenate([z_kernel[:, 0], z_kernel[:, 1]], axis=-1)
    filter_t = filter_weights.reshape(taps * frame_count, 2 * frame_count).T
    out = post_of(flat, fresh_before, fresh_after, low_t, filter_t)
    return out.reshape(image.shape)


def solution(mesh):
    return jax.shard_map(
        local,
        mesh=mesh,
        in_specs=(
            P(("groups", "dom"), None, None, None),
            P(("groups", "dom"), None, None, None),
            P(("groups", "dom"), None, None, None),
            P(("groups", "dom"), None),
            P(("groups", "dom"), None, None, None, None),
            P(),
            P(),
            P(),
        ),
        out_specs=P(("groups", "dom"), None, None, None),
        check_vma=False,
    )
```

```python
import jax
import jax.numpy as jnp
from jax import lax
from jax.sharding import PartitionSpec as P
import functools
from jax.experimental import pallas as pl
from jax.experimental.pallas import tpu as pltpu

SOFT_CUT = 0.25


def padded_2(block, sides, width):
    for axis, dim in sides:
        count = lax.axis_size(axis)
        forward = [(i, i + 1) for i in range(count - 1)]
        backward = [(target, source) for source, target in forward]
        low = lax.ppermute(
            lax.slice_in_dim(block, block.shape[dim] - width, None, axis=dim), axis, forward
        )
        high = lax.ppermute(lax.slice_in_dim(block, 0, width, axis=dim), axis, backward)
        block = jnp.concatenate([low, block, high], axis=dim)
    return block


def rotate(field_values):
    half_width = field_values.shape[-1] // 2
    return jnp.concatenate(
        [-field_values[..., half_width:], field_values[..., :half_width]], axis=-1
    )


def complex_times(left_value, right_value):
    half_width = left_value.shape[-1] // 2
    left_real, left_imag = (left_value[..., :half_width], left_value[..., half_width:])
    right_real, right_imag = (right_value[..., :half_width], right_value[..., half_width:])
    return jnp.concatenate(
        [
            left_real * right_real - left_imag * right_imag,
            left_real * right_imag + left_imag * right_real,
        ],
        axis=-1,
    )


def conj_times(left_value, right_value):
    half_width = left_value.shape[-1] // 2
    left_real, left_imag = (left_value[..., :half_width], left_value[..., half_width:])
    right_real, right_imag = (right_value[..., :half_width], right_value[..., half_width:])
    return jnp.concatenate(
        [
            left_real * right_real + left_imag * right_imag,
            left_real * right_imag - left_imag * right_real,
        ],
        axis=-1,
    )


def grid_gradient(image_plane, plane_maps, counts, plane_map, blocks):
    frame_count, tile_count, lane_width = image_plane.shape
    read_tiles, link_count = (plane_map.shape[2], plane_map.shape[3])
    coil_count = plane_maps.shape[0]
    tile_ids = jnp.arange(tile_count, dtype=jnp.int32)

    def one_slot(spoke_slot, accum):
        tile_index = lax.dynamic_index_in_dim(plane_map, spoke_slot, axis=1, keepdims=False)
        flat_index = tile_index.reshape(frame_count, read_tiles * link_count)
        image_picked = jnp.take_along_axis(image_plane, flat_index[:, :, None], axis=1)
        image_picked = image_picked.reshape(frame_count, read_tiles, link_count, lane_width)
        maps_picked = jnp.take(plane_maps, flat_index.reshape(-1), axis=1)
        maps_picked = maps_picked.reshape(
            coil_count, frame_count, read_tiles, link_count, lane_width
        ).astype(jnp.float32)
        coil_tiles = complex_times(maps_picked, image_picked.astype(jnp.float32)[None]).astype(
            jnp.bfloat16
        )
        samples = jnp.einsum(
            "ctqji,qjio->ctqo", coil_tiles, blocks, preferred_element_type=jnp.float32
        )
        live_mask = (counts > spoke_slot).astype(jnp.float32)[None, :, None, None]
        samples = (samples * live_mask).astype(jnp.bfloat16)
        spread = jnp.einsum("ctqo,qjio->ctqji", samples, blocks, preferred_element_type=jnp.float32)
        back_sum = jnp.sum(conj_times(maps_picked, spread), axis=0)
        back_sum = back_sum.reshape(frame_count, read_tiles * link_count, lane_width)
        onehot = (flat_index[:, :, None] == tile_ids).astype(jnp.float32)
        return accum + jnp.einsum("tkn,tkw->tnw", onehot, back_sum, precision=lax.Precision.HIGHEST)

    most_spokes = jnp.max(counts)
    start_value = jnp.zeros((frame_count, tile_count, lane_width), jnp.float32)
    return lax.fori_loop(0, most_spokes, one_slot, start_value)


def gradient_kernel(idx_ref, cnt_ref, nsl_ref, img_ref, adj_ref, maps_ref,
                    bf_ref, bt_ref, btr_ref, out_ref, x_scr, rx_scr, g_scr,
                    lhs_scr, y_scr, ry_scr, mrr_ref, mii_ref, *, fb, slots, links, coils):
    b = pl.program_id(0)
    reads = links // 2
    img = img_ref[...].astype(jnp.float32)
    x_scr[...] = img
    half = img.shape[-1] // 2
    lane = lax.broadcasted_iota(jnp.int32, img.shape, 2)
    sign = jnp.where(lane < half, -1.0, 1.0).astype(jnp.float32)
    rx_scr[...] = pltpu.roll(img, half, 2) * sign

    @pl.when(b == 0)
    def _():
        maps = maps_ref[...].astype(jnp.float32)
        map_lane = lax.broadcasted_iota(jnp.int32, maps.shape, 2) < half
        swapped = pltpu.roll(maps, half, 2)
        mrr_ref[...] = jnp.where(map_lane, maps, swapped)
        mii_ref[...] = jnp.where(map_lane, swapped, maps)
    g_scr[...] = jnp.zeros_like(g_scr)
    lhs_scr[...] = jnp.zeros_like(lhs_scr)

    def slot_body(s, carry):
        for q in range(reads):
            def gather_t(t, c):
                frame = b * fb + t
                base = (frame * slots + s) * links + q * 2
                row = pl.multiple_of(t * coils, coils)
                for j in range(2):
                    p = idx_ref[base + j]
                    xv = x_scr[t, pl.ds(p, 1), :]
                    rxv = rx_scr[t, pl.ds(p, 1), :]
                    ct = mrr_ref[p] * xv + mii_ref[p] * rxv
                    lhs_scr[pl.ds(row, coils), pl.ds(j * 128, 128)] = ct.astype(jnp.bfloat16)
                return c

            lax.fori_loop(0, fb, gather_t, 0, unroll=True)
            samples = jnp.dot(lhs_scr[...], bf_ref[q], preferred_element_type=jnp.float32)
            samples = samples.astype(jnp.bfloat16)
            y_scr[...] = jnp.dot(samples, bt_ref[q], preferred_element_type=jnp.float32)
            ry_scr[...] = jnp.dot(samples, btr_ref[q], preferred_element_type=jnp.float32)

            def scatter_t(t, c):
                frame = b * fb + t
                live = cnt_ref[frame] > s
                base = (frame * slots + s) * links + q * 2
                row = pl.multiple_of(t * coils, coils)

                keep = live.astype(jnp.float32)
                for j in range(2):
                    p = idx_ref[base + j]
                    yv = y_scr[pl.ds(row, coils), pl.ds(j * 128, 128)]
                    ryv = ry_scr[pl.ds(row, coils), pl.ds(j * 128, 128)]
                    v = mrr_ref[p] * yv - mii_ref[p] * ryv
                    back = jnp.sum(v, axis=0, keepdims=True) * keep
                    g_scr[t, pl.ds(p, 1), :] = g_scr[t, pl.ds(p, 1), :] + back
                return c

            lax.fori_loop(0, fb, scatter_t, 0, unroll=True)
        return carry

    lax.fori_loop(0, nsl_ref[b], slot_body, 0)
    out_ref[...] = (x_scr[...] - (g_scr[...] - adj_ref[...].astype(jnp.float32))).astype(out_ref.dtype)


def fresh_image_of(image_plane, adjoint_plane, plane_maps, counts, plane_map, blocks):
    frame_count, tile_count, lane_width = image_plane.shape
    slots, reads, links = plane_map.shape[1], plane_map.shape[2], plane_map.shape[3]
    coils = plane_maps.shape[0]
    fb = 16 if frame_count % 16 == 0 else frame_count
    nblocks = frame_count // fb
    half = lane_width // 2
    maps_t = jnp.swapaxes(plane_maps, 0, 1)
    bf = blocks.reshape(reads, links * lane_width, lane_width)
    bt4 = jnp.transpose(blocks, (0, 3, 1, 2))
    bt = bt4.reshape(reads, lane_width, links * lane_width)
    btr = rotate(bt4).reshape(reads, lane_width, links * lane_width)
    idx = plane_map.reshape(-1).astype(jnp.int32)
    cnt = counts.astype(jnp.int32)
    nsl = jnp.minimum(jnp.max(cnt.reshape(nblocks, fb), axis=1), slots).astype(jnp.int32)
    kernel = functools.partial(
        gradient_kernel, fb=fb, slots=slots, links=reads * links, coils=coils
    )
    plane_spec = pl.BlockSpec((fb, tile_count, lane_width), lambda b, *_: (b, 0, 0))
    whole3 = lambda shape: pl.BlockSpec(shape, lambda b, *_: (0, 0, 0))
    flops = 2 * frame_count * slots * reads * coils * (links * lane_width) * lane_width * 3
    return pl.pallas_call(
        kernel,
        out_shape=jax.ShapeDtypeStruct(image_plane.shape, jnp.bfloat16),
        grid_spec=pltpu.PrefetchScalarGridSpec(
            num_scalar_prefetch=3,
            grid=(nblocks,),
            in_specs=[
                plane_spec,
                plane_spec,
                whole3(maps_t.shape),
                whole3(bf.shape),
                whole3(bt.shape),
                whole3(btr.shape),
            ],
            out_specs=plane_spec,
            scratch_shapes=[
                pltpu.VMEM((fb, tile_count, lane_width), jnp.float32),
                pltpu.VMEM((fb, tile_count, lane_width), jnp.float32),
                pltpu.VMEM((fb, tile_count, lane_width), jnp.float32),
                pltpu.VMEM((fb * coils, links * lane_width), jnp.bfloat16),
                pltpu.VMEM((fb * coils, links * lane_width), jnp.float32),
                pltpu.VMEM((fb * coils, links * lane_width), jnp.float32),
                pltpu.VMEM(maps_t.shape, jnp.float32),
                pltpu.VMEM(maps_t.shape, jnp.float32),
            ],
        ),
        compiler_params=pltpu.CompilerParams(dimension_semantics=("arbitrary",)),
        cost_estimate=pl.CostEstimate(
            flops=flops, transcendentals=0, bytes_accessed=image_plane.size * 6 + maps_t.size * 2
        ),
    )(idx, cnt, nsl, image_plane, adjoint_plane, maps_t, bf, bt, btr)


def post_kernel(x_ref, xb_ref, xa_ref, wl_ref, wz_ref, out_ref, *, cut):
    frames, width = x_ref.shape
    lane = lax.broadcasted_iota(jnp.int32, (frames, width), 1) % 128
    low_lane = lane < 64

    def turn(v):
        return jnp.where(low_lane, -pltpu.roll(v, width - 64, 1), pltpu.roll(v, 64, 1))

    def pair(v):
        return jnp.where(low_lane, pltpu.roll(v, width - 64, 1), pltpu.roll(v, 64, 1))

    def low_of(plane):
        mixed = jnp.dot(wl_ref[...], plane, preferred_element_type=jnp.float32)
        return mixed[:frames] + turn(mixed[frames:])

    def remainder_of(plane):
        return (plane.astype(jnp.float32) - low_of(plane)).astype(jnp.bfloat16)

    x = x_ref[...]
    low = low_of(x)
    rem = (x.astype(jnp.float32) - low).astype(jnp.bfloat16)
    planes = jnp.concatenate([remainder_of(xb_ref[...]), rem, remainder_of(xa_ref[...])], axis=0)
    mixed = jnp.dot(wz_ref[...], planes, preferred_element_type=jnp.float32)
    filtered = mixed[:frames] + turn(mixed[frames:])
    square = filtered * filtered
    magnitude = jnp.sqrt(square + pair(square))
    scale = jnp.maximum(magnitude - cut, 0.0) / jnp.maximum(magnitude, cut)
    out_ref[...] = (low + filtered * scale).astype(out_ref.dtype)


def post_of(plane, before, after, low_t, filter_t):
    frames, width = plane.shape
    nb = 2048 if width % 2048 == 0 else width
    lane_spec = pl.BlockSpec((frames, nb), lambda i: (0, i))
    whole2 = lambda shape: pl.BlockSpec(shape, lambda i: (0, 0))
    return pl.pallas_call(
        functools.partial(post_kernel, cut=SOFT_CUT),
        out_shape=jax.ShapeDtypeStruct(plane.shape, jnp.bfloat16),
        grid=(width // nb,),
        in_specs=[lane_spec, lane_spec, lane_spec, whole2(low_t.shape), whole2(filter_t.shape)],
        out_specs=lane_spec,
        compiler_params=pltpu.CompilerParams(dimension_semantics=("arbitrary",)),
        cost_estimate=pl.CostEstimate(
            flops=2 * width * frames * (2 * frames) * 6, transcendentals=width * frames,
            bytes_accessed=plane.size * 8,
        ),
    )(plane, before, after, low_t, filter_t)


def solve_kernel(a_ref, x0_ref, s_ref, out_ref, *, steps):
    size = a_ref.shape[0]
    rows = lax.broadcasted_iota(jnp.int32, (size, size), 0)
    cols = lax.broadcasted_iota(jnp.int32, (size, size), 1)
    twice = jnp.where(rows == cols, 2.0, 0.0).astype(jnp.float32)
    a = a_ref[...]
    high = lax.Precision.HIGHEST

    def step(i, x):
        t = jnp.dot(a, x, precision=high, preferred_element_type=jnp.float32)
        return jnp.dot(x, twice - t, precision=high, preferred_element_type=jnp.float32)

    x = x0_ref[...]
    for i in range(steps):
        x = step(i, x)
    out_ref[...] = jnp.dot(x, s_ref[...], precision=high, preferred_element_type=jnp.float32)


def shrink_of(stacked, threshold_sq, rank_value):
    size = stacked.shape[0]
    unit_matrix = jnp.eye(size, dtype=jnp.float32)
    system = stacked + threshold_sq * unit_matrix
    start = unit_matrix * (2.0 / (threshold_sq * (2.0 + rank_value)))
    whole = pl.BlockSpec(memory_space=pltpu.VMEM)
    return pl.pallas_call(
        functools.partial(solve_kernel, steps=12),
        out_shape=jax.ShapeDtypeStruct((size, size), jnp.float32),
        in_specs=[whole, whole, whole],
        out_specs=whole,
    )(system, start, stacked)


def apply_frames(mix_real, mix_imag, field_values):
    direct = jnp.einsum("fg,zftw->zgtw", mix_real, field_values, preferred_element_type=jnp.float32)
    turned = jnp.einsum(
        "fg,zftw->zgtw", mix_imag, rotate(field_values), preferred_element_type=jnp.float32
    )
    return direct + turned


def soft_shrink(filtered):
    half_width = filtered.shape[-1] // 2
    real_part, imag_part = (filtered[..., :half_width], filtered[..., half_width:])
    magnitude = jnp.sqrt(real_part * real_part + imag_part * imag_part)
    scale_values = jnp.maximum(magnitude - SOFT_CUT, 0.0) / jnp.maximum(magnitude, SOFT_CUT)
    return filtered * jnp.concatenate([scale_values, scale_values], axis=-1)


def tree_sum(value, axis):
    count = lax.axis_size(axis)
    if count & (count - 1):
        return lax.psum(value, axis)
    step = 1
    while step < count:
        pairs = [(i, i ^ step) for i in range(count)]
        value = value + lax.ppermute(value, axis, pairs)
        step *= 2
    return value


def mix_frames(weights, field_values):
    half = weights.shape[1] // 2
    mixed = jnp.einsum("kh,ktw->htw", weights, field_values, preferred_element_type=jnp.float32)
    return mixed[:half] + rotate(mixed[half:])


def local(image, adjoint_data, coil_maps, spoke_counts, tile_map, blocks, z_kernel, rank_cap):
    frame_count = image.shape[1]
    fresh = fresh_image_of(
        image[0], adjoint_data[0], coil_maps[0], spoke_counts[0], tile_map[0], blocks
    )
    count = lax.axis_size("dom")
    forward = [(i, i + 1) for i in range(count - 1)]
    backward = [(target, source) for source, target in forward]
    flat = fresh.reshape(frame_count, -1)
    rows_real = flat
    rows_turned = rotate(fresh).reshape(frame_count, -1)
    gram_real = jnp.einsum("fn,gn->fg", rows_real, rows_real, preferred_element_type=jnp.float32)
    gram_imag = jnp.einsum("fn,gn->fg", rows_turned, rows_real, preferred_element_type=jnp.float32)
    gram_real, gram_imag = tree_sum(jnp.stack([gram_real, gram_imag]), "dom")
    flat, gram_real, gram_imag = lax.optimization_barrier((flat, gram_real, gram_imag))
    fresh_before = lax.ppermute(flat, "dom", forward)
    fresh_after = lax.ppermute(flat, "dom", backward)
    stacked = jnp.block([[gram_real, -gram_imag], [gram_imag, gram_real]])
    rank_value = rank_cap[0].astype(jnp.float32)
    threshold_sq = jnp.trace(gram_real) / rank_value
    shrink = shrink_of(stacked, threshold_sq, rank_value)
    shrink_real = shrink[:frame_count, :frame_count].astype(jnp.bfloat16)
    shrink_imag = shrink[frame_count:, :frame_count].astype(jnp.bfloat16)
    low_t = jnp.concatenate([shrink_real, shrink_imag], axis=1).T
    taps = z_kernel.shape[0]
    filter_weights = jnp.concatenate([z_kernel[:, 0], z_kernel[:, 1]], axis=-1)
    filter_t = filter_weights.reshape(taps * frame_count, 2 * frame_count).T
    out = post_of(flat, fresh_before, fresh_after, low_t, filter_t)
    return out.reshape(image.shape)


def solution(mesh):
    return jax.shard_map(
        local,
        mesh=mesh,
        in_specs=(
            P(("groups", "dom"), None, None, None),
            P(("groups", "dom"), None, None, None),
            P(("groups", "dom"), None, None, None),
            P(("groups", "dom"), None),
            P(("groups", "dom"), None, None, None, None),
            P(),
            P(),
            P(),
        ),
        out_specs=P(("groups", "dom"), None, None, None),
        check_vma=False,
    )
```

```python
import jax
import jax.numpy as jnp
from jax import lax
from jax.sharding import PartitionSpec as P
import functools
from jax.experimental import pallas as pl
from jax.experimental.pallas import tpu as pltpu

SOFT_CUT = 0.25


def rotate(field_values):
    half_width = field_values.shape[-1] // 2
    return jnp.concatenate(
        [-field_values[..., half_width:], field_values[..., :half_width]], axis=-1
    )


def gradient_kernel(idx_ref, cnt_ref, nsl_ref, img_ref, adj_ref, maps_ref,
                    bf_ref, bt_ref, btr_ref, out_ref, x_scr, rx_scr, g_scr,
                    lhs_scr, y_scr, ry_scr, mrr_ref, mii_ref, *, fb, block, slots, links, coils):
    b = block
    reads = links // 2
    img = img_ref[...].astype(jnp.float32)
    x_scr[...] = img
    half = img.shape[-1] // 2
    lane = lax.broadcasted_iota(jnp.int32, img.shape, 2)
    sign = jnp.where(lane < half, -1.0, 1.0).astype(jnp.float32)
    rx_scr[...] = pltpu.roll(img, half, 2) * sign

    maps = maps_ref[...].astype(jnp.float32)
    map_lane = lax.broadcasted_iota(jnp.int32, maps.shape, 2) < half
    swapped = pltpu.roll(maps, half, 2)
    mrr_ref[...] = jnp.where(map_lane, maps, swapped)
    mii_ref[...] = jnp.where(map_lane, swapped, maps)
    g_scr[...] = jnp.zeros_like(g_scr)
    lhs_scr[...] = jnp.zeros_like(lhs_scr)

    def slot_body(s, carry):
        for q in range(reads):
            def gather_t(t, c):
                frame = b * fb + t
                base = (frame * slots + s) * links + q * 2
                row = pl.multiple_of(t * coils, coils)
                for j in range(2):
                    p = idx_ref[base + j]
                    xv = x_scr[t, pl.ds(p, 1), :]
                    rxv = rx_scr[t, pl.ds(p, 1), :]
                    ct = mrr_ref[p] * xv + mii_ref[p] * rxv
                    lhs_scr[pl.ds(row, coils), pl.ds(j * 128, 128)] = ct.astype(jnp.bfloat16)
                return c

            lax.fori_loop(0, fb, gather_t, 0, unroll=True)
            samples = jnp.dot(lhs_scr[...], bf_ref[q], preferred_element_type=jnp.float32)
            samples = samples.astype(jnp.bfloat16)
            y_scr[...] = jnp.dot(samples, bt_ref[q], preferred_element_type=jnp.float32)
            ry_scr[...] = jnp.dot(samples, btr_ref[q], preferred_element_type=jnp.float32)

            def scatter_t(t, c):
                frame = b * fb + t
                live = cnt_ref[frame] > s
                base = (frame * slots + s) * links + q * 2
                row = pl.multiple_of(t * coils, coils)

                keep = live.astype(jnp.float32)
                for j in range(2):
                    p = idx_ref[base + j]
                    yv = y_scr[pl.ds(row, coils), pl.ds(j * 128, 128)]
                    ryv = ry_scr[pl.ds(row, coils), pl.ds(j * 128, 128)]
                    v = mrr_ref[p] * yv - mii_ref[p] * ryv
                    back = jnp.sum(v, axis=0, keepdims=True) * keep
                    g_scr[t, pl.ds(p, 1), :] = g_scr[t, pl.ds(p, 1), :] + back
                return c

            lax.fori_loop(0, fb, scatter_t, 0, unroll=True)
        return carry

    lax.fori_loop(0, nsl_ref[b], slot_body, 0)
    out_ref[...] = (x_scr[...] - (g_scr[...] - adj_ref[...].astype(jnp.float32))).astype(out_ref.dtype)


def fresh_blocks_of(image_plane, adjoint_plane, plane_maps, counts, plane_map, blocks):
    frame_count, tile_count, lane_width = image_plane.shape
    slots, reads, links = plane_map.shape[1], plane_map.shape[2], plane_map.shape[3]
    coils = plane_maps.shape[0]
    fb = 16 if frame_count % 16 == 0 else frame_count
    nblocks = frame_count // fb
    maps_t = jnp.swapaxes(plane_maps, 0, 1)
    bf = blocks.reshape(reads, links * lane_width, lane_width)
    bt4 = jnp.transpose(blocks, (0, 3, 1, 2))
    bt = bt4.reshape(reads, lane_width, links * lane_width)
    btr = rotate(bt4).reshape(reads, lane_width, links * lane_width)
    idx = plane_map.reshape(-1).astype(jnp.int32)
    cnt = counts.astype(jnp.int32)
    nsl = jnp.minimum(jnp.max(cnt.reshape(nblocks, fb), axis=1), slots).astype(jnp.int32)
    whole3 = lambda shape: pl.BlockSpec(shape, lambda i, *_: (0, 0, 0))
    flops = 2 * fb * slots * reads * coils * (links * lane_width) * lane_width * 3
    outs = []
    for block in range(nblocks):
        kernel = functools.partial(
            gradient_kernel, fb=fb, block=block, slots=slots, links=reads * links, coils=coils
        )
        plane_spec = pl.BlockSpec(
            (fb, tile_count, lane_width), functools.partial(lambda k, i, *_: (k, 0, 0), block)
        )
        out_spec = pl.BlockSpec((fb, tile_count, lane_width), lambda i, *_: (0, 0, 0))
        outs.append(grad_call(kernel, fb, tile_count, lane_width, plane_spec, out_spec,
                              whole3, maps_t, bf, bt, btr, coils, links, flops,
                              idx, cnt, nsl, image_plane, adjoint_plane))
    return outs


def grad_call(kernel, fb, tile_count, lane_width, plane_spec, out_spec, whole3, maps_t, bf, bt,
              btr, coils, links, flops, idx, cnt, nsl, image_plane, adjoint_plane):
    return (pl.pallas_call(
            kernel,
            out_shape=jax.ShapeDtypeStruct((fb, tile_count, lane_width), jnp.bfloat16),
            grid_spec=pltpu.PrefetchScalarGridSpec(
                num_scalar_prefetch=3,
                grid=(1,),
                in_specs=[
                    plane_spec,
                    plane_spec,
                    whole3(maps_t.shape),
                    whole3(bf.shape),
                    whole3(bt.shape),
                    whole3(btr.shape),
                ],
                out_specs=out_spec,
                scratch_shapes=[
                    pltpu.VMEM((fb, tile_count, lane_width), jnp.float32),
                    pltpu.VMEM((fb, tile_count, lane_width), jnp.float32),
                    pltpu.VMEM((fb, tile_count, lane_width), jnp.float32),
                    pltpu.VMEM((fb * coils, links * lane_width), jnp.bfloat16),
                    pltpu.VMEM((fb * coils, links * lane_width), jnp.float32),
                    pltpu.VMEM((fb * coils, links * lane_width), jnp.float32),
                    pltpu.VMEM(maps_t.shape, jnp.float32),
                    pltpu.VMEM(maps_t.shape, jnp.float32),
                ],
            ),
            compiler_params=pltpu.CompilerParams(dimension_semantics=("arbitrary",)),
            cost_estimate=pl.CostEstimate(
                flops=flops, transcendentals=0,
                bytes_accessed=fb * tile_count * lane_width * 6 + maps_t.size * 2,
            ),
        )(idx, cnt, nsl, image_plane, adjoint_plane, maps_t, bf, bt, btr))


def post_kernel(*refs, pieces, cut):
    x_ref = refs[0]
    before = refs[1:1 + pieces]
    after = refs[1 + pieces:1 + 2 * pieces]
    wl_ref, wz_ref, out_ref = refs[1 + 2 * pieces:]
    frames, width = x_ref.shape
    lane = lax.broadcasted_iota(jnp.int32, (frames, width), 1) % 128
    low_lane = lane < 64

    def turn(v):
        return jnp.where(low_lane, -pltpu.roll(v, width - 64, 1), pltpu.roll(v, 64, 1))

    def pair(v):
        return jnp.where(low_lane, pltpu.roll(v, width - 64, 1), pltpu.roll(v, 64, 1))

    def low_of(plane):
        mixed = jnp.dot(wl_ref[...], plane, preferred_element_type=jnp.float32)
        return mixed[:frames] + turn(mixed[frames:])

    def remainder_of(plane):
        return (plane.astype(jnp.float32) - low_of(plane)).astype(jnp.bfloat16)

    x = x_ref[...]
    low = low_of(x)
    rem = (x.astype(jnp.float32) - low).astype(jnp.bfloat16)
    plane_before = jnp.concatenate([r[...] for r in before], axis=0)
    plane_after = jnp.concatenate([r[...] for r in after], axis=0)
    planes = jnp.concatenate([remainder_of(plane_before), rem, remainder_of(plane_after)], axis=0)
    mixed = jnp.dot(wz_ref[...], planes, preferred_element_type=jnp.float32)
    filtered = mixed[:frames] + turn(mixed[frames:])
    square = filtered * filtered
    magnitude = jnp.sqrt(square + pair(square))
    scale = jnp.maximum(magnitude - cut, 0.0) / jnp.maximum(magnitude, cut)
    out_ref[...] = (low + filtered * scale).astype(out_ref.dtype)


def post_of(plane, before, after, low_t, filter_t):
    frames, width = plane.shape
    pieces = len(before)
    piece = before[0].shape[0]
    nb = 2048 if width % 2048 == 0 else width
    lane_spec = pl.BlockSpec((frames, nb), lambda i: (0, i))
    piece_spec = pl.BlockSpec((piece, nb), lambda i: (0, i))
    whole2 = lambda shape: pl.BlockSpec(shape, lambda i: (0, 0))
    return pl.pallas_call(
        functools.partial(post_kernel, pieces=pieces, cut=SOFT_CUT),
        out_shape=jax.ShapeDtypeStruct(plane.shape, jnp.bfloat16),
        grid=(width // nb,),
        in_specs=[lane_spec] + [piece_spec] * (2 * pieces) + [whole2(low_t.shape), whole2(filter_t.shape)],
        out_specs=lane_spec,
        compiler_params=pltpu.CompilerParams(dimension_semantics=("arbitrary",)),
        cost_estimate=pl.CostEstimate(
            flops=2 * width * frames * (2 * frames) * 6, transcendentals=width * frames,
            bytes_accessed=plane.size * 8,
        ),
    )(plane, *before, *after, low_t, filter_t)


def solve_kernel(a_ref, x0_ref, s_ref, out_ref, *, steps):
    size = a_ref.shape[0]
    rows = lax.broadcasted_iota(jnp.int32, (size, size), 0)
    cols = lax.broadcasted_iota(jnp.int32, (size, size), 1)
    twice = jnp.where(rows == cols, 2.0, 0.0).astype(jnp.float32)
    a = a_ref[...]
    high = lax.Precision.HIGHEST

    def step(x):
        t = jnp.dot(a, x, precision=high, preferred_element_type=jnp.float32)
        return jnp.dot(x, twice - t, precision=high, preferred_element_type=jnp.float32)

    x = x0_ref[...]
    for _ in range(steps):
        x = step(x)
    out_ref[...] = jnp.dot(x, s_ref[...], precision=high, preferred_element_type=jnp.float32)


def shrink_of(stacked, threshold_sq, rank_value):
    size = stacked.shape[0]
    unit_matrix = jnp.eye(size, dtype=jnp.float32)
    system = stacked + threshold_sq * unit_matrix
    start = unit_matrix * (2.0 / (threshold_sq * (2.0 + rank_value)))
    whole = pl.BlockSpec(memory_space=pltpu.VMEM)
    return pl.pallas_call(
        functools.partial(solve_kernel, steps=12),
        out_shape=jax.ShapeDtypeStruct((size, size), jnp.float32),
        in_specs=[whole, whole, whole],
        out_specs=whole,
    )(system, start, stacked)


def tree_sum(value, axis):
    count = lax.axis_size(axis)
    if count & (count - 1):
        return lax.psum(value, axis)
    step = 1
    while step < count:
        pairs = [(i, i ^ step) for i in range(count)]
        value = value + lax.ppermute(value, axis, pairs)
        step *= 2
    return value


def local(image, adjoint_data, coil_maps, spoke_counts, tile_map, blocks, z_kernel, rank_cap):
    frame_count = image.shape[1]
    pieces = fresh_blocks_of(
        image[0], adjoint_data[0], coil_maps[0], spoke_counts[0], tile_map[0], blocks
    )
    count = lax.axis_size("dom")
    forward = [(i, i + 1) for i in range(count - 1)]
    backward = [(target, source) for source, target in forward]
    flat_pieces = [piece.reshape(piece.shape[0], -1) for piece in pieces]
    before, after = [], []
    for piece in flat_pieces[:-1]:
        before.append(lax.ppermute(piece, "dom", forward))
        after.append(lax.ppermute(piece, "dom", backward))
    fresh = jnp.concatenate(pieces, axis=0)
    flat = jnp.concatenate(flat_pieces, axis=0)
    rows_real = flat
    rows_turned = rotate(fresh).reshape(frame_count, -1)
    gram_real = jnp.einsum("fn,gn->fg", rows_real, rows_real, preferred_element_type=jnp.float32)
    gram_imag = jnp.einsum("fn,gn->fg", rows_turned, rows_real, preferred_element_type=jnp.float32)
    gram_real, gram_imag = tree_sum(jnp.stack([gram_real, gram_imag]), "dom")
    last, gram_real, gram_imag = lax.optimization_barrier((flat_pieces[-1], gram_real, gram_imag))
    before.append(lax.ppermute(last, "dom", forward))
    after.append(lax.ppermute(last, "dom", backward))
    stacked = jnp.block([[gram_real, -gram_imag], [gram_imag, gram_real]])
    rank_value = rank_cap[0].astype(jnp.float32)
    threshold_sq = jnp.trace(gram_real) / rank_value
    shrink = shrink_of(stacked, threshold_sq, rank_value)
    shrink_real = shrink[:frame_count, :frame_count].astype(jnp.bfloat16)
    shrink_imag = shrink[frame_count:, :frame_count].astype(jnp.bfloat16)
    low_t = jnp.concatenate([shrink_real, shrink_imag], axis=1).T
    taps = z_kernel.shape[0]
    filter_weights = jnp.concatenate([z_kernel[:, 0], z_kernel[:, 1]], axis=-1)
    filter_t = filter_weights.reshape(taps * frame_count, 2 * frame_count).T
    out = post_of(flat, before, after, low_t, filter_t)
    return out.reshape(image.shape)


def solution(mesh):
    return jax.shard_map(
        local,
        mesh=mesh,
        in_specs=(
            P(("groups", "dom"), None, None, None),
            P(("groups", "dom"), None, None, None),
            P(("groups", "dom"), None, None, None),
            P(("groups", "dom"), None),
            P(("groups", "dom"), None, None, None, None),
            P(),
            P(),
            P(),
        ),
        out_specs=P(("groups", "dom"), None, None, None),
        check_vma=False,
    )
```

```python
import jax
import jax.numpy as jnp
from jax import lax
from jax.sharding import PartitionSpec as P
import functools
from jax.experimental import pallas as pl
from jax.experimental.pallas import tpu as pltpu

SOFT_CUT = 0.25


def padded_2(block, sides, width):
    for axis, dim in sides:
        count = lax.axis_size(axis)
        forward = [(i, i + 1) for i in range(count - 1)]
        backward = [(target, source) for source, target in forward]
        low = lax.ppermute(
            lax.slice_in_dim(block, block.shape[dim] - width, None, axis=dim), axis, forward
        )
        high = lax.ppermute(lax.slice_in_dim(block, 0, width, axis=dim), axis, backward)
        block = jnp.concatenate([low, block, high], axis=dim)
    return block


def rotate(field_values):
    half_width = field_values.shape[-1] // 2
    return jnp.concatenate(
        [-field_values[..., half_width:], field_values[..., :half_width]], axis=-1
    )


def complex_times(left_value, right_value):
    half_width = left_value.shape[-1] // 2
    left_real, left_imag = (left_value[..., :half_width], left_value[..., half_width:])
    right_real, right_imag = (right_value[..., :half_width], right_value[..., half_width:])
    return jnp.concatenate(
        [
            left_real * right_real - left_imag * right_imag,
            left_real * right_imag + left_imag * right_real,
        ],
        axis=-1,
    )


def conj_times(left_value, right_value):
    half_width = left_value.shape[-1] // 2
    left_real, left_imag = (left_value[..., :half_width], left_value[..., half_width:])
    right_real, right_imag = (right_value[..., :half_width], right_value[..., half_width:])
    return jnp.concatenate(
        [
            left_real * right_real + left_imag * right_imag,
            left_real * right_imag - left_imag * right_real,
        ],
        axis=-1,
    )


def grid_gradient(image_plane, plane_maps, counts, plane_map, blocks):
    frame_count, tile_count, lane_width = image_plane.shape
    read_tiles, link_count = (plane_map.shape[2], plane_map.shape[3])
    coil_count = plane_maps.shape[0]
    tile_ids = jnp.arange(tile_count, dtype=jnp.int32)

    def one_slot(spoke_slot, accum):
        tile_index = lax.dynamic_index_in_dim(plane_map, spoke_slot, axis=1, keepdims=False)
        flat_index = tile_index.reshape(frame_count, read_tiles * link_count)
        image_picked = jnp.take_along_axis(image_plane, flat_index[:, :, None], axis=1)
        image_picked = image_picked.reshape(frame_count, read_tiles, link_count, lane_width)
        maps_picked = jnp.take(plane_maps, flat_index.reshape(-1), axis=1)
        maps_picked = maps_picked.reshape(
            coil_count, frame_count, read_tiles, link_count, lane_width
        ).astype(jnp.float32)
        coil_tiles = complex_times(maps_picked, image_picked.astype(jnp.float32)[None]).astype(
            jnp.bfloat16
        )
        samples = jnp.einsum(
            "ctqji,qjio->ctqo", coil_tiles, blocks, preferred_element_type=jnp.float32
        )
        live_mask = (counts > spoke_slot).astype(jnp.float32)[None, :, None, None]
        samples = (samples * live_mask).astype(jnp.bfloat16)
        spread = jnp.einsum("ctqo,qjio->ctqji", samples, blocks, preferred_element_type=jnp.float32)
        back_sum = jnp.sum(conj_times(maps_picked, spread), axis=0)
        back_sum = back_sum.reshape(frame_count, read_tiles * link_count, lane_width)
        onehot = (flat_index[:, :, None] == tile_ids).astype(jnp.float32)
        return accum + jnp.einsum("tkn,tkw->tnw", onehot, back_sum, precision=lax.Precision.HIGHEST)

    most_spokes = jnp.max(counts)
    start_value = jnp.zeros((frame_count, tile_count, lane_width), jnp.float32)
    return lax.fori_loop(0, most_spokes, one_slot, start_value)


def gradient_kernel(idx_ref, cnt_ref, nsl_ref, img_ref, adj_ref, maps_ref,
                    bf_ref, bt_ref, btr_ref, out_ref, x_scr, rx_scr, g_scr,
                    lhs_scr, y_scr, ry_scr, mrr_ref, mii_ref, *, fb, slots, links, coils):
    b = pl.program_id(0)
    reads = links // 2
    img = img_ref[...].astype(jnp.float32)
    x_scr[...] = img
    half = img.shape[-1] // 2
    lane = lax.broadcasted_iota(jnp.int32, img.shape, 2)
    sign = jnp.where(lane < half, -1.0, 1.0).astype(jnp.float32)
    rx_scr[...] = pltpu.roll(img, half, 2) * sign

    @pl.when(b == 0)
    def _():
        maps = maps_ref[...].astype(jnp.float32)
        map_lane = lax.broadcasted_iota(jnp.int32, maps.shape, 2) < half
        swapped = pltpu.roll(maps, half, 2)
        mrr_ref[...] = jnp.where(map_lane, maps, swapped)
        mii_ref[...] = jnp.where(map_lane, swapped, maps)
    g_scr[...] = jnp.zeros_like(g_scr)
    lhs_scr[...] = jnp.zeros_like(lhs_scr)

    def slot_body(s, carry):
        for q in range(reads):
            def gather_t(t, c):
                frame = b * fb + t
                base = (frame * slots + s) * links + q * 2
                row = pl.multiple_of(t * coils, coils)
                for j in range(2):
                    p = idx_ref[base + j]
                    xv = x_scr[t, pl.ds(p, 1), :]
                    rxv = rx_scr[t, pl.ds(p, 1), :]
                    ct = mrr_ref[p] * xv + mii_ref[p] * rxv
                    lhs_scr[pl.ds(row, coils), pl.ds(j * 128, 128)] = ct.astype(jnp.bfloat16)
                return c

            lax.fori_loop(0, fb, gather_t, 0, unroll=True)
            samples = jnp.dot(lhs_scr[...], bf_ref[q], preferred_element_type=jnp.float32)
            samples = samples.astype(jnp.bfloat16)
            y_scr[...] = jnp.dot(samples, bt_ref[q], preferred_element_type=jnp.float32)
            ry_scr[...] = jnp.dot(samples, btr_ref[q], preferred_element_type=jnp.float32)

            def scatter_t(t, c):
                frame = b * fb + t
                live = cnt_ref[frame] > s
                base = (frame * slots + s) * links + q * 2
                row = pl.multiple_of(t * coils, coils)

                keep = live.astype(jnp.float32)
                for j in range(2):
                    p = idx_ref[base + j]
                    yv = y_scr[pl.ds(row, coils), pl.ds(j * 128, 128)]
                    ryv = ry_scr[pl.ds(row, coils), pl.ds(j * 128, 128)]
                    v = mrr_ref[p] * yv - mii_ref[p] * ryv
                    back = jnp.sum(v, axis=0, keepdims=True) * keep
                    g_scr[t, pl.ds(p, 1), :] = g_scr[t, pl.ds(p, 1), :] + back
                return c

            lax.fori_loop(0, fb, scatter_t, 0, unroll=True)
        return carry

    lax.fori_loop(0, nsl_ref[b], slot_body, 0)
    out_ref[...] = (x_scr[...] - (g_scr[...] - adj_ref[...].astype(jnp.float32))).astype(out_ref.dtype)


def fresh_image_of(image_plane, adjoint_plane, plane_maps, counts, plane_map, blocks):
    frame_count, tile_count, lane_width = image_plane.shape
    slots, reads, links = plane_map.shape[1], plane_map.shape[2], plane_map.shape[3]
    coils = plane_maps.shape[0]
    fb = 16 if frame_count % 16 == 0 else frame_count
    nblocks = frame_count // fb
    half = lane_width // 2
    maps_t = jnp.swapaxes(plane_maps, 0, 1)
    bf = blocks.reshape(reads, links * lane_width, lane_width)
    bt4 = jnp.transpose(blocks, (0, 3, 1, 2))
    bt = bt4.reshape(reads, lane_width, links * lane_width)
    btr = rotate(bt4).reshape(reads, lane_width, links * lane_width)
    idx = plane_map.reshape(-1).astype(jnp.int32)
    cnt = counts.astype(jnp.int32)
    nsl = jnp.minimum(jnp.max(cnt.reshape(nblocks, fb), axis=1), slots).astype(jnp.int32)
    kernel = functools.partial(
        gradient_kernel, fb=fb, slots=slots, links=reads * links, coils=coils
    )
    plane_spec = pl.BlockSpec((fb, tile_count, lane_width), lambda b, *_: (b, 0, 0))
    whole3 = lambda shape: pl.BlockSpec(shape, lambda b, *_: (0, 0, 0))
    flops = 2 * frame_count * slots * reads * coils * (links * lane_width) * lane_width * 3
    return pl.pallas_call(
        kernel,
        out_shape=jax.ShapeDtypeStruct(image_plane.shape, jnp.bfloat16),
        grid_spec=pltpu.PrefetchScalarGridSpec(
            num_scalar_prefetch=3,
            grid=(nblocks,),
            in_specs=[
                plane_spec,
                plane_spec,
                whole3(maps_t.shape),
                whole3(bf.shape),
                whole3(bt.shape),
                whole3(btr.shape),
            ],
            out_specs=plane_spec,
            scratch_shapes=[
                pltpu.VMEM((fb, tile_count, lane_width), jnp.float32),
                pltpu.VMEM((fb, tile_count, lane_width), jnp.float32),
                pltpu.VMEM((fb, tile_count, lane_width), jnp.float32),
                pltpu.VMEM((fb * coils, links * lane_width), jnp.bfloat16),
                pltpu.VMEM((fb * coils, links * lane_width), jnp.float32),
                pltpu.VMEM((fb * coils, links * lane_width), jnp.float32),
                pltpu.VMEM(maps_t.shape, jnp.float32),
                pltpu.VMEM(maps_t.shape, jnp.float32),
            ],
        ),
        compiler_params=pltpu.CompilerParams(dimension_semantics=("arbitrary",)),
        cost_estimate=pl.CostEstimate(
            flops=flops, transcendentals=0, bytes_accessed=image_plane.size * 6 + maps_t.size * 2
        ),
    )(idx, cnt, nsl, image_plane, adjoint_plane, maps_t, bf, bt, btr)


def post_kernel(x_ref, xb_ref, xa_ref, wl_ref, wz_ref, out_ref, *, cut):
    frames, width = x_ref.shape
    lane = lax.broadcasted_iota(jnp.int32, (frames, width), 1) % 128
    low_lane = lane < 64

    def turn(v):
        return jnp.where(low_lane, -pltpu.roll(v, width - 64, 1), pltpu.roll(v, 64, 1))

    def pair(v):
        return jnp.where(low_lane, pltpu.roll(v, width - 64, 1), pltpu.roll(v, 64, 1))

    def low_of(plane):
        mixed = jnp.dot(wl_ref[...], plane, preferred_element_type=jnp.float32)
        return mixed[:frames] + turn(mixed[frames:])

    def remainder_of(plane):
        return (plane.astype(jnp.float32) - low_of(plane)).astype(jnp.bfloat16)

    x = x_ref[...]
    low = low_of(x)
    rem = (x.astype(jnp.float32) - low).astype(jnp.bfloat16)
    planes = jnp.concatenate([remainder_of(xb_ref[...]), rem, remainder_of(xa_ref[...])], axis=0)
    mixed = jnp.dot(wz_ref[...], planes, preferred_element_type=jnp.float32)
    filtered = mixed[:frames] + turn(mixed[frames:])
    square = filtered * filtered
    magnitude = jnp.sqrt(square + pair(square))
    scale = jnp.maximum(magnitude - cut, 0.0) / jnp.maximum(magnitude, cut)
    out_ref[...] = (low + filtered * scale).astype(out_ref.dtype)


def post_of(plane, before, after, low_t, filter_t):
    frames, width = plane.shape
    nb = 2048 if width % 2048 == 0 else width
    lane_spec = pl.BlockSpec((frames, nb), lambda i: (0, i))
    whole2 = lambda shape: pl.BlockSpec(shape, lambda i: (0, 0))
    return pl.pallas_call(
        functools.partial(post_kernel, cut=SOFT_CUT),
        out_shape=jax.ShapeDtypeStruct(plane.shape, jnp.bfloat16),
        grid=(width // nb,),
        in_specs=[lane_spec, lane_spec, lane_spec, whole2(low_t.shape), whole2(filter_t.shape)],
        out_specs=lane_spec,
        compiler_params=pltpu.CompilerParams(dimension_semantics=("arbitrary",)),
        cost_estimate=pl.CostEstimate(
            flops=2 * width * frames * (2 * frames) * 6, transcendentals=width * frames,
            bytes_accessed=plane.size * 8,
        ),
    )(plane, before, after, low_t, filter_t)


def solve_kernel(a_ref, x0_ref, s_ref, out_ref, *, steps):
    size = a_ref.shape[0]
    rows = lax.broadcasted_iota(jnp.int32, (size, size), 0)
    cols = lax.broadcasted_iota(jnp.int32, (size, size), 1)
    twice = jnp.where(rows == cols, 2.0, 0.0).astype(jnp.float32)
    a = a_ref[...]
    high = lax.Precision.HIGHEST

    def step(i, x):
        t = jnp.dot(a, x, precision=high, preferred_element_type=jnp.float32)
        return jnp.dot(x, twice - t, precision=high, preferred_element_type=jnp.float32)

    x = x0_ref[...]
    for i in range(steps):
        x = step(i, x)
    out_ref[...] = jnp.dot(x, s_ref[...], precision=high, preferred_element_type=jnp.float32)


def shrink_of(stacked, threshold_sq, rank_value):
    size = stacked.shape[0]
    unit_matrix = jnp.eye(size, dtype=jnp.float32)
    system = stacked + threshold_sq * unit_matrix
    start = unit_matrix * (2.0 / (threshold_sq * (2.0 + rank_value)))
    whole = pl.BlockSpec(memory_space=pltpu.VMEM)
    return pl.pallas_call(
        functools.partial(solve_kernel, steps=12),
        out_shape=jax.ShapeDtypeStruct((size, size), jnp.float32),
        in_specs=[whole, whole, whole],
        out_specs=whole,
    )(system, start, stacked)


def apply_frames(mix_real, mix_imag, field_values):
    direct = jnp.einsum("fg,zftw->zgtw", mix_real, field_values, preferred_element_type=jnp.float32)
    turned = jnp.einsum(
        "fg,zftw->zgtw", mix_imag, rotate(field_values), preferred_element_type=jnp.float32
    )
    return direct + turned


def soft_shrink(filtered):
    half_width = filtered.shape[-1] // 2
    real_part, imag_part = (filtered[..., :half_width], filtered[..., half_width:])
    magnitude = jnp.sqrt(real_part * real_part + imag_part * imag_part)
    scale_values = jnp.maximum(magnitude - SOFT_CUT, 0.0) / jnp.maximum(magnitude, SOFT_CUT)
    return filtered * jnp.concatenate([scale_values, scale_values], axis=-1)


def tree_sum(value, axis):
    count = lax.axis_size(axis)
    if count & (count - 1):
        return lax.psum(value, axis)
    me = lax.axis_index(axis)
    step = 1
    while step < count:
        if step * 4 <= count:
            got = [value] + [
                lax.ppermute(value, axis, [(i, i ^ (k * step)) for i in range(count)])
                for k in range(1, 4)
            ]
            digit = (me // step) % 4
            ordered = []
            for j in range(4):
                picked = got[0]
                for k in range(1, 4):
                    picked = jnp.where((digit ^ j) == k, got[k], picked)
                ordered.append(picked)
            value = (ordered[0] + ordered[1]) + (ordered[2] + ordered[3])
            step *= 4
        else:
            value = value + lax.ppermute(value, axis, [(i, i ^ step) for i in range(count)])
            step *= 2
    return value


def gram_kernel(x_ref, out_ref):
    frames, width = x_ref.shape
    step = pl.program_id(0)

    @pl.when(step == 0)
    def _():
        out_ref[...] = jnp.zeros_like(out_ref)

    x = x_ref[...]
    wide = x.astype(jnp.float32)
    low_lane = lax.broadcasted_iota(jnp.int32, (frames, width), 1) % 128 < 64
    turned = jnp.where(low_lane, -pltpu.roll(wide, width - 64, 1), pltpu.roll(wide, 64, 1))
    turned = turned.astype(jnp.bfloat16)
    pairs = (((1,), (1,)), ((), ()))
    out_ref[0] += lax.dot_general(x, x, pairs, preferred_element_type=jnp.float32)
    out_ref[1] += lax.dot_general(turned, x, pairs, preferred_element_type=jnp.float32)


def gram_of(flat):
    frames, width = flat.shape
    nb = 2048 if width % 2048 == 0 else width
    return pl.pallas_call(
        gram_kernel,
        out_shape=jax.ShapeDtypeStruct((2, frames, frames), jnp.float32),
        grid=(width // nb,),
        in_specs=[pl.BlockSpec((frames, nb), lambda i: (0, i))],
        out_specs=pl.BlockSpec((2, frames, frames), lambda i: (0, 0, 0)),
        compiler_params=pltpu.CompilerParams(dimension_semantics=("arbitrary",)),
        cost_estimate=pl.CostEstimate(
            flops=4 * frames * frames * width, transcendentals=0, bytes_accessed=flat.size * 2
        ),
    )(flat)


def mix_frames(weights, field_values):
    half = weights.shape[1] // 2
    mixed = jnp.einsum("kh,ktw->htw", weights, field_values, preferred_element_type=jnp.float32)
    return mixed[:half] + rotate(mixed[half:])


def local(image, adjoint_data, coil_maps, spoke_counts, tile_map, blocks, z_kernel, rank_cap):
    frame_count = image.shape[1]
    fresh = fresh_image_of(
        image[0], adjoint_data[0], coil_maps[0], spoke_counts[0], tile_map[0], blocks
    )
    count = lax.axis_size("dom")
    forward = [(i, i + 1) for i in range(count - 1)]
    backward = [(target, source) for source, target in forward]
    flat = fresh.reshape(frame_count, -1)
    gram_real, gram_imag = tree_sum(gram_of(flat), "dom")
    flat, gram_real, gram_imag = lax.optimization_barrier((flat, gram_real, gram_imag))
    fresh_before = lax.ppermute(flat, "dom", forward)
    fresh_after = lax.ppermute(flat, "dom", backward)
    stacked = jnp.block([[gram_real, -gram_imag], [gram_imag, gram_real]])
    rank_value = rank_cap[0].astype(jnp.float32)
    threshold_sq = jnp.trace(gram_real) / rank_value
    shrink = shrink_of(stacked, threshold_sq, rank_value)
    shrink_real = shrink[:frame_count, :frame_count].astype(jnp.bfloat16)
    shrink_imag = shrink[frame_count:, :frame_count].astype(jnp.bfloat16)
    low_t = jnp.concatenate([shrink_real, shrink_imag], axis=1).T
    taps = z_kernel.shape[0]
    filter_weights = jnp.concatenate([z_kernel[:, 0], z_kernel[:, 1]], axis=-1)
    filter_t = filter_weights.reshape(taps * frame_count, 2 * frame_count).T
    out = post_of(flat, fresh_before, fresh_after, low_t, filter_t)
    return out.reshape(image.shape)


def solution(mesh):
    return jax.shard_map(
        local,
        mesh=mesh,
        in_specs=(
            P(("groups", "dom"), None, None, None),
            P(("groups", "dom"), None, None, None),
            P(("groups", "dom"), None, None, None),
            P(("groups", "dom"), None),
            P(("groups", "dom"), None, None, None, None),
            P(),
            P(),
            P(),
        ),
        out_specs=P(("groups", "dom"), None, None, None),
        check_vma=False,
    )
```

```python
import jax
import jax.numpy as jnp
from jax import lax
from jax.sharding import PartitionSpec as P
import functools
from jax.experimental import pallas as pl
from jax.experimental.pallas import tpu as pltpu

SOFT_CUT = 0.25


def padded_2(block, sides, width):
    for axis, dim in sides:
        count = lax.axis_size(axis)
        forward = [(i, i + 1) for i in range(count - 1)]
        backward = [(target, source) for source, target in forward]
        low = lax.ppermute(
            lax.slice_in_dim(block, block.shape[dim] - width, None, axis=dim), axis, forward
        )
        high = lax.ppermute(lax.slice_in_dim(block, 0, width, axis=dim), axis, backward)
        block = jnp.concatenate([low, block, high], axis=dim)
    return block


def rotate(field_values):
    half_width = field_values.shape[-1] // 2
    return jnp.concatenate(
        [-field_values[..., half_width:], field_values[..., :half_width]], axis=-1
    )


def complex_times(left_value, right_value):
    half_width = left_value.shape[-1] // 2
    left_real, left_imag = (left_value[..., :half_width], left_value[..., half_width:])
    right_real, right_imag = (right_value[..., :half_width], right_value[..., half_width:])
    return jnp.concatenate(
        [
            left_real * right_real - left_imag * right_imag,
            left_real * right_imag + left_imag * right_real,
        ],
        axis=-1,
    )


def conj_times(left_value, right_value):
    half_width = left_value.shape[-1] // 2
    left_real, left_imag = (left_value[..., :half_width], left_value[..., half_width:])
    right_real, right_imag = (right_value[..., :half_width], right_value[..., half_width:])
    return jnp.concatenate(
        [
            left_real * right_real + left_imag * right_imag,
            left_real * right_imag - left_imag * right_real,
        ],
        axis=-1,
    )


def grid_gradient(image_plane, plane_maps, counts, plane_map, blocks):
    frame_count, tile_count, lane_width = image_plane.shape
    read_tiles, link_count = (plane_map.shape[2], plane_map.shape[3])
    coil_count = plane_maps.shape[0]
    tile_ids = jnp.arange(tile_count, dtype=jnp.int32)

    def one_slot(spoke_slot, accum):
        tile_index = lax.dynamic_index_in_dim(plane_map, spoke_slot, axis=1, keepdims=False)
        flat_index = tile_index.reshape(frame_count, read_tiles * link_count)
        image_picked = jnp.take_along_axis(image_plane, flat_index[:, :, None], axis=1)
        image_picked = image_picked.reshape(frame_count, read_tiles, link_count, lane_width)
        maps_picked = jnp.take(plane_maps, flat_index.reshape(-1), axis=1)
        maps_picked = maps_picked.reshape(
            coil_count, frame_count, read_tiles, link_count, lane_width
        ).astype(jnp.float32)
        coil_tiles = complex_times(maps_picked, image_picked.astype(jnp.float32)[None]).astype(
            jnp.bfloat16
        )
        samples = jnp.einsum(
            "ctqji,qjio->ctqo", coil_tiles, blocks, preferred_element_type=jnp.float32
        )
        live_mask = (counts > spoke_slot).astype(jnp.float32)[None, :, None, None]
        samples = (samples * live_mask).astype(jnp.bfloat16)
        spread = jnp.einsum("ctqo,qjio->ctqji", samples, blocks, preferred_element_type=jnp.float32)
        back_sum = jnp.sum(conj_times(maps_picked, spread), axis=0)
        back_sum = back_sum.reshape(frame_count, read_tiles * link_count, lane_width)
        onehot = (flat_index[:, :, None] == tile_ids).astype(jnp.float32)
        return accum + jnp.einsum("tkn,tkw->tnw", onehot, back_sum, precision=lax.Precision.HIGHEST)

    most_spokes = jnp.max(counts)
    start_value = jnp.zeros((frame_count, tile_count, lane_width), jnp.float32)
    return lax.fori_loop(0, most_spokes, one_slot, start_value)


def gradient_kernel(idx_ref, cnt_ref, nsl_ref, img_ref, adj_ref, maps_ref,
                    bf_ref, bt_ref, btr_ref, out_ref, x_scr, rx_scr, g_scr, g2_scr,
                    lhs_a, y_a, ry_a, lhs_b, y_b, ry_b, mrr_ref, mii_ref, *, fb, slots, links,
                    coils):
    b = pl.program_id(0)
    reads = links // 2
    img = img_ref[...].astype(jnp.float32)
    x_scr[...] = img
    half = img.shape[-1] // 2
    lane = lax.broadcasted_iota(jnp.int32, img.shape, 2)
    sign = jnp.where(lane < half, -1.0, 1.0).astype(jnp.float32)
    rx_scr[...] = pltpu.roll(img, half, 2) * sign

    @pl.when(b == 0)
    def _():
        maps = maps_ref[...].astype(jnp.float32)
        map_lane = lax.broadcasted_iota(jnp.int32, maps.shape, 2) < half
        swapped = pltpu.roll(maps, half, 2)
        mrr_ref[...] = jnp.where(map_lane, maps, swapped)
        mii_ref[...] = jnp.where(map_lane, swapped, maps)
    g_scr[...] = jnp.zeros_like(g_scr)
    g2_scr[...] = jnp.zeros_like(g2_scr)
    lhs_a[...] = jnp.zeros_like(lhs_a)
    lhs_b[...] = jnp.zeros_like(lhs_b)
    accums = (g_scr, g2_scr)

    def slot_body(s, carry):
        for q in range(reads):
            lhs_scr, y_scr, ry_scr = (lhs_a, y_a, ry_a) if q % 2 == 0 else (lhs_b, y_b, ry_b)

            def gather_t(t, c):
                frame = b * fb + t
                base = (frame * slots + s) * links + q * 2
                row = pl.multiple_of(t * coils, coils)
                for j in range(2):
                    p = idx_ref[base + j]
                    xv = x_scr[t, pl.ds(p, 1), :]
                    rxv = rx_scr[t, pl.ds(p, 1), :]
                    ct = mrr_ref[p] * xv + mii_ref[p] * rxv
                    lhs_scr[pl.ds(row, coils), pl.ds(j * 128, 128)] = ct.astype(jnp.bfloat16)
                return c

            lax.fori_loop(0, fb, gather_t, 0, unroll=True)
            samples = jnp.dot(lhs_scr[...], bf_ref[q], preferred_element_type=jnp.float32)
            samples = samples.astype(jnp.bfloat16)
            y_scr[...] = jnp.dot(samples, bt_ref[q], preferred_element_type=jnp.float32)
            ry_scr[...] = jnp.dot(samples, btr_ref[q], preferred_element_type=jnp.float32)

            def scatter_t(t, c):
                frame = b * fb + t
                live = cnt_ref[frame] > s
                base = (frame * slots + s) * links + q * 2
                row = pl.multiple_of(t * coils, coils)

                keep = live.astype(jnp.float32)
                for j in range(2):
                    p = idx_ref[base + j]
                    yv = y_scr[pl.ds(row, coils), pl.ds(j * 128, 128)]
                    ryv = ry_scr[pl.ds(row, coils), pl.ds(j * 128, 128)]
                    v = mrr_ref[p] * yv - mii_ref[p] * ryv
                    back = jnp.sum(v, axis=0, keepdims=True) * keep
                    acc = accums[j]
                    acc[t, pl.ds(p, 1), :] = acc[t, pl.ds(p, 1), :] + back
                return c

            lax.fori_loop(0, fb, scatter_t, 0, unroll=True)
        return carry

    lax.fori_loop(0, nsl_ref[b], slot_body, 0)
    grad = g_scr[...] + g2_scr[...]
    out_ref[...] = (x_scr[...] - (grad - adj_ref[...].astype(jnp.float32))).astype(out_ref.dtype)


def fresh_image_of(image_plane, adjoint_plane, plane_maps, counts, plane_map, blocks):
    frame_count, tile_count, lane_width = image_plane.shape
    slots, reads, links = plane_map.shape[1], plane_map.shape[2], plane_map.shape[3]
    coils = plane_maps.shape[0]
    fb = 16 if frame_count % 16 == 0 else frame_count
    nblocks = frame_count // fb
    half = lane_width // 2
    maps_t = jnp.swapaxes(plane_maps, 0, 1)
    bf = blocks.reshape(reads, links * lane_width, lane_width)
    bt4 = jnp.transpose(blocks, (0, 3, 1, 2))
    bt = bt4.reshape(reads, lane_width, links * lane_width)
    btr = rotate(bt4).reshape(reads, lane_width, links * lane_width)
    idx = plane_map.reshape(-1).astype(jnp.int32)
    cnt = counts.astype(jnp.int32)
    nsl = jnp.minimum(jnp.max(cnt.reshape(nblocks, fb), axis=1), slots).astype(jnp.int32)
    kernel = functools.partial(
        gradient_kernel, fb=fb, slots=slots, links=reads * links, coils=coils
    )
    plane_spec = pl.BlockSpec((fb, tile_count, lane_width), lambda b, *_: (b, 0, 0))
    whole3 = lambda shape: pl.BlockSpec(shape, lambda b, *_: (0, 0, 0))
    flops = 2 * frame_count * slots * reads * coils * (links * lane_width) * lane_width * 3
    return pl.pallas_call(
        kernel,
        out_shape=jax.ShapeDtypeStruct(image_plane.shape, jnp.bfloat16),
        grid_spec=pltpu.PrefetchScalarGridSpec(
            num_scalar_prefetch=3,
            grid=(nblocks,),
            in_specs=[
                plane_spec,
                plane_spec,
                whole3(maps_t.shape),
                whole3(bf.shape),
                whole3(bt.shape),
                whole3(btr.shape),
            ],
            out_specs=plane_spec,
            scratch_shapes=[
                pltpu.VMEM((fb, tile_count, lane_width), jnp.float32),
                pltpu.VMEM((fb, tile_count, lane_width), jnp.float32),
                pltpu.VMEM((fb, tile_count, lane_width), jnp.float32),
                pltpu.VMEM((fb, tile_count, lane_width), jnp.float32),
                pltpu.VMEM((fb * coils, links * lane_width), jnp.bfloat16),
                pltpu.VMEM((fb * coils, links * lane_width), jnp.float32),
                pltpu.VMEM((fb * coils, links * lane_width), jnp.float32),
                pltpu.VMEM((fb * coils, links * lane_width), jnp.bfloat16),
                pltpu.VMEM((fb * coils, links * lane_width), jnp.float32),
                pltpu.VMEM((fb * coils, links * lane_width), jnp.float32),
                pltpu.VMEM(maps_t.shape, jnp.float32),
                pltpu.VMEM(maps_t.shape, jnp.float32),
            ],
        ),
        compiler_params=pltpu.CompilerParams(dimension_semantics=("arbitrary",)),
        cost_estimate=pl.CostEstimate(
            flops=flops, transcendentals=0, bytes_accessed=image_plane.size * 6 + maps_t.size * 2
        ),
    )(idx, cnt, nsl, image_plane, adjoint_plane, maps_t, bf, bt, btr)


def post_kernel(x_ref, xb_ref, xa_ref, wl_ref, wz_ref, out_ref, *, cut):
    frames, width = x_ref.shape
    lane = lax.broadcasted_iota(jnp.int32, (frames, width), 1) % 128
    low_lane = lane < 64

    def turn(v):
        return jnp.where(low_lane, -pltpu.roll(v, width - 64, 1), pltpu.roll(v, 64, 1))

    def pair(v):
        return jnp.where(low_lane, pltpu.roll(v, width - 64, 1), pltpu.roll(v, 64, 1))

    def low_of(plane):
        mixed = jnp.dot(wl_ref[...], plane, preferred_element_type=jnp.float32)
        return mixed[:frames] + turn(mixed[frames:])

    def remainder_of(plane):
        return (plane.astype(jnp.float32) - low_of(plane)).astype(jnp.bfloat16)

    x = x_ref[...]
    low = low_of(x)
    rem = (x.astype(jnp.float32) - low).astype(jnp.bfloat16)
    planes = jnp.concatenate([remainder_of(xb_ref[...]), rem, remainder_of(xa_ref[...])], axis=0)
    mixed = jnp.dot(wz_ref[...], planes, preferred_element_type=jnp.float32)
    filtered = mixed[:frames] + turn(mixed[frames:])
    square = filtered * filtered
    magnitude = jnp.sqrt(square + pair(square))
    scale = jnp.maximum(magnitude - cut, 0.0) / jnp.maximum(magnitude, cut)
    out_ref[...] = (low + filtered * scale).astype(out_ref.dtype)


def post_of(plane, before, after, low_t, filter_t):
    frames, width = plane.shape
    nb = 2048 if width % 2048 == 0 else width
    lane_spec = pl.BlockSpec((frames, nb), lambda i: (0, i))
    whole2 = lambda shape: pl.BlockSpec(shape, lambda i: (0, 0))
    return pl.pallas_call(
        functools.partial(post_kernel, cut=SOFT_CUT),
        out_shape=jax.ShapeDtypeStruct(plane.shape, jnp.bfloat16),
        grid=(width // nb,),
        in_specs=[lane_spec, lane_spec, lane_spec, whole2(low_t.shape), whole2(filter_t.shape)],
        out_specs=lane_spec,
        compiler_params=pltpu.CompilerParams(dimension_semantics=("arbitrary",)),
        cost_estimate=pl.CostEstimate(
            flops=2 * width * frames * (2 * frames) * 6, transcendentals=width * frames,
            bytes_accessed=plane.size * 8,
        ),
    )(plane, before, after, low_t, filter_t)


def solve_kernel(a_ref, x0_ref, s_ref, out_ref, *, steps):
    size = a_ref.shape[0]
    rows = lax.broadcasted_iota(jnp.int32, (size, size), 0)
    cols = lax.broadcasted_iota(jnp.int32, (size, size), 1)
    twice = jnp.where(rows == cols, 2.0, 0.0).astype(jnp.float32)
    a = a_ref[...]
    high = lax.Precision.HIGHEST

    def step(i, x):
        t = jnp.dot(a, x, precision=high, preferred_element_type=jnp.float32)
        return jnp.dot(x, twice - t, precision=high, preferred_element_type=jnp.float32)

    x = x0_ref[...]
    for i in range(steps):
        x = step(i, x)
    out_ref[...] = jnp.dot(x, s_ref[...], precision=high, preferred_element_type=jnp.float32)


def shrink_of(stacked, threshold_sq, rank_value):
    size = stacked.shape[0]
    unit_matrix = jnp.eye(size, dtype=jnp.float32)
    system = stacked + threshold_sq * unit_matrix
    start = unit_matrix * (2.0 / (threshold_sq * (2.0 + rank_value)))
    whole = pl.BlockSpec(memory_space=pltpu.VMEM)
    return pl.pallas_call(
        functools.partial(solve_kernel, steps=12),
        out_shape=jax.ShapeDtypeStruct((size, size), jnp.float32),
        in_specs=[whole, whole, whole],
        out_specs=whole,
    )(system, start, stacked)


def apply_frames(mix_real, mix_imag, field_values):
    direct = jnp.einsum("fg,zftw->zgtw", mix_real, field_values, preferred_element_type=jnp.float32)
    turned = jnp.einsum(
        "fg,zftw->zgtw", mix_imag, rotate(field_values), preferred_element_type=jnp.float32
    )
    return direct + turned


def soft_shrink(filtered):
    half_width = filtered.shape[-1] // 2
    real_part, imag_part = (filtered[..., :half_width], filtered[..., half_width:])
    magnitude = jnp.sqrt(real_part * real_part + imag_part * imag_part)
    scale_values = jnp.maximum(magnitude - SOFT_CUT, 0.0) / jnp.maximum(magnitude, SOFT_CUT)
    return filtered * jnp.concatenate([scale_values, scale_values], axis=-1)


def tree_sum(value, axis):
    count = lax.axis_size(axis)
    if count & (count - 1):
        return lax.psum(value, axis)
    step = 1
    while step < count:
        pairs = [(i, i ^ step) for i in range(count)]
        value = value + lax.ppermute(value, axis, pairs)
        step *= 2
    return value


def mix_frames(weights, field_values):
    half = weights.shape[1] // 2
    mixed = jnp.einsum("kh,ktw->htw", weights, field_values, preferred_element_type=jnp.float32)
    return mixed[:half] + rotate(mixed[half:])


def local(image, adjoint_data, coil_maps, spoke_counts, tile_map, blocks, z_kernel, rank_cap):
    frame_count = image.shape[1]
    fresh = fresh_image_of(
        image[0], adjoint_data[0], coil_maps[0], spoke_counts[0], tile_map[0], blocks
    )
    count = lax.axis_size("dom")
    forward = [(i, i + 1) for i in range(count - 1)]
    backward = [(target, source) for source, target in forward]
    flat = fresh.reshape(frame_count, -1)
    rows_real = flat
    rows_turned = rotate(fresh).reshape(frame_count, -1)
    gram_real = jnp.einsum("fn,gn->fg", rows_real, rows_real, preferred_element_type=jnp.float32)
    gram_imag = jnp.einsum("fn,gn->fg", rows_turned, rows_real, preferred_element_type=jnp.float32)
    gram_real, gram_imag = tree_sum(jnp.stack([gram_real, gram_imag]), "dom")
    flat, gram_real, gram_imag = lax.optimization_barrier((flat, gram_real, gram_imag))
    fresh_before = lax.ppermute(flat, "dom", forward)
    fresh_after = lax.ppermute(flat, "dom", backward)
    stacked = jnp.block([[gram_real, -gram_imag], [gram_imag, gram_real]])
    rank_value = rank_cap[0].astype(jnp.float32)
    threshold_sq = jnp.trace(gram_real) / rank_value
    shrink = shrink_of(stacked, threshold_sq, rank_value)
    shrink_real = shrink[:frame_count, :frame_count].astype(jnp.bfloat16)
    shrink_imag = shrink[frame_count:, :frame_count].astype(jnp.bfloat16)
    low_t = jnp.concatenate([shrink_real, shrink_imag], axis=1).T
    taps = z_kernel.shape[0]
    filter_weights = jnp.concatenate([z_kernel[:, 0], z_kernel[:, 1]], axis=-1)
    filter_t = filter_weights.reshape(taps * frame_count, 2 * frame_count).T
    out = post_of(flat, fresh_before, fresh_after, low_t, filter_t)
    return out.reshape(image.shape)


def solution(mesh):
    return jax.shard_map(
        local,
        mesh=mesh,
        in_specs=(
            P(("groups", "dom"), None, None, None),
            P(("groups", "dom"), None, None, None),
            P(("groups", "dom"), None, None, None),
            P(("groups", "dom"), None),
            P(("groups", "dom"), None, None, None, None),
            P(),
            P(),
            P(),
        ),
        out_specs=P(("groups", "dom"), None, None, None),
        check_vma=False,
    )
```

```python
import jax
import jax.numpy as jnp
from jax import lax
from jax.sharding import PartitionSpec as P
import functools
from jax.experimental import pallas as pl
from jax.experimental.pallas import tpu as pltpu

SOFT_CUT = 0.25


def padded_2(block, sides, width):
    for axis, dim in sides:
        count = lax.axis_size(axis)
        forward = [(i, i + 1) for i in range(count - 1)]
        backward = [(target, source) for source, target in forward]
        low = lax.ppermute(
            lax.slice_in_dim(block, block.shape[dim] - width, None, axis=dim), axis, forward
        )
        high = lax.ppermute(lax.slice_in_dim(block, 0, width, axis=dim), axis, backward)
        block = jnp.concatenate([low, block, high], axis=dim)
    return block


def rotate(field_values):
    half_width = field_values.shape[-1] // 2
    return jnp.concatenate(
        [-field_values[..., half_width:], field_values[..., :half_width]], axis=-1
    )


def complex_times(left_value, right_value):
    half_width = left_value.shape[-1] // 2
    left_real, left_imag = (left_value[..., :half_width], left_value[..., half_width:])
    right_real, right_imag = (right_value[..., :half_width], right_value[..., half_width:])
    return jnp.concatenate(
        [
            left_real * right_real - left_imag * right_imag,
            left_real * right_imag + left_imag * right_real,
        ],
        axis=-1,
    )


def conj_times(left_value, right_value):
    half_width = left_value.shape[-1] // 2
    left_real, left_imag = (left_value[..., :half_width], left_value[..., half_width:])
    right_real, right_imag = (right_value[..., :half_width], right_value[..., half_width:])
    return jnp.concatenate(
        [
            left_real * right_real + left_imag * right_imag,
            left_real * right_imag - left_imag * right_real,
        ],
        axis=-1,
    )


def grid_gradient(image_plane, plane_maps, counts, plane_map, blocks):
    frame_count, tile_count, lane_width = image_plane.shape
    read_tiles, link_count = (plane_map.shape[2], plane_map.shape[3])
    coil_count = plane_maps.shape[0]
    tile_ids = jnp.arange(tile_count, dtype=jnp.int32)

    def one_slot(spoke_slot, accum):
        tile_index = lax.dynamic_index_in_dim(plane_map, spoke_slot, axis=1, keepdims=False)
        flat_index = tile_index.reshape(frame_count, read_tiles * link_count)
        image_picked = jnp.take_along_axis(image_plane, flat_index[:, :, None], axis=1)
        image_picked = image_picked.reshape(frame_count, read_tiles, link_count, lane_width)
        maps_picked = jnp.take(plane_maps, flat_index.reshape(-1), axis=1)
        maps_picked = maps_picked.reshape(
            coil_count, frame_count, read_tiles, link_count, lane_width
        ).astype(jnp.float32)
        coil_tiles = complex_times(maps_picked, image_picked.astype(jnp.float32)[None]).astype(
            jnp.bfloat16
        )
        samples = jnp.einsum(
            "ctqji,qjio->ctqo", coil_tiles, blocks, preferred_element_type=jnp.float32
        )
        live_mask = (counts > spoke_slot).astype(jnp.float32)[None, :, None, None]
        samples = (samples * live_mask).astype(jnp.bfloat16)
        spread = jnp.einsum("ctqo,qjio->ctqji", samples, blocks, preferred_element_type=jnp.float32)
        back_sum = jnp.sum(conj_times(maps_picked, spread), axis=0)
        back_sum = back_sum.reshape(frame_count, read_tiles * link_count, lane_width)
        onehot = (flat_index[:, :, None] == tile_ids).astype(jnp.float32)
        return accum + jnp.einsum("tkn,tkw->tnw", onehot, back_sum, precision=lax.Precision.HIGHEST)

    most_spokes = jnp.max(counts)
    start_value = jnp.zeros((frame_count, tile_count, lane_width), jnp.float32)
    return lax.fori_loop(0, most_spokes, one_slot, start_value)


def gradient_kernel(idx_ref, cnt_ref, nsl_ref, img_ref, adj_ref, maps_ref,
                    bf_ref, bt_ref, btr_ref, out_ref, x_scr, rx_scr, g_scr, g2_scr,
                    lhs_a, y_a, ry_a, lhs_b, y_b, ry_b, mrr_ref, mii_ref, *, fb, slots, links,
                    coils):
    b = pl.program_id(0)
    reads = links // 2
    img = img_ref[...].astype(jnp.float32)
    x_scr[...] = img
    half = img.shape[-1] // 2
    lane = lax.broadcasted_iota(jnp.int32, img.shape, 2)
    sign = jnp.where(lane < half, -1.0, 1.0).astype(jnp.float32)
    rx_scr[...] = pltpu.roll(img, half, 2) * sign

    @pl.when(b == 0)
    def _():
        maps = maps_ref[...].astype(jnp.float32)
        map_lane = lax.broadcasted_iota(jnp.int32, maps.shape, 2) < half
        swapped = pltpu.roll(maps, half, 2)
        mrr_ref[...] = jnp.where(map_lane, maps, swapped)
        mii_ref[...] = jnp.where(map_lane, swapped, maps)
    g_scr[...] = jnp.zeros_like(g_scr)
    g2_scr[...] = jnp.zeros_like(g2_scr)
    lhs_a[...] = jnp.zeros_like(lhs_a)
    lhs_b[...] = jnp.zeros_like(lhs_b)
    accums = (g_scr, g2_scr)

    def slot_body(s, carry):
        for q in range(reads):
            lhs_scr, y_scr, ry_scr = (lhs_a, y_a, ry_a) if q % 2 == 0 else (lhs_b, y_b, ry_b)

            def gather_t(t, c):
                frame = b * fb + t
                base = (frame * slots + s) * links + q * 2
                row = pl.multiple_of(t * coils, coils)
                for j in range(2):
                    p = idx_ref[base + j]
                    xv = x_scr[t, pl.ds(p, 1), :]
                    rxv = rx_scr[t, pl.ds(p, 1), :]
                    ct = mrr_ref[p] * xv + mii_ref[p] * rxv
                    lhs_scr[pl.ds(row, coils), pl.ds(j * 128, 128)] = ct.astype(jnp.bfloat16)
                return c

            lax.fori_loop(0, fb, gather_t, 0, unroll=True)
            samples = jnp.dot(lhs_scr[...], bf_ref[q], preferred_element_type=jnp.float32)
            samples = samples.astype(jnp.bfloat16)
            y_scr[...] = jnp.dot(samples, bt_ref[q], preferred_element_type=jnp.float32)
            ry_scr[...] = jnp.dot(samples, btr_ref[q], preferred_element_type=jnp.float32)

            def scatter_t(t, c):
                frame = b * fb + t
                live = cnt_ref[frame] > s
                base = (frame * slots + s) * links + q * 2
                row = pl.multiple_of(t * coils, coils)

                keep = live.astype(jnp.float32)
                for j in range(2):
                    p = idx_ref[base + j]
                    yv = y_scr[pl.ds(row, coils), pl.ds(j * 128, 128)]
                    ryv = ry_scr[pl.ds(row, coils), pl.ds(j * 128, 128)]
                    v = mrr_ref[p] * yv - mii_ref[p] * ryv
                    back = jnp.sum(v, axis=0, keepdims=True) * keep
                    acc = accums[j]
                    acc[t, pl.ds(p, 1), :] = acc[t, pl.ds(p, 1), :] + back
                return c

            lax.fori_loop(0, fb, scatter_t, 0, unroll=True)
        return carry

    lax.fori_loop(0, nsl_ref[b], slot_body, 0)
    grad = g_scr[...] + g2_scr[...]
    out_ref[...] = (x_scr[...] - (grad - adj_ref[...].astype(jnp.float32))).astype(out_ref.dtype)


def fresh_image_of(image_plane, adjoint_plane, plane_maps, counts, plane_map, blocks):
    frame_count, tile_count, lane_width = image_plane.shape
    slots, reads, links = plane_map.shape[1], plane_map.shape[2], plane_map.shape[3]
    coils = plane_maps.shape[0]
    fb = 16 if frame_count % 16 == 0 else frame_count
    nblocks = frame_count // fb
    half = lane_width // 2
    maps_t = jnp.swapaxes(plane_maps, 0, 1)
    bf = blocks.reshape(reads, links * lane_width, lane_width)
    bt4 = jnp.transpose(blocks, (0, 3, 1, 2))
    bt = bt4.reshape(reads, lane_width, links * lane_width)
    btr = rotate(bt4).reshape(reads, lane_width, links * lane_width)
    idx = plane_map.reshape(-1).astype(jnp.int32)
    cnt = counts.astype(jnp.int32)
    nsl = jnp.minimum(jnp.max(cnt.reshape(nblocks, fb), axis=1), slots).astype(jnp.int32)
    kernel = functools.partial(
        gradient_kernel, fb=fb, slots=slots, links=reads * links, coils=coils
    )
    plane_spec = pl.BlockSpec((fb, tile_count, lane_width), lambda b, *_: (b, 0, 0))
    whole3 = lambda shape: pl.BlockSpec(shape, lambda b, *_: (0, 0, 0))
    flops = 2 * frame_count * slots * reads * coils * (links * lane_width) * lane_width * 3
    return pl.pallas_call(
        kernel,
        out_shape=jax.ShapeDtypeStruct(image_plane.shape, jnp.bfloat16),
        grid_spec=pltpu.PrefetchScalarGridSpec(
            num_scalar_prefetch=3,
            grid=(nblocks,),
            in_specs=[
                plane_spec,
                plane_spec,
                whole3(maps_t.shape),
                whole3(bf.shape),
                whole3(bt.shape),
                whole3(btr.shape),
            ],
            out_specs=plane_spec,
            scratch_shapes=[
                pltpu.VMEM((fb, tile_count, lane_width), jnp.float32),
                pltpu.VMEM((fb, tile_count, lane_width), jnp.float32),
                pltpu.VMEM((fb, tile_count, lane_width), jnp.float32),
                pltpu.VMEM((fb, tile_count, lane_width), jnp.float32),
                pltpu.VMEM((fb * coils, links * lane_width), jnp.bfloat16),
                pltpu.VMEM((fb * coils, links * lane_width), jnp.float32),
                pltpu.VMEM((fb * coils, links * lane_width), jnp.float32),
                pltpu.VMEM((fb * coils, links * lane_width), jnp.bfloat16),
                pltpu.VMEM((fb * coils, links * lane_width), jnp.float32),
                pltpu.VMEM((fb * coils, links * lane_width), jnp.float32),
                pltpu.VMEM(maps_t.shape, jnp.float32),
                pltpu.VMEM(maps_t.shape, jnp.float32),
            ],
        ),
        compiler_params=pltpu.CompilerParams(dimension_semantics=("arbitrary",)),
        cost_estimate=pl.CostEstimate(
            flops=flops, transcendentals=0, bytes_accessed=image_plane.size * 6 + maps_t.size * 2
        ),
    )(idx, cnt, nsl, image_plane, adjoint_plane, maps_t, bf, bt, btr)


def post_kernel(x_ref, xb_ref, xa_ref, wl_ref, wz_ref, out_ref, *, cut):
    frames, width = x_ref.shape
    lane = lax.broadcasted_iota(jnp.int32, (frames, width), 1) % 128
    low_lane = lane < 64

    def turn(v):
        return jnp.where(low_lane, -pltpu.roll(v, width - 64, 1), pltpu.roll(v, 64, 1))

    def pair(v):
        return jnp.where(low_lane, pltpu.roll(v, width - 64, 1), pltpu.roll(v, 64, 1))

    def low_of(plane):
        mixed = jnp.dot(wl_ref[...], plane, preferred_element_type=jnp.float32)
        return mixed[:frames] + turn(mixed[frames:])

    def remainder_of(plane):
        return (plane.astype(jnp.float32) - low_of(plane)).astype(jnp.bfloat16)

    x = x_ref[...]
    low = low_of(x)
    rem = (x.astype(jnp.float32) - low).astype(jnp.bfloat16)
    planes = jnp.concatenate([remainder_of(xb_ref[...]), rem, remainder_of(xa_ref[...])], axis=0)
    mixed = jnp.dot(wz_ref[...], planes, preferred_element_type=jnp.float32)
    filtered = mixed[:frames] + turn(mixed[frames:])
    square = filtered * filtered
    magnitude = jnp.sqrt(square + pair(square))
    scale = jnp.maximum(magnitude - cut, 0.0) / jnp.maximum(magnitude, cut)
    out_ref[...] = (low + filtered * scale).astype(out_ref.dtype)


def post_of(plane, before, after, low_t, filter_t):
    frames, width = plane.shape
    nb = 2048 if width % 2048 == 0 else width
    lane_spec = pl.BlockSpec((frames, nb), lambda i: (0, i))
    whole2 = lambda shape: pl.BlockSpec(shape, lambda i: (0, 0))
    return pl.pallas_call(
        functools.partial(post_kernel, cut=SOFT_CUT),
        out_shape=jax.ShapeDtypeStruct(plane.shape, jnp.bfloat16),
        grid=(width // nb,),
        in_specs=[lane_spec, lane_spec, lane_spec, whole2(low_t.shape), whole2(filter_t.shape)],
        out_specs=lane_spec,
        compiler_params=pltpu.CompilerParams(dimension_semantics=("arbitrary",)),
        cost_estimate=pl.CostEstimate(
            flops=2 * width * frames * (2 * frames) * 6, transcendentals=width * frames,
            bytes_accessed=plane.size * 8,
        ),
    )(plane, before, after, low_t, filter_t)


def solve_kernel(a_ref, x0_ref, s_ref, out_ref, *, steps):
    size = a_ref.shape[0]
    rows = lax.broadcasted_iota(jnp.int32, (size, size), 0)
    cols = lax.broadcasted_iota(jnp.int32, (size, size), 1)
    twice = jnp.where(rows == cols, 2.0, 0.0).astype(jnp.float32)
    a = a_ref[...]
    high = lax.Precision.HIGHEST

    def step(i, x):
        t = jnp.dot(a, x, precision=high, preferred_element_type=jnp.float32)
        return jnp.dot(x, twice - t, precision=high, preferred_element_type=jnp.float32)

    x = x0_ref[...]
    for i in range(steps):
        x = step(i, x)
    out_ref[...] = jnp.dot(x, s_ref[...], precision=high, preferred_element_type=jnp.float32)


def shrink_of(stacked, threshold_sq, rank_value):
    size = stacked.shape[0]
    unit_matrix = jnp.eye(size, dtype=jnp.float32)
    system = stacked + threshold_sq * unit_matrix
    start = unit_matrix * (2.0 / (threshold_sq * (2.0 + rank_value)))
    whole = pl.BlockSpec(memory_space=pltpu.VMEM)
    return pl.pallas_call(
        functools.partial(solve_kernel, steps=12),
        out_shape=jax.ShapeDtypeStruct((size, size), jnp.float32),
        in_specs=[whole, whole, whole],
        out_specs=whole,
    )(system, start, stacked)


def apply_frames(mix_real, mix_imag, field_values):
    direct = jnp.einsum("fg,zftw->zgtw", mix_real, field_values, preferred_element_type=jnp.float32)
    turned = jnp.einsum(
        "fg,zftw->zgtw", mix_imag, rotate(field_values), preferred_element_type=jnp.float32
    )
    return direct + turned


def soft_shrink(filtered):
    half_width = filtered.shape[-1] // 2
    real_part, imag_part = (filtered[..., :half_width], filtered[..., half_width:])
    magnitude = jnp.sqrt(real_part * real_part + imag_part * imag_part)
    scale_values = jnp.maximum(magnitude - SOFT_CUT, 0.0) / jnp.maximum(magnitude, SOFT_CUT)
    return filtered * jnp.concatenate([scale_values, scale_values], axis=-1)


def tree_sum(value, axis):
    count = lax.axis_size(axis)
    if count & (count - 1):
        return lax.psum(value, axis)
    step = 1
    while step < count:
        pairs = [(i, i ^ step) for i in range(count)]
        value = value + lax.ppermute(value, axis, pairs)
        step *= 2
    return value


def mix_frames(weights, field_values):
    half = weights.shape[1] // 2
    mixed = jnp.einsum("kh,ktw->htw", weights, field_values, preferred_element_type=jnp.float32)
    return mixed[:half] + rotate(mixed[half:])


def local(image, adjoint_data, coil_maps, spoke_counts, tile_map, blocks, z_kernel, rank_cap):
    frame_count = image.shape[1]
    fresh = fresh_image_of(
        image[0], adjoint_data[0], coil_maps[0], spoke_counts[0], tile_map[0], blocks
    )
    count = lax.axis_size("dom")
    forward = [(i, i + 1) for i in range(count - 1)]
    backward = [(target, source) for source, target in forward]
    flat = fresh.reshape(frame_count, -1)
    rows_real = flat
    rows_turned = rotate(fresh).reshape(frame_count, -1)
    gram_real = jnp.einsum("fn,gn->fg", rows_real, rows_real, preferred_element_type=jnp.float32)
    gram_imag = jnp.einsum("fn,gn->fg", rows_turned, rows_real, preferred_element_type=jnp.float32)
    fresh_before = lax.ppermute(flat, "dom", forward)
    fresh_after = lax.ppermute(flat, "dom", backward)
    gram_real, gram_imag = tree_sum(jnp.stack([gram_real, gram_imag]), "dom")
    stacked = jnp.block([[gram_real, -gram_imag], [gram_imag, gram_real]])
    rank_value = rank_cap[0].astype(jnp.float32)
    threshold_sq = jnp.trace(gram_real) / rank_value
    shrink = shrink_of(stacked, threshold_sq, rank_value)
    shrink_real = shrink[:frame_count, :frame_count].astype(jnp.bfloat16)
    shrink_imag = shrink[frame_count:, :frame_count].astype(jnp.bfloat16)
    low_t = jnp.concatenate([shrink_real, shrink_imag], axis=1).T
    taps = z_kernel.shape[0]
    filter_weights = jnp.concatenate([z_kernel[:, 0], z_kernel[:, 1]], axis=-1)
    filter_t = filter_weights.reshape(taps * frame_count, 2 * frame_count).T
    out = post_of(flat, fresh_before, fresh_after, low_t, filter_t)
    return out.reshape(image.shape)


def solution(mesh):
    return jax.shard_map(
        local,
        mesh=mesh,
        in_specs=(
            P(("groups", "dom"), None, None, None),
            P(("groups", "dom"), None, None, None),
            P(("groups", "dom"), None, None, None),
            P(("groups", "dom"), None),
            P(("groups", "dom"), None, None, None, None),
            P(),
            P(),
            P(),
        ),
        out_specs=P(("groups", "dom"), None, None, None),
        check_vma=False,
    )
```

```python
import jax
import jax.numpy as jnp
from jax import lax
from jax.sharding import PartitionSpec as P
import functools
from jax.experimental import pallas as pl
from jax.experimental.pallas import tpu as pltpu

SOFT_CUT = 0.25


def padded_2(block, sides, width):
    for axis, dim in sides:
        count = lax.axis_size(axis)
        forward = [(i, i + 1) for i in range(count - 1)]
        backward = [(target, source) for source, target in forward]
        low = lax.ppermute(
            lax.slice_in_dim(block, block.shape[dim] - width, None, axis=dim), axis, forward
        )
        high = lax.ppermute(lax.slice_in_dim(block, 0, width, axis=dim), axis, backward)
        block = jnp.concatenate([low, block, high], axis=dim)
    return block


def rotate(field_values):
    half_width = field_values.shape[-1] // 2
    return jnp.concatenate(
        [-field_values[..., half_width:], field_values[..., :half_width]], axis=-1
    )


def complex_times(left_value, right_value):
    half_width = left_value.shape[-1] // 2
    left_real, left_imag = (left_value[..., :half_width], left_value[..., half_width:])
    right_real, right_imag = (right_value[..., :half_width], right_value[..., half_width:])
    return jnp.concatenate(
        [
            left_real * right_real - left_imag * right_imag,
            left_real * right_imag + left_imag * right_real,
        ],
        axis=-1,
    )


def conj_times(left_value, right_value):
    half_width = left_value.shape[-1] // 2
    left_real, left_imag = (left_value[..., :half_width], left_value[..., half_width:])
    right_real, right_imag = (right_value[..., :half_width], right_value[..., half_width:])
    return jnp.concatenate(
        [
            left_real * right_real + left_imag * right_imag,
            left_real * right_imag - left_imag * right_real,
        ],
        axis=-1,
    )


def grid_gradient(image_plane, plane_maps, counts, plane_map, blocks):
    frame_count, tile_count, lane_width = image_plane.shape
    read_tiles, link_count = (plane_map.shape[2], plane_map.shape[3])
    coil_count = plane_maps.shape[0]
    tile_ids = jnp.arange(tile_count, dtype=jnp.int32)

    def one_slot(spoke_slot, accum):
        tile_index = lax.dynamic_index_in_dim(plane_map, spoke_slot, axis=1, keepdims=False)
        flat_index = tile_index.reshape(frame_count, read_tiles * link_count)
        image_picked = jnp.take_along_axis(image_plane, flat_index[:, :, None], axis=1)
        image_picked = image_picked.reshape(frame_count, read_tiles, link_count, lane_width)
        maps_picked = jnp.take(plane_maps, flat_index.reshape(-1), axis=1)
        maps_picked = maps_picked.reshape(
            coil_count, frame_count, read_tiles, link_count, lane_width
        ).astype(jnp.float32)
        coil_tiles = complex_times(maps_picked, image_picked.astype(jnp.float32)[None]).astype(
            jnp.bfloat16
        )
        samples = jnp.einsum(
            "ctqji,qjio->ctqo", coil_tiles, blocks, preferred_element_type=jnp.float32
        )
        live_mask = (counts > spoke_slot).astype(jnp.float32)[None, :, None, None]
        samples = (samples * live_mask).astype(jnp.bfloat16)
        spread = jnp.einsum("ctqo,qjio->ctqji", samples, blocks, preferred_element_type=jnp.float32)
        back_sum = jnp.sum(conj_times(maps_picked, spread), axis=0)
        back_sum = back_sum.reshape(frame_count, read_tiles * link_count, lane_width)
        onehot = (flat_index[:, :, None] == tile_ids).astype(jnp.float32)
        return accum + jnp.einsum("tkn,tkw->tnw", onehot, back_sum, precision=lax.Precision.HIGHEST)

    most_spokes = jnp.max(counts)
    start_value = jnp.zeros((frame_count, tile_count, lane_width), jnp.float32)
    return lax.fori_loop(0, most_spokes, one_slot, start_value)


def gradient_kernel(idx_ref, cnt_ref, nsl_ref, img_ref, adj_ref, maps_ref,
                    bf_ref, bt_ref, btr_ref, out_ref, x_scr, rx_scr, g_scr, g2_scr,
                    lhs_a, y_a, ry_a, lhs_b, y_b, ry_b, mrr_ref, mii_ref, *, fb, slots, links,
                    coils):
    b = pl.program_id(0)
    reads = links // 2
    img = img_ref[...].astype(jnp.float32)
    x_scr[...] = img
    half = img.shape[-1] // 2
    lane = lax.broadcasted_iota(jnp.int32, img.shape, 2)
    sign = jnp.where(lane < half, -1.0, 1.0).astype(jnp.float32)
    rx_scr[...] = pltpu.roll(img, half, 2) * sign

    @pl.when(b == 0)
    def _():
        maps = maps_ref[...].astype(jnp.float32)
        map_lane = lax.broadcasted_iota(jnp.int32, maps.shape, 2) < half
        swapped = pltpu.roll(maps, half, 2)
        mrr_ref[...] = jnp.where(map_lane, maps, swapped)
        mii_ref[...] = jnp.where(map_lane, swapped, maps)
    g_scr[...] = jnp.zeros_like(g_scr)
    g2_scr[...] = jnp.zeros_like(g2_scr)
    lhs_a[...] = jnp.zeros_like(lhs_a)
    lhs_b[...] = jnp.zeros_like(lhs_b)
    accums = (g_scr, g2_scr)

    def slot_body(s, carry):
        for q in range(reads):
            lhs_scr, y_scr, ry_scr = (lhs_a, y_a, ry_a) if q % 2 == 0 else (lhs_b, y_b, ry_b)

            def gather_t(t, c):
                frame = b * fb + t
                base = (frame * slots + s) * links + q * 2
                row = pl.multiple_of(t * coils, coils)
                for j in range(2):
                    p = idx_ref[base + j]
                    xv = x_scr[t, pl.ds(p, 1), :]
                    rxv = rx_scr[t, pl.ds(p, 1), :]
                    ct = mrr_ref[p] * xv + mii_ref[p] * rxv
                    lhs_scr[pl.ds(row, coils), pl.ds(j * 128, 128)] = ct.astype(jnp.bfloat16)
                return c

            lax.fori_loop(0, fb, gather_t, 0, unroll=True)
            samples = jnp.dot(lhs_scr[...], bf_ref[q], preferred_element_type=jnp.float32)
            samples = samples.astype(jnp.bfloat16)
            y_scr[...] = jnp.dot(samples, bt_ref[q], preferred_element_type=jnp.float32)
            ry_scr[...] = jnp.dot(samples, btr_ref[q], preferred_element_type=jnp.float32)

            def scatter_t(t, c):
                frame = b * fb + t
                live = cnt_ref[frame] > s
                base = (frame * slots + s) * links + q * 2
                row = pl.multiple_of(t * coils, coils)

                keep = live.astype(jnp.float32)
                for j in range(2):
                    p = idx_ref[base + j]
                    yv = y_scr[pl.ds(row, coils), pl.ds(j * 128, 128)]
                    ryv = ry_scr[pl.ds(row, coils), pl.ds(j * 128, 128)]
                    v = mrr_ref[p] * yv - mii_ref[p] * ryv
                    back = jnp.sum(v, axis=0, keepdims=True) * keep
                    acc = accums[j]
                    acc[t, pl.ds(p, 1), :] = acc[t, pl.ds(p, 1), :] + back
                return c

            lax.fori_loop(0, fb, scatter_t, 0, unroll=True)
        return carry

    lax.fori_loop(0, nsl_ref[b], slot_body, 0)
    grad = g_scr[...] + g2_scr[...]
    out_ref[...] = (x_scr[...] - (grad - adj_ref[...].astype(jnp.float32))).astype(out_ref.dtype)


def fresh_image_of(image_plane, adjoint_plane, plane_maps, counts, plane_map, blocks):
    frame_count, tile_count, lane_width = image_plane.shape
    slots, reads, links = plane_map.shape[1], plane_map.shape[2], plane_map.shape[3]
    coils = plane_maps.shape[0]
    fb = 32 if frame_count % 32 == 0 else frame_count
    nblocks = frame_count // fb
    half = lane_width // 2
    maps_t = jnp.swapaxes(plane_maps, 0, 1)
    bf = blocks.reshape(reads, links * lane_width, lane_width)
    bt4 = jnp.transpose(blocks, (0, 3, 1, 2))
    bt = bt4.reshape(reads, lane_width, links * lane_width)
    btr = rotate(bt4).reshape(reads, lane_width, links * lane_width)
    idx = plane_map.reshape(-1).astype(jnp.int32)
    cnt = counts.astype(jnp.int32)
    nsl = jnp.minimum(jnp.max(cnt.reshape(nblocks, fb), axis=1), slots).astype(jnp.int32)
    kernel = functools.partial(
        gradient_kernel, fb=fb, slots=slots, links=reads * links, coils=coils
    )
    plane_spec = pl.BlockSpec((fb, tile_count, lane_width), lambda b, *_: (b, 0, 0))
    whole3 = lambda shape: pl.BlockSpec(shape, lambda b, *_: (0, 0, 0))
    flops = 2 * frame_count * slots * reads * coils * (links * lane_width) * lane_width * 3
    return pl.pallas_call(
        kernel,
        out_shape=jax.ShapeDtypeStruct(image_plane.shape, jnp.bfloat16),
        grid_spec=pltpu.PrefetchScalarGridSpec(
            num_scalar_prefetch=3,
            grid=(nblocks,),
            in_specs=[
                plane_spec,
                plane_spec,
                whole3(maps_t.shape),
                whole3(bf.shape),
                whole3(bt.shape),
                whole3(btr.shape),
            ],
            out_specs=plane_spec,
            scratch_shapes=[
                pltpu.VMEM((fb, tile_count, lane_width), jnp.float32),
                pltpu.VMEM((fb, tile_count, lane_width), jnp.float32),
                pltpu.VMEM((fb, tile_count, lane_width), jnp.float32),
                pltpu.VMEM((fb, tile_count, lane_width), jnp.float32),
                pltpu.VMEM((fb * coils, links * lane_width), jnp.bfloat16),
                pltpu.VMEM((fb * coils, links * lane_width), jnp.float32),
                pltpu.VMEM((fb * coils, links * lane_width), jnp.float32),
                pltpu.VMEM((fb * coils, links * lane_width), jnp.bfloat16),
                pltpu.VMEM((fb * coils, links * lane_width), jnp.float32),
                pltpu.VMEM((fb * coils, links * lane_width), jnp.float32),
                pltpu.VMEM(maps_t.shape, jnp.float32),
                pltpu.VMEM(maps_t.shape, jnp.float32),
            ],
        ),
        compiler_params=pltpu.CompilerParams(dimension_semantics=("arbitrary",)),
        cost_estimate=pl.CostEstimate(
            flops=flops, transcendentals=0, bytes_accessed=image_plane.size * 6 + maps_t.size * 2
        ),
    )(idx, cnt, nsl, image_plane, adjoint_plane, maps_t, bf, bt, btr)


def post_kernel(x_ref, xb_ref, xa_ref, wl_ref, wz_ref, out_ref, *, cut):
    frames, width = x_ref.shape
    lane = lax.broadcasted_iota(jnp.int32, (frames, width), 1) % 128
    low_lane = lane < 64

    def turn(v):
        return jnp.where(low_lane, -pltpu.roll(v, width - 64, 1), pltpu.roll(v, 64, 1))

    def pair(v):
        return jnp.where(low_lane, pltpu.roll(v, width - 64, 1), pltpu.roll(v, 64, 1))

    def low_of(plane):
        mixed = jnp.dot(wl_ref[...], plane, preferred_element_type=jnp.float32)
        return mixed[:frames] + turn(mixed[frames:])

    def remainder_of(plane):
        return (plane.astype(jnp.float32) - low_of(plane)).astype(jnp.bfloat16)

    x = x_ref[...]
    low = low_of(x)
    rem = (x.astype(jnp.float32) - low).astype(jnp.bfloat16)
    planes = jnp.concatenate([remainder_of(xb_ref[...]), rem, remainder_of(xa_ref[...])], axis=0)
    mixed = jnp.dot(wz_ref[...], planes, preferred_element_type=jnp.float32)
    filtered = mixed[:frames] + turn(mixed[frames:])
    square = filtered * filtered
    magnitude = jnp.sqrt(square + pair(square))
    scale = jnp.maximum(magnitude - cut, 0.0) / jnp.maximum(magnitude, cut)
    out_ref[...] = (low + filtered * scale).astype(out_ref.dtype)


def post_of(plane, before, after, low_t, filter_t):
    frames, width = plane.shape
    nb = 2048 if width % 2048 == 0 else width
    lane_spec = pl.BlockSpec((frames, nb), lambda i: (0, i))
    whole2 = lambda shape: pl.BlockSpec(shape, lambda i: (0, 0))
    return pl.pallas_call(
        functools.partial(post_kernel, cut=SOFT_CUT),
        out_shape=jax.ShapeDtypeStruct(plane.shape, jnp.bfloat16),
        grid=(width // nb,),
        in_specs=[lane_spec, lane_spec, lane_spec, whole2(low_t.shape), whole2(filter_t.shape)],
        out_specs=lane_spec,
        compiler_params=pltpu.CompilerParams(dimension_semantics=("arbitrary",)),
        cost_estimate=pl.CostEstimate(
            flops=2 * width * frames * (2 * frames) * 6, transcendentals=width * frames,
            bytes_accessed=plane.size * 8,
        ),
    )(plane, before, after, low_t, filter_t)


def solve_kernel(a_ref, x0_ref, s_ref, out_ref, *, steps):
    size = a_ref.shape[0]
    rows = lax.broadcasted_iota(jnp.int32, (size, size), 0)
    cols = lax.broadcasted_iota(jnp.int32, (size, size), 1)
    twice = jnp.where(rows == cols, 2.0, 0.0).astype(jnp.float32)
    a = a_ref[...]
    high = lax.Precision.HIGHEST

    def step(i, x):
        t = jnp.dot(a, x, precision=high, preferred_element_type=jnp.float32)
        return jnp.dot(x, twice - t, precision=high, preferred_element_type=jnp.float32)

    x = x0_ref[...]
    for i in range(steps):
        x = step(i, x)
    out_ref[...] = jnp.dot(x, s_ref[...], precision=high, preferred_element_type=jnp.float32)


def shrink_of(stacked, threshold_sq, rank_value):
    size = stacked.shape[0]
    unit_matrix = jnp.eye(size, dtype=jnp.float32)
    system = stacked + threshold_sq * unit_matrix
    start = unit_matrix * (2.0 / (threshold_sq * (2.0 + rank_value)))
    whole = pl.BlockSpec(memory_space=pltpu.VMEM)
    return pl.pallas_call(
        functools.partial(solve_kernel, steps=12),
        out_shape=jax.ShapeDtypeStruct((size, size), jnp.float32),
        in_specs=[whole, whole, whole],
        out_specs=whole,
    )(system, start, stacked)


def apply_frames(mix_real, mix_imag, field_values):
    direct = jnp.einsum("fg,zftw->zgtw", mix_real, field_values, preferred_element_type=jnp.float32)
    turned = jnp.einsum(
        "fg,zftw->zgtw", mix_imag, rotate(field_values), preferred_element_type=jnp.float32
    )
    return direct + turned


def soft_shrink(filtered):
    half_width = filtered.shape[-1] // 2
    real_part, imag_part = (filtered[..., :half_width], filtered[..., half_width:])
    magnitude = jnp.sqrt(real_part * real_part + imag_part * imag_part)
    scale_values = jnp.maximum(magnitude - SOFT_CUT, 0.0) / jnp.maximum(magnitude, SOFT_CUT)
    return filtered * jnp.concatenate([scale_values, scale_values], axis=-1)


def tree_sum(value, axis):
    count = lax.axis_size(axis)
    if count & (count - 1):
        return lax.psum(value, axis)
    step = 1
    while step < count:
        pairs = [(i, i ^ step) for i in range(count)]
        value = value + lax.ppermute(value, axis, pairs)
        step *= 2
    return value


def mix_frames(weights, field_values):
    half = weights.shape[1] // 2
    mixed = jnp.einsum("kh,ktw->htw", weights, field_values, preferred_element_type=jnp.float32)
    return mixed[:half] + rotate(mixed[half:])


def local(image, adjoint_data, coil_maps, spoke_counts, tile_map, blocks, z_kernel, rank_cap):
    frame_count = image.shape[1]
    fresh = fresh_image_of(
        image[0], adjoint_data[0], coil_maps[0], spoke_counts[0], tile_map[0], blocks
    )
    count = lax.axis_size("dom")
    forward = [(i, i + 1) for i in range(count - 1)]
    backward = [(target, source) for source, target in forward]
    flat = fresh.reshape(frame_count, -1)
    rows_real = flat
    rows_turned = rotate(fresh).reshape(frame_count, -1)
    gram_real = jnp.einsum("fn,gn->fg", rows_real, rows_real, preferred_element_type=jnp.float32)
    gram_imag = jnp.einsum("fn,gn->fg", rows_turned, rows_real, preferred_element_type=jnp.float32)
    gram_real, gram_imag = tree_sum(jnp.stack([gram_real, gram_imag]), "dom")
    flat, gram_real, gram_imag = lax.optimization_barrier((flat, gram_real, gram_imag))
    fresh_before = lax.ppermute(flat, "dom", forward)
    fresh_after = lax.ppermute(flat, "dom", backward)
    stacked = jnp.block([[gram_real, -gram_imag], [gram_imag, gram_real]])
    rank_value = rank_cap[0].astype(jnp.float32)
    threshold_sq = jnp.trace(gram_real) / rank_value
    shrink = shrink_of(stacked, threshold_sq, rank_value)
    shrink_real = shrink[:frame_count, :frame_count].astype(jnp.bfloat16)
    shrink_imag = shrink[frame_count:, :frame_count].astype(jnp.bfloat16)
    low_t = jnp.concatenate([shrink_real, shrink_imag], axis=1).T
    taps = z_kernel.shape[0]
    filter_weights = jnp.concatenate([z_kernel[:, 0], z_kernel[:, 1]], axis=-1)
    filter_t = filter_weights.reshape(taps * frame_count, 2 * frame_count).T
    out = post_of(flat, fresh_before, fresh_after, low_t, filter_t)
    return out.reshape(image.shape)


def solution(mesh):
    return jax.shard_map(
        local,
        mesh=mesh,
        in_specs=(
            P(("groups", "dom"), None, None, None),
            P(("groups", "dom"), None, None, None),
            P(("groups", "dom"), None, None, None),
            P(("groups", "dom"), None),
            P(("groups", "dom"), None, None, None, None),
            P(),
            P(),
            P(),
        ),
        out_specs=P(("groups", "dom"), None, None, None),
        check_vma=False,
    )
```

```python
import jax
import jax.numpy as jnp
from jax import lax
from jax.sharding import PartitionSpec as P
import functools
from jax.experimental import pallas as pl
from jax.experimental.pallas import tpu as pltpu

SOFT_CUT = 0.25


def padded_2(block, sides, width):
    for axis, dim in sides:
        count = lax.axis_size(axis)
        forward = [(i, i + 1) for i in range(count - 1)]
        backward = [(target, source) for source, target in forward]
        low = lax.ppermute(
            lax.slice_in_dim(block, block.shape[dim] - width, None, axis=dim), axis, forward
        )
        high = lax.ppermute(lax.slice_in_dim(block, 0, width, axis=dim), axis, backward)
        block = jnp.concatenate([low, block, high], axis=dim)
    return block


def rotate(field_values):
    half_width = field_values.shape[-1] // 2
    return jnp.concatenate(
        [-field_values[..., half_width:], field_values[..., :half_width]], axis=-1
    )


def complex_times(left_value, right_value):
    half_width = left_value.shape[-1] // 2
    left_real, left_imag = (left_value[..., :half_width], left_value[..., half_width:])
    right_real, right_imag = (right_value[..., :half_width], right_value[..., half_width:])
    return jnp.concatenate(
        [
            left_real * right_real - left_imag * right_imag,
            left_real * right_imag + left_imag * right_real,
        ],
        axis=-1,
    )


def conj_times(left_value, right_value):
    half_width = left_value.shape[-1] // 2
    left_real, left_imag = (left_value[..., :half_width], left_value[..., half_width:])
    right_real, right_imag = (right_value[..., :half_width], right_value[..., half_width:])
    return jnp.concatenate(
        [
            left_real * right_real + left_imag * right_imag,
            left_real * right_imag - left_imag * right_real,
        ],
        axis=-1,
    )


def grid_gradient(image_plane, plane_maps, counts, plane_map, blocks):
    frame_count, tile_count, lane_width = image_plane.shape
    read_tiles, link_count = (plane_map.shape[2], plane_map.shape[3])
    coil_count = plane_maps.shape[0]
    tile_ids = jnp.arange(tile_count, dtype=jnp.int32)

    def one_slot(spoke_slot, accum):
        tile_index = lax.dynamic_index_in_dim(plane_map, spoke_slot, axis=1, keepdims=False)
        flat_index = tile_index.reshape(frame_count, read_tiles * link_count)
        image_picked = jnp.take_along_axis(image_plane, flat_index[:, :, None], axis=1)
        image_picked = image_picked.reshape(frame_count, read_tiles, link_count, lane_width)
        maps_picked = jnp.take(plane_maps, flat_index.reshape(-1), axis=1)
        maps_picked = maps_picked.reshape(
            coil_count, frame_count, read_tiles, link_count, lane_width
        ).astype(jnp.float32)
        coil_tiles = complex_times(maps_picked, image_picked.astype(jnp.float32)[None]).astype(
            jnp.bfloat16
        )
        samples = jnp.einsum(
            "ctqji,qjio->ctqo", coil_tiles, blocks, preferred_element_type=jnp.float32
        )
        live_mask = (counts > spoke_slot).astype(jnp.float32)[None, :, None, None]
        samples = (samples * live_mask).astype(jnp.bfloat16)
        spread = jnp.einsum("ctqo,qjio->ctqji", samples, blocks, preferred_element_type=jnp.float32)
        back_sum = jnp.sum(conj_times(maps_picked, spread), axis=0)
        back_sum = back_sum.reshape(frame_count, read_tiles * link_count, lane_width)
        onehot = (flat_index[:, :, None] == tile_ids).astype(jnp.float32)
        return accum + jnp.einsum("tkn,tkw->tnw", onehot, back_sum, precision=lax.Precision.HIGHEST)

    most_spokes = jnp.max(counts)
    start_value = jnp.zeros((frame_count, tile_count, lane_width), jnp.float32)
    return lax.fori_loop(0, most_spokes, one_slot, start_value)


def gradient_kernel(idx_ref, cnt_ref, nsl_ref, img_ref, adj_ref, maps_ref,
                    bf_ref, bt_ref, btr_ref, out_ref, x_scr, rx_scr, g_scr, g2_scr,
                    lhs_a, y_a, ry_a, lhs_b, y_b, ry_b, mrr_ref, mii_ref, *, fb, slots, links,
                    coils):
    b = pl.program_id(0)
    reads = links // 2
    img = img_ref[...].astype(jnp.float32)
    x_scr[...] = img
    half = img.shape[-1] // 2
    lane = lax.broadcasted_iota(jnp.int32, img.shape, 2)
    sign = jnp.where(lane < half, -1.0, 1.0).astype(jnp.float32)
    rx_scr[...] = pltpu.roll(img, half, 2) * sign

    @pl.when(b == 0)
    def _():
        maps = maps_ref[...].astype(jnp.float32)
        map_lane = lax.broadcasted_iota(jnp.int32, maps.shape, 2) < half
        swapped = pltpu.roll(maps, half, 2)
        mrr_ref[...] = jnp.where(map_lane, maps, swapped)
        mii_ref[...] = jnp.where(map_lane, swapped, maps)
    g_scr[...] = jnp.zeros_like(g_scr)
    g2_scr[...] = jnp.zeros_like(g2_scr)
    lhs_a[...] = jnp.zeros_like(lhs_a)
    lhs_b[...] = jnp.zeros_like(lhs_b)
    accums = (g_scr, g2_scr)

    def slot_body(s, carry):
        for q in range(reads):
            lhs_scr, y_scr, ry_scr = (lhs_a, y_a, ry_a) if q % 2 == 0 else (lhs_b, y_b, ry_b)

            def gather_t(t, c):
                frame = b * fb + t
                base = (frame * slots + s) * links + q * 2
                row = pl.multiple_of(t * coils, coils)
                for j in range(2):
                    p = idx_ref[base + j]
                    xv = x_scr[t, pl.ds(p, 1), :]
                    rxv = rx_scr[t, pl.ds(p, 1), :]
                    ct = mrr_ref[p] * xv + mii_ref[p] * rxv
                    lhs_scr[pl.ds(row, coils), pl.ds(j * 128, 128)] = ct.astype(jnp.bfloat16)
                return c

            lax.fori_loop(0, fb, gather_t, 0, unroll=True)
            samples = jnp.dot(lhs_scr[...], bf_ref[q], preferred_element_type=jnp.float32)
            samples = samples.astype(jnp.bfloat16)
            y_scr[...] = jnp.dot(samples, bt_ref[q], preferred_element_type=jnp.float32)
            ry_scr[...] = jnp.dot(samples, btr_ref[q], preferred_element_type=jnp.float32)

            def scatter_t(t, c):
                frame = b * fb + t
                live = cnt_ref[frame] > s
                base = (frame * slots + s) * links + q * 2
                row = pl.multiple_of(t * coils, coils)

                keep = live.astype(jnp.float32)
                for j in range(2):
                    p = idx_ref[base + j]
                    yv = y_scr[pl.ds(row, coils), pl.ds(j * 128, 128)]
                    ryv = ry_scr[pl.ds(row, coils), pl.ds(j * 128, 128)]
                    v = mrr_ref[p] * yv - mii_ref[p] * ryv
                    back = jnp.sum(v, axis=0, keepdims=True) * keep
                    acc = accums[j]
                    acc[t, pl.ds(p, 1), :] = acc[t, pl.ds(p, 1), :] + back
                return c

            lax.fori_loop(0, fb, scatter_t, 0, unroll=True)
        return carry

    lax.fori_loop(0, nsl_ref[b], slot_body, 0)
    grad = g_scr[...] + g2_scr[...]
    out_ref[...] = (x_scr[...] - (grad - adj_ref[...].astype(jnp.float32))).astype(out_ref.dtype)


def fresh_image_of(image_plane, adjoint_plane, plane_maps, counts, plane_map, blocks):
    frame_count, tile_count, lane_width = image_plane.shape
    slots, reads, links = plane_map.shape[1], plane_map.shape[2], plane_map.shape[3]
    coils = plane_maps.shape[0]
    fb = 32 if frame_count % 32 == 0 else frame_count
    nblocks = frame_count // fb
    half = lane_width // 2
    maps_t = jnp.swapaxes(plane_maps, 0, 1)
    bf = blocks.reshape(reads, links * lane_width, lane_width)
    bt4 = jnp.transpose(blocks, (0, 3, 1, 2))
    bt = bt4.reshape(reads, lane_width, links * lane_width)
    btr = rotate(bt4).reshape(reads, lane_width, links * lane_width)
    idx = plane_map.reshape(-1).astype(jnp.int32)
    cnt = counts.astype(jnp.int32)
    nsl = jnp.minimum(jnp.max(cnt.reshape(nblocks, fb), axis=1), slots).astype(jnp.int32)
    kernel = functools.partial(
        gradient_kernel, fb=fb, slots=slots, links=reads * links, coils=coils
    )
    plane_spec = pl.BlockSpec((fb, tile_count, lane_width), lambda b, *_: (b, 0, 0))
    whole3 = lambda shape: pl.BlockSpec(shape, lambda b, *_: (0, 0, 0))
    flops = 2 * frame_count * slots * reads * coils * (links * lane_width) * lane_width * 3
    return pl.pallas_call(
        kernel,
        out_shape=jax.ShapeDtypeStruct(image_plane.shape, jnp.bfloat16),
        grid_spec=pltpu.PrefetchScalarGridSpec(
            num_scalar_prefetch=3,
            grid=(nblocks,),
            in_specs=[
                plane_spec,
                plane_spec,
                whole3(maps_t.shape),
                whole3(bf.shape),
                whole3(bt.shape),
                whole3(btr.shape),
            ],
            out_specs=plane_spec,
            scratch_shapes=[
                pltpu.VMEM((fb, tile_count, lane_width), jnp.float32),
                pltpu.VMEM((fb, tile_count, lane_width), jnp.float32),
                pltpu.VMEM((fb, tile_count, lane_width), jnp.float32),
                pltpu.VMEM((fb, tile_count, lane_width), jnp.float32),
                pltpu.VMEM((fb * coils, links * lane_width), jnp.bfloat16),
                pltpu.VMEM((fb * coils, links * lane_width), jnp.float32),
                pltpu.VMEM((fb * coils, links * lane_width), jnp.float32),
                pltpu.VMEM((fb * coils, links * lane_width), jnp.bfloat16),
                pltpu.VMEM((fb * coils, links * lane_width), jnp.float32),
                pltpu.VMEM((fb * coils, links * lane_width), jnp.float32),
                pltpu.VMEM(maps_t.shape, jnp.float32),
                pltpu.VMEM(maps_t.shape, jnp.float32),
            ],
        ),
        compiler_params=pltpu.CompilerParams(dimension_semantics=("arbitrary",)),
        cost_estimate=pl.CostEstimate(
            flops=flops, transcendentals=0, bytes_accessed=image_plane.size * 6 + maps_t.size * 2
        ),
    )(idx, cnt, nsl, image_plane, adjoint_plane, maps_t, bf, bt, btr)


def post_kernel(x_ref, xb_ref, xa_ref, wl_ref, wz_ref, out_ref, *, cut):
    frames, width = x_ref.shape
    lane = lax.broadcasted_iota(jnp.int32, (frames, width), 1) % 128
    low_lane = lane < 64

    def turn(v):
        return jnp.where(low_lane, -pltpu.roll(v, width - 64, 1), pltpu.roll(v, 64, 1))

    def pair(v):
        return jnp.where(low_lane, pltpu.roll(v, width - 64, 1), pltpu.roll(v, 64, 1))

    def low_of(plane):
        mixed = jnp.dot(wl_ref[...], plane, preferred_element_type=jnp.float32)
        return mixed[:frames] + turn(mixed[frames:])

    def remainder_of(plane):
        return (plane.astype(jnp.float32) - low_of(plane)).astype(jnp.bfloat16)

    x = x_ref[...]
    low = low_of(x)
    rem = (x.astype(jnp.float32) - low).astype(jnp.bfloat16)
    planes = jnp.concatenate([remainder_of(xb_ref[...]), rem, remainder_of(xa_ref[...])], axis=0)
    mixed = jnp.dot(wz_ref[...], planes, preferred_element_type=jnp.float32)
    filtered = mixed[:frames] + turn(mixed[frames:])
    square = filtered * filtered
    magnitude = jnp.sqrt(square + pair(square))
    scale = jnp.maximum(magnitude - cut, 0.0) / jnp.maximum(magnitude, cut)
    out_ref[...] = (low + filtered * scale).astype(out_ref.dtype)


def post_of(plane, before, after, low_t, filter_t):
    frames, width = plane.shape
    nb = 2048 if width % 2048 == 0 else width
    lane_spec = pl.BlockSpec((frames, nb), lambda i: (0, i))
    whole2 = lambda shape: pl.BlockSpec(shape, lambda i: (0, 0))
    return pl.pallas_call(
        functools.partial(post_kernel, cut=SOFT_CUT),
        out_shape=jax.ShapeDtypeStruct(plane.shape, jnp.bfloat16),
        grid=(width // nb,),
        in_specs=[lane_spec, lane_spec, lane_spec, whole2(low_t.shape), whole2(filter_t.shape)],
        out_specs=lane_spec,
        compiler_params=pltpu.CompilerParams(dimension_semantics=("arbitrary",)),
        cost_estimate=pl.CostEstimate(
            flops=2 * width * frames * (2 * frames) * 6, transcendentals=width * frames,
            bytes_accessed=plane.size * 8,
        ),
    )(plane, before, after, low_t, filter_t)


def solve_kernel(a_ref, x0_ref, s_ref, out_ref, *, steps):
    size = a_ref.shape[0]
    rows = lax.broadcasted_iota(jnp.int32, (size, size), 0)
    cols = lax.broadcasted_iota(jnp.int32, (size, size), 1)
    twice = jnp.where(rows == cols, 2.0, 0.0).astype(jnp.float32)
    a = a_ref[...]
    high = lax.Precision.HIGHEST

    def step(i, x):
        t = jnp.dot(a, x, precision=high, preferred_element_type=jnp.float32)
        return jnp.dot(x, twice - t, precision=high, preferred_element_type=jnp.float32)

    x = x0_ref[...]
    for i in range(steps):
        x = step(i, x)
    out_ref[...] = jnp.dot(x, s_ref[...], precision=high, preferred_element_type=jnp.float32)


def shrink_of(stacked, threshold_sq, rank_value):
    size = stacked.shape[0]
    unit_matrix = jnp.eye(size, dtype=jnp.float32)
    system = stacked + threshold_sq * unit_matrix
    start = unit_matrix * (2.0 / (threshold_sq * (2.0 + rank_value)))
    whole = pl.BlockSpec(memory_space=pltpu.VMEM)
    return pl.pallas_call(
        functools.partial(solve_kernel, steps=12),
        out_shape=jax.ShapeDtypeStruct((size, size), jnp.float32),
        in_specs=[whole, whole, whole],
        out_specs=whole,
    )(system, start, stacked)


def apply_frames(mix_real, mix_imag, field_values):
    direct = jnp.einsum("fg,zftw->zgtw", mix_real, field_values, preferred_element_type=jnp.float32)
    turned = jnp.einsum(
        "fg,zftw->zgtw", mix_imag, rotate(field_values), preferred_element_type=jnp.float32
    )
    return direct + turned


def soft_shrink(filtered):
    half_width = filtered.shape[-1] // 2
    real_part, imag_part = (filtered[..., :half_width], filtered[..., half_width:])
    magnitude = jnp.sqrt(real_part * real_part + imag_part * imag_part)
    scale_values = jnp.maximum(magnitude - SOFT_CUT, 0.0) / jnp.maximum(magnitude, SOFT_CUT)
    return filtered * jnp.concatenate([scale_values, scale_values], axis=-1)


def tree_sum(value, axis):
    count = lax.axis_size(axis)
    if count & (count - 1):
        return lax.psum(value, axis)
    step = 1
    while step < count:
        pairs = [(i, i ^ step) for i in range(count)]
        value = value + lax.ppermute(value, axis, pairs)
        step *= 2
    return value


def mix_frames(weights, field_values):
    half = weights.shape[1] // 2
    mixed = jnp.einsum("kh,ktw->htw", weights, field_values, preferred_element_type=jnp.float32)
    return mixed[:half] + rotate(mixed[half:])


def local(image, adjoint_data, coil_maps, spoke_counts, tile_map, blocks, z_kernel, rank_cap):
    frame_count = image.shape[1]
    fresh = fresh_image_of(
        image[0], adjoint_data[0], coil_maps[0], spoke_counts[0], tile_map[0], blocks
    )
    count = lax.axis_size("dom")
    forward = [(i, i + 1) for i in range(count - 1)]
    backward = [(target, source) for source, target in forward]
    flat = fresh.reshape(frame_count, -1)
    rows_real = flat
    half = fresh.shape[-1] // 2
    gram_real = jnp.einsum("fn,gn->fg", rows_real, rows_real, preferred_element_type=jnp.float32)
    cross = jnp.einsum(
        "ftw,gtw->fg", fresh[..., :half], fresh[..., half:], preferred_element_type=jnp.float32
    )
    gram_imag = cross - cross.T
    gram_real, gram_imag = tree_sum(jnp.stack([gram_real, gram_imag]), "dom")
    flat, gram_real, gram_imag = lax.optimization_barrier((flat, gram_real, gram_imag))
    fresh_before = lax.ppermute(flat, "dom", forward)
    fresh_after = lax.ppermute(flat, "dom", backward)
    stacked = jnp.block([[gram_real, -gram_imag], [gram_imag, gram_real]])
    rank_value = rank_cap[0].astype(jnp.float32)
    threshold_sq = jnp.trace(gram_real) / rank_value
    shrink = shrink_of(stacked, threshold_sq, rank_value)
    shrink_real = shrink[:frame_count, :frame_count].astype(jnp.bfloat16)
    shrink_imag = shrink[frame_count:, :frame_count].astype(jnp.bfloat16)
    low_t = jnp.concatenate([shrink_real, shrink_imag], axis=1).T
    taps = z_kernel.shape[0]
    filter_weights = jnp.concatenate([z_kernel[:, 0], z_kernel[:, 1]], axis=-1)
    filter_t = filter_weights.reshape(taps * frame_count, 2 * frame_count).T
    out = post_of(flat, fresh_before, fresh_after, low_t, filter_t)
    return out.reshape(image.shape)


def solution(mesh):
    return jax.shard_map(
        local,
        mesh=mesh,
        in_specs=(
            P(("groups", "dom"), None, None, None),
            P(("groups", "dom"), None, None, None),
            P(("groups", "dom"), None, None, None),
            P(("groups", "dom"), None),
            P(("groups", "dom"), None, None, None, None),
            P(),
            P(),
            P(),
        ),
        out_specs=P(("groups", "dom"), None, None, None),
        check_vma=False,
    )
```

```python
import jax
import jax.numpy as jnp
from jax import lax
from jax.sharding import PartitionSpec as P
import functools
from jax.experimental import pallas as pl
from jax.experimental.pallas import tpu as pltpu

SOFT_CUT = 0.25


def padded_2(block, sides, width):
    for axis, dim in sides:
        count = lax.axis_size(axis)
        forward = [(i, i + 1) for i in range(count - 1)]
        backward = [(target, source) for source, target in forward]
        low = lax.ppermute(
            lax.slice_in_dim(block, block.shape[dim] - width, None, axis=dim), axis, forward
        )
        high = lax.ppermute(lax.slice_in_dim(block, 0, width, axis=dim), axis, backward)
        block = jnp.concatenate([low, block, high], axis=dim)
    return block


def rotate(field_values):
    half_width = field_values.shape[-1] // 2
    return jnp.concatenate(
        [-field_values[..., half_width:], field_values[..., :half_width]], axis=-1
    )


def complex_times(left_value, right_value):
    half_width = left_value.shape[-1] // 2
    left_real, left_imag = (left_value[..., :half_width], left_value[..., half_width:])
    right_real, right_imag = (right_value[..., :half_width], right_value[..., half_width:])
    return jnp.concatenate(
        [
            left_real * right_real - left_imag * right_imag,
            left_real * right_imag + left_imag * right_real,
        ],
        axis=-1,
    )


def conj_times(left_value, right_value):
    half_width = left_value.shape[-1] // 2
    left_real, left_imag = (left_value[..., :half_width], left_value[..., half_width:])
    right_real, right_imag = (right_value[..., :half_width], right_value[..., half_width:])
    return jnp.concatenate(
        [
            left_real * right_real + left_imag * right_imag,
            left_real * right_imag - left_imag * right_real,
        ],
        axis=-1,
    )


def grid_gradient(image_plane, plane_maps, counts, plane_map, blocks):
    frame_count, tile_count, lane_width = image_plane.shape
    read_tiles, link_count = (plane_map.shape[2], plane_map.shape[3])
    coil_count = plane_maps.shape[0]
    tile_ids = jnp.arange(tile_count, dtype=jnp.int32)

    def one_slot(spoke_slot, accum):
        tile_index = lax.dynamic_index_in_dim(plane_map, spoke_slot, axis=1, keepdims=False)
        flat_index = tile_index.reshape(frame_count, read_tiles * link_count)
        image_picked = jnp.take_along_axis(image_plane, flat_index[:, :, None], axis=1)
        image_picked = image_picked.reshape(frame_count, read_tiles, link_count, lane_width)
        maps_picked = jnp.take(plane_maps, flat_index.reshape(-1), axis=1)
        maps_picked = maps_picked.reshape(
            coil_count, frame_count, read_tiles, link_count, lane_width
        ).astype(jnp.float32)
        coil_tiles = complex_times(maps_picked, image_picked.astype(jnp.float32)[None]).astype(
            jnp.bfloat16
        )
        samples = jnp.einsum(
            "ctqji,qjio->ctqo", coil_tiles, blocks, preferred_element_type=jnp.float32
        )
        live_mask = (counts > spoke_slot).astype(jnp.float32)[None, :, None, None]
        samples = (samples * live_mask).astype(jnp.bfloat16)
        spread = jnp.einsum("ctqo,qjio->ctqji", samples, blocks, preferred_element_type=jnp.float32)
        back_sum = jnp.sum(conj_times(maps_picked, spread), axis=0)
        back_sum = back_sum.reshape(frame_count, read_tiles * link_count, lane_width)
        onehot = (flat_index[:, :, None] == tile_ids).astype(jnp.float32)
        return accum + jnp.einsum("tkn,tkw->tnw", onehot, back_sum, precision=lax.Precision.HIGHEST)

    most_spokes = jnp.max(counts)
    start_value = jnp.zeros((frame_count, tile_count, lane_width), jnp.float32)
    return lax.fori_loop(0, most_spokes, one_slot, start_value)


def gradient_kernel(idx_ref, cnt_ref, nsl_ref, img_ref, adj_ref, maps_ref,
                    bf_ref, bt_ref, btr_ref, out_ref, x_scr, rx_scr, g_scr, g2_scr,
                    lhs_a, y_a, ry_a, lhs_b, y_b, ry_b, mrr_ref, mii_ref, *, fb, slots, links,
                    coils):
    b = pl.program_id(0)
    reads = links // 2
    img = img_ref[...].astype(jnp.float32)
    x_scr[...] = img
    half = img.shape[-1] // 2
    lane = lax.broadcasted_iota(jnp.int32, img.shape, 2)
    sign = jnp.where(lane < half, -1.0, 1.0).astype(jnp.float32)
    rx_scr[...] = pltpu.roll(img, half, 2) * sign

    @pl.when(b == 0)
    def _():
        maps = maps_ref[...].astype(jnp.float32)
        map_lane = lax.broadcasted_iota(jnp.int32, maps.shape, 2) < half
        swapped = pltpu.roll(maps, half, 2)
        mrr_ref[...] = jnp.where(map_lane, maps, swapped)
        mii_ref[...] = jnp.where(map_lane, swapped, maps)
    g_scr[...] = jnp.zeros_like(g_scr)
    g2_scr[...] = jnp.zeros_like(g2_scr)
    lhs_a[...] = jnp.zeros_like(lhs_a)
    lhs_b[...] = jnp.zeros_like(lhs_b)
    accums = (g_scr, g2_scr)

    def slot_body(s, carry):
        for q in range(reads):
            lhs_scr, y_scr, ry_scr = (lhs_a, y_a, ry_a) if q % 2 == 0 else (lhs_b, y_b, ry_b)

            def gather_t(t, c):
                frame = b * fb + t
                base = (frame * slots + s) * links + q * 2
                row = pl.multiple_of(t * coils, coils)
                for j in range(2):
                    p = idx_ref[base + j]
                    xv = x_scr[t, pl.ds(p, 1), :]
                    rxv = rx_scr[t, pl.ds(p, 1), :]
                    ct = mrr_ref[p] * xv + mii_ref[p] * rxv
                    lhs_scr[pl.ds(row, coils), pl.ds(j * 128, 128)] = ct.astype(jnp.bfloat16)
                return c

            lax.fori_loop(0, fb, gather_t, 0, unroll=True)
            samples = jnp.dot(lhs_scr[...], bf_ref[q], preferred_element_type=jnp.float32)
            samples = samples.astype(jnp.bfloat16)
            y_scr[...] = jnp.dot(samples, bt_ref[q], preferred_element_type=jnp.float32)
            ry_scr[...] = jnp.dot(samples, btr_ref[q], preferred_element_type=jnp.float32)

            def scatter_t(t, c):
                frame = b * fb + t
                live = cnt_ref[frame] > s
                base = (frame * slots + s) * links + q * 2
                row = pl.multiple_of(t * coils, coils)

                keep = live.astype(jnp.float32)
                for j in range(2):
                    p = idx_ref[base + j]
                    yv = y_scr[pl.ds(row, coils), pl.ds(j * 128, 128)]
                    ryv = ry_scr[pl.ds(row, coils), pl.ds(j * 128, 128)]
                    v = mrr_ref[p] * yv - mii_ref[p] * ryv
                    back = jnp.sum(v, axis=0, keepdims=True) * keep
                    acc = accums[j]
                    acc[t, pl.ds(p, 1), :] = acc[t, pl.ds(p, 1), :] + back
                return c

            lax.fori_loop(0, fb, scatter_t, 0, unroll=True)
        return carry

    lax.fori_loop(0, nsl_ref[b], slot_body, 0)
    grad = g_scr[...] + g2_scr[...]
    out_ref[...] = (x_scr[...] - (grad - adj_ref[...].astype(jnp.float32))).astype(out_ref.dtype)


def fresh_image_of(image_plane, adjoint_plane, plane_maps, counts, plane_map, blocks):
    frame_count, tile_count, lane_width = image_plane.shape
    slots, reads, links = plane_map.shape[1], plane_map.shape[2], plane_map.shape[3]
    coils = plane_maps.shape[0]
    fb = 32 if frame_count % 32 == 0 else frame_count
    nblocks = frame_count // fb
    half = lane_width // 2
    maps_t = jnp.swapaxes(plane_maps, 0, 1)
    bf = blocks.reshape(reads, links * lane_width, lane_width)
    bt4 = jnp.transpose(blocks, (0, 3, 1, 2))
    bt = bt4.reshape(reads, lane_width, links * lane_width)
    btr = rotate(bt4).reshape(reads, lane_width, links * lane_width)
    idx = plane_map.reshape(-1).astype(jnp.int32)
    cnt = counts.astype(jnp.int32)
    nsl = jnp.minimum(jnp.max(cnt.reshape(nblocks, fb), axis=1), slots).astype(jnp.int32)
    kernel = functools.partial(
        gradient_kernel, fb=fb, slots=slots, links=reads * links, coils=coils
    )
    plane_spec = pl.BlockSpec((fb, tile_count, lane_width), lambda b, *_: (b, 0, 0))
    whole3 = lambda shape: pl.BlockSpec(shape, lambda b, *_: (0, 0, 0))
    flops = 2 * frame_count * slots * reads * coils * (links * lane_width) * lane_width * 3
    return pl.pallas_call(
        kernel,
        out_shape=jax.ShapeDtypeStruct(image_plane.shape, jnp.bfloat16),
        grid_spec=pltpu.PrefetchScalarGridSpec(
            num_scalar_prefetch=3,
            grid=(nblocks,),
            in_specs=[
                plane_spec,
                plane_spec,
                whole3(maps_t.shape),
                whole3(bf.shape),
                whole3(bt.shape),
                whole3(btr.shape),
            ],
            out_specs=plane_spec,
            scratch_shapes=[
                pltpu.VMEM((fb, tile_count, lane_width), jnp.float32),
                pltpu.VMEM((fb, tile_count, lane_width), jnp.float32),
                pltpu.VMEM((fb, tile_count, lane_width), jnp.float32),
                pltpu.VMEM((fb, tile_count, lane_width), jnp.float32),
                pltpu.VMEM((fb * coils, links * lane_width), jnp.bfloat16),
                pltpu.VMEM((fb * coils, links * lane_width), jnp.float32),
                pltpu.VMEM((fb * coils, links * lane_width), jnp.float32),
                pltpu.VMEM((fb * coils, links * lane_width), jnp.bfloat16),
                pltpu.VMEM((fb * coils, links * lane_width), jnp.float32),
                pltpu.VMEM((fb * coils, links * lane_width), jnp.float32),
                pltpu.VMEM(maps_t.shape, jnp.float32),
                pltpu.VMEM(maps_t.shape, jnp.float32),
            ],
        ),
        compiler_params=pltpu.CompilerParams(dimension_semantics=("arbitrary",)),
        cost_estimate=pl.CostEstimate(
            flops=flops, transcendentals=0, bytes_accessed=image_plane.size * 6 + maps_t.size * 2
        ),
    )(idx, cnt, nsl, image_plane, adjoint_plane, maps_t, bf, bt, btr)


def post_kernel(x_ref, xb_ref, xa_ref, wl_ref, wz_ref, out_ref, *, cut):
    frames, width = x_ref.shape
    lane = lax.broadcasted_iota(jnp.int32, (frames, width), 1) % 128
    low_lane = lane < 64

    def turn(v):
        return jnp.where(low_lane, -pltpu.roll(v, width - 64, 1), pltpu.roll(v, 64, 1))

    def pair(v):
        return jnp.where(low_lane, pltpu.roll(v, width - 64, 1), pltpu.roll(v, 64, 1))

    def low_of(plane):
        mixed = jnp.dot(wl_ref[...], plane, preferred_element_type=jnp.float32)
        return mixed[:frames] + turn(mixed[frames:])

    def remainder_of(plane):
        return (plane.astype(jnp.float32) - low_of(plane)).astype(jnp.bfloat16)

    x = x_ref[...]
    low = low_of(x)
    rem = (x.astype(jnp.float32) - low).astype(jnp.bfloat16)
    planes = jnp.concatenate([remainder_of(xb_ref[...]), rem, remainder_of(xa_ref[...])], axis=0)
    mixed = jnp.dot(wz_ref[...], planes, preferred_element_type=jnp.float32)
    filtered = mixed[:frames] + turn(mixed[frames:])
    square = filtered * filtered
    magnitude = jnp.sqrt(square + pair(square))
    scale = jnp.maximum(magnitude - cut, 0.0) / jnp.maximum(magnitude, cut)
    out_ref[...] = (low + filtered * scale).astype(out_ref.dtype)


def post_of(plane, before, after, low_t, filter_t):
    frames, width = plane.shape
    nb = 4096 if width % 4096 == 0 else width
    lane_spec = pl.BlockSpec((frames, nb), lambda i: (0, i))
    whole2 = lambda shape: pl.BlockSpec(shape, lambda i: (0, 0))
    return pl.pallas_call(
        functools.partial(post_kernel, cut=SOFT_CUT),
        out_shape=jax.ShapeDtypeStruct(plane.shape, jnp.bfloat16),
        grid=(width // nb,),
        in_specs=[lane_spec, lane_spec, lane_spec, whole2(low_t.shape), whole2(filter_t.shape)],
        out_specs=lane_spec,
        compiler_params=pltpu.CompilerParams(dimension_semantics=("arbitrary",)),
        cost_estimate=pl.CostEstimate(
            flops=2 * width * frames * (2 * frames) * 6, transcendentals=width * frames,
            bytes_accessed=plane.size * 8,
        ),
    )(plane, before, after, low_t, filter_t)


def solve_kernel(a_ref, x0_ref, s_ref, out_ref, *, steps):
    size = a_ref.shape[0]
    rows = lax.broadcasted_iota(jnp.int32, (size, size), 0)
    cols = lax.broadcasted_iota(jnp.int32, (size, size), 1)
    twice = jnp.where(rows == cols, 2.0, 0.0).astype(jnp.float32)
    a = a_ref[...]
    high = lax.Precision.HIGHEST

    def step(i, x):
        t = jnp.dot(a, x, precision=high, preferred_element_type=jnp.float32)
        return jnp.dot(x, twice - t, precision=high, preferred_element_type=jnp.float32)

    x = x0_ref[...]
    for i in range(steps):
        x = step(i, x)
    out_ref[...] = jnp.dot(x, s_ref[...], precision=high, preferred_element_type=jnp.float32)


def shrink_of(stacked, threshold_sq, rank_value):
    size = stacked.shape[0]
    unit_matrix = jnp.eye(size, dtype=jnp.float32)
    system = stacked + threshold_sq * unit_matrix
    start = unit_matrix * (2.0 / (threshold_sq * (2.0 + rank_value)))
    whole = pl.BlockSpec(memory_space=pltpu.VMEM)
    return pl.pallas_call(
        functools.partial(solve_kernel, steps=10),
        out_shape=jax.ShapeDtypeStruct((size, size), jnp.float32),
        in_specs=[whole, whole, whole],
        out_specs=whole,
    )(system, start, stacked)


def apply_frames(mix_real, mix_imag, field_values):
    direct = jnp.einsum("fg,zftw->zgtw", mix_real, field_values, preferred_element_type=jnp.float32)
    turned = jnp.einsum(
        "fg,zftw->zgtw", mix_imag, rotate(field_values), preferred_element_type=jnp.float32
    )
    return direct + turned


def soft_shrink(filtered):
    half_width = filtered.shape[-1] // 2
    real_part, imag_part = (filtered[..., :half_width], filtered[..., half_width:])
    magnitude = jnp.sqrt(real_part * real_part + imag_part * imag_part)
    scale_values = jnp.maximum(magnitude - SOFT_CUT, 0.0) / jnp.maximum(magnitude, SOFT_CUT)
    return filtered * jnp.concatenate([scale_values, scale_values], axis=-1)


def tree_sum(value, axis):
    count = lax.axis_size(axis)
    if count & (count - 1):
        return lax.psum(value, axis)
    step = 1
    while step < count:
        pairs = [(i, i ^ step) for i in range(count)]
        value = value + lax.ppermute(value, axis, pairs)
        step *= 2
    return value


def mix_frames(weights, field_values):
    half = weights.shape[1] // 2
    mixed = jnp.einsum("kh,ktw->htw", weights, field_values, preferred_element_type=jnp.float32)
    return mixed[:half] + rotate(mixed[half:])


def local(image, adjoint_data, coil_maps, spoke_counts, tile_map, blocks, z_kernel, rank_cap):
    frame_count = image.shape[1]
    fresh = fresh_image_of(
        image[0], adjoint_data[0], coil_maps[0], spoke_counts[0], tile_map[0], blocks
    )
    count = lax.axis_size("dom")
    forward = [(i, i + 1) for i in range(count - 1)]
    backward = [(target, source) for source, target in forward]
    flat = fresh.reshape(frame_count, -1)
    rows_real = flat
    rows_turned = rotate(fresh).reshape(frame_count, -1)
    gram_real = jnp.einsum("fn,gn->fg", rows_real, rows_real, preferred_element_type=jnp.float32)
    gram_imag = jnp.einsum("fn,gn->fg", rows_turned, rows_real, preferred_element_type=jnp.float32)
    gram_real, gram_imag = tree_sum(jnp.stack([gram_real, gram_imag]), "dom")
    flat, gram_real, gram_imag = lax.optimization_barrier((flat, gram_real, gram_imag))
    fresh_before = lax.ppermute(flat, "dom", forward)
    fresh_after = lax.ppermute(flat, "dom", backward)
    stacked = jnp.block([[gram_real, -gram_imag], [gram_imag, gram_real]])
    rank_value = rank_cap[0].astype(jnp.float32)
    threshold_sq = jnp.trace(gram_real) / rank_value
    shrink = shrink_of(stacked, threshold_sq, rank_value)
    shrink_real = shrink[:frame_count, :frame_count].astype(jnp.bfloat16)
    shrink_imag = shrink[frame_count:, :frame_count].astype(jnp.bfloat16)
    low_t = jnp.concatenate([shrink_real, shrink_imag], axis=1).T
    taps = z_kernel.shape[0]
    filter_weights = jnp.concatenate([z_kernel[:, 0], z_kernel[:, 1]], axis=-1)
    filter_t = filter_weights.reshape(taps * frame_count, 2 * frame_count).T
    out = post_of(flat, fresh_before, fresh_after, low_t, filter_t)
    return out.reshape(image.shape)


def solution(mesh):
    return jax.shard_map(
        local,
        mesh=mesh,
        in_specs=(
            P(("groups", "dom"), None, None, None),
            P(("groups", "dom"), None, None, None),
            P(("groups", "dom"), None, None, None),
            P(("groups", "dom"), None),
            P(("groups", "dom"), None, None, None, None),
            P(),
            P(),
            P(),
        ),
        out_specs=P(("groups", "dom"), None, None, None),
        check_vma=False,
    )
```

```python
import jax
import jax.numpy as jnp
from jax import lax
from jax.sharding import PartitionSpec as P
import functools
from jax.experimental import pallas as pl
from jax.experimental.pallas import tpu as pltpu

SOFT_CUT = 0.25


def padded_2(block, sides, width):
    for axis, dim in sides:
        count = lax.axis_size(axis)
        forward = [(i, i + 1) for i in range(count - 1)]
        backward = [(target, source) for source, target in forward]
        low = lax.ppermute(
            lax.slice_in_dim(block, block.shape[dim] - width, None, axis=dim), axis, forward
        )
        high = lax.ppermute(lax.slice_in_dim(block, 0, width, axis=dim), axis, backward)
        block = jnp.concatenate([low, block, high], axis=dim)
    return block


def rotate(field_values):
    half_width = field_values.shape[-1] // 2
    return jnp.concatenate(
        [-field_values[..., half_width:], field_values[..., :half_width]], axis=-1
    )


def complex_times(left_value, right_value):
    half_width = left_value.shape[-1] // 2
    left_real, left_imag = (left_value[..., :half_width], left_value[..., half_width:])
    right_real, right_imag = (right_value[..., :half_width], right_value[..., half_width:])
    return jnp.concatenate(
        [
            left_real * right_real - left_imag * right_imag,
            left_real * right_imag + left_imag * right_real,
        ],
        axis=-1,
    )


def conj_times(left_value, right_value):
    half_width = left_value.shape[-1] // 2
    left_real, left_imag = (left_value[..., :half_width], left_value[..., half_width:])
    right_real, right_imag = (right_value[..., :half_width], right_value[..., half_width:])
    return jnp.concatenate(
        [
            left_real * right_real + left_imag * right_imag,
            left_real * right_imag - left_imag * right_real,
        ],
        axis=-1,
    )


def grid_gradient(image_plane, plane_maps, counts, plane_map, blocks):
    frame_count, tile_count, lane_width = image_plane.shape
    read_tiles, link_count = (plane_map.shape[2], plane_map.shape[3])
    coil_count = plane_maps.shape[0]
    tile_ids = jnp.arange(tile_count, dtype=jnp.int32)

    def one_slot(spoke_slot, accum):
        tile_index = lax.dynamic_index_in_dim(plane_map, spoke_slot, axis=1, keepdims=False)
        flat_index = tile_index.reshape(frame_count, read_tiles * link_count)
        image_picked = jnp.take_along_axis(image_plane, flat_index[:, :, None], axis=1)
        image_picked = image_picked.reshape(frame_count, read_tiles, link_count, lane_width)
        maps_picked = jnp.take(plane_maps, flat_index.reshape(-1), axis=1)
        maps_picked = maps_picked.reshape(
            coil_count, frame_count, read_tiles, link_count, lane_width
        ).astype(jnp.float32)
        coil_tiles = complex_times(maps_picked, image_picked.astype(jnp.float32)[None]).astype(
            jnp.bfloat16
        )
        samples = jnp.einsum(
            "ctqji,qjio->ctqo", coil_tiles, blocks, preferred_element_type=jnp.float32
        )
        live_mask = (counts > spoke_slot).astype(jnp.float32)[None, :, None, None]
        samples = (samples * live_mask).astype(jnp.bfloat16)
        spread = jnp.einsum("ctqo,qjio->ctqji", samples, blocks, preferred_element_type=jnp.float32)
        back_sum = jnp.sum(conj_times(maps_picked, spread), axis=0)
        back_sum = back_sum.reshape(frame_count, read_tiles * link_count, lane_width)
        onehot = (flat_index[:, :, None] == tile_ids).astype(jnp.float32)
        return accum + jnp.einsum("tkn,tkw->tnw", onehot, back_sum, precision=lax.Precision.HIGHEST)

    most_spokes = jnp.max(counts)
    start_value = jnp.zeros((frame_count, tile_count, lane_width), jnp.float32)
    return lax.fori_loop(0, most_spokes, one_slot, start_value)


def gradient_kernel(idx_ref, cnt_ref, nsl_ref, img_ref, adj_ref, maps_ref,
                    bf_ref, bt_ref, btr_ref, out_ref, x_scr, rx_scr, g_scr, g2_scr,
                    lhs_a, y_a, ry_a, lhs_b, y_b, ry_b, mrr_ref, mii_ref, *, fb, slots, links,
                    coils):
    b = pl.program_id(0)
    reads = links // 2
    img = img_ref[...].astype(jnp.float32)
    x_scr[...] = img
    half = img.shape[-1] // 2
    lane = lax.broadcasted_iota(jnp.int32, img.shape, 2)
    sign = jnp.where(lane < half, -1.0, 1.0).astype(jnp.float32)
    rx_scr[...] = pltpu.roll(img, half, 2) * sign

    @pl.when(b == 0)
    def _():
        maps = maps_ref[...].astype(jnp.float32)
        map_lane = lax.broadcasted_iota(jnp.int32, maps.shape, 2) < half
        swapped = pltpu.roll(maps, half, 2)
        mrr_ref[...] = jnp.where(map_lane, maps, swapped)
        mii_ref[...] = jnp.where(map_lane, swapped, maps)
    g_scr[...] = jnp.zeros_like(g_scr)
    g2_scr[...] = jnp.zeros_like(g2_scr)
    lhs_a[...] = jnp.zeros_like(lhs_a)
    lhs_b[...] = jnp.zeros_like(lhs_b)
    accums = (g_scr, g2_scr)

    def slot_body(s, carry):
        for q in range(reads):
            lhs_scr, y_scr, ry_scr = (lhs_a, y_a, ry_a) if q % 2 == 0 else (lhs_b, y_b, ry_b)

            def gather_t(t, c):
                frame = b * fb + t
                base = (frame * slots + s) * links + q * 2
                row = pl.multiple_of(t * coils, coils)
                for j in range(2):
                    p = idx_ref[base + j]
                    xv = x_scr[t, pl.ds(p, 1), :]
                    rxv = rx_scr[t, pl.ds(p, 1), :]
                    ct = mrr_ref[p] * xv + mii_ref[p] * rxv
                    lhs_scr[pl.ds(row, coils), pl.ds(j * 128, 128)] = ct.astype(jnp.bfloat16)
                return c

            lax.fori_loop(0, fb, gather_t, 0, unroll=True)
            samples = jnp.dot(lhs_scr[...], bf_ref[q], preferred_element_type=jnp.float32)
            samples = samples.astype(jnp.bfloat16)
            y_scr[...] = jnp.dot(samples, bt_ref[q], preferred_element_type=jnp.float32)
            ry_scr[...] = jnp.dot(samples, btr_ref[q], preferred_element_type=jnp.float32)

            def scatter_t(t, c):
                frame = b * fb + t
                live = cnt_ref[frame] > s
                base = (frame * slots + s) * links + q * 2
                row = pl.multiple_of(t * coils, coils)

                keep = live.astype(jnp.float32)
                for j in range(2):
                    p = idx_ref[base + j]
                    yv = y_scr[pl.ds(row, coils), pl.ds(j * 128, 128)]
                    ryv = ry_scr[pl.ds(row, coils), pl.ds(j * 128, 128)]
                    v = mrr_ref[p] * yv - mii_ref[p] * ryv
                    back = jnp.sum(v, axis=0, keepdims=True) * keep
                    acc = accums[j]
                    acc[t, pl.ds(p, 1), :] = acc[t, pl.ds(p, 1), :] + back
                return c

            lax.fori_loop(0, fb, scatter_t, 0, unroll=True)
        return carry

    lax.fori_loop(0, nsl_ref[b], slot_body, 0)
    grad = g_scr[...] + g2_scr[...]
    out_ref[...] = (x_scr[...] - (grad - adj_ref[...].astype(jnp.float32))).astype(out_ref.dtype)


def fresh_image_of(image_plane, adjoint_plane, plane_maps, counts, plane_map, blocks):
    frame_count, tile_count, lane_width = image_plane.shape
    slots, reads, links = plane_map.shape[1], plane_map.shape[2], plane_map.shape[3]
    coils = plane_maps.shape[0]
    fb = 32 if frame_count % 32 == 0 else frame_count
    nblocks = frame_count // fb
    half = lane_width // 2
    maps_t = jnp.swapaxes(plane_maps, 0, 1)
    bf = blocks.reshape(reads, links * lane_width, lane_width)
    bt4 = jnp.transpose(blocks, (0, 3, 1, 2))
    bt = bt4.reshape(reads, lane_width, links * lane_width)
    btr = rotate(bt4).reshape(reads, lane_width, links * lane_width)
    idx = plane_map.reshape(-1).astype(jnp.int32)
    cnt = counts.astype(jnp.int32)
    nsl = jnp.minimum(jnp.max(cnt.reshape(nblocks, fb), axis=1), slots).astype(jnp.int32)
    kernel = functools.partial(
        gradient_kernel, fb=fb, slots=slots, links=reads * links, coils=coils
    )
    plane_spec = pl.BlockSpec((fb, tile_count, lane_width), lambda b, *_: (b, 0, 0))
    whole3 = lambda shape: pl.BlockSpec(shape, lambda b, *_: (0, 0, 0))
    flops = 2 * frame_count * slots * reads * coils * (links * lane_width) * lane_width * 3
    return pl.pallas_call(
        kernel,
        out_shape=jax.ShapeDtypeStruct(image_plane.shape, jnp.bfloat16),
        grid_spec=pltpu.PrefetchScalarGridSpec(
            num_scalar_prefetch=3,
            grid=(nblocks,),
            in_specs=[
                plane_spec,
                plane_spec,
                whole3(maps_t.shape),
                whole3(bf.shape),
                whole3(bt.shape),
                whole3(btr.shape),
            ],
            out_specs=plane_spec,
            scratch_shapes=[
                pltpu.VMEM((fb, tile_count, lane_width), jnp.float32),
                pltpu.VMEM((fb, tile_count, lane_width), jnp.float32),
                pltpu.VMEM((fb, tile_count, lane_width), jnp.float32),
                pltpu.VMEM((fb, tile_count, lane_width), jnp.float32),
                pltpu.VMEM((fb * coils, links * lane_width), jnp.bfloat16),
                pltpu.VMEM((fb * coils, links * lane_width), jnp.float32),
                pltpu.VMEM((fb * coils, links * lane_width), jnp.float32),
                pltpu.VMEM((fb * coils, links * lane_width), jnp.bfloat16),
                pltpu.VMEM((fb * coils, links * lane_width), jnp.float32),
                pltpu.VMEM((fb * coils, links * lane_width), jnp.float32),
                pltpu.VMEM(maps_t.shape, jnp.float32),
                pltpu.VMEM(maps_t.shape, jnp.float32),
            ],
        ),
        compiler_params=pltpu.CompilerParams(dimension_semantics=("arbitrary",)),
        cost_estimate=pl.CostEstimate(
            flops=flops, transcendentals=0, bytes_accessed=image_plane.size * 6 + maps_t.size * 2
        ),
    )(idx, cnt, nsl, image_plane, adjoint_plane, maps_t, bf, bt, btr)


def lane_tools(frames, width):
    lane = lax.broadcasted_iota(jnp.int32, (frames, width), 1) % 128
    low_lane = lane < 64

    def turn(v):
        return jnp.where(low_lane, -pltpu.roll(v, width - 64, 1), pltpu.roll(v, 64, 1))

    def pair(v):
        return jnp.where(low_lane, pltpu.roll(v, width - 64, 1), pltpu.roll(v, 64, 1))

    return turn, pair


def low_of(wl_ref, plane, turn):
    frames = plane.shape[0]
    mixed = jnp.dot(wl_ref[...], plane, preferred_element_type=jnp.float32)
    return mixed[:frames] + turn(mixed[frames:])


def own_kernel(x_ref, wl_ref, low_ref, rem_ref):
    frames, width = x_ref.shape
    turn, _ = lane_tools(frames, width)
    x = x_ref[...]
    low = low_of(wl_ref, x, turn)
    low_ref[...] = low
    rem_ref[...] = (x.astype(jnp.float32) - low).astype(jnp.bfloat16)


def post_kernel(low_ref, rem_ref, xb_ref, xa_ref, wl_ref, wz_ref, out_ref, *, cut):
    frames, width = rem_ref.shape
    turn, pair = lane_tools(frames, width)

    def remainder_of(plane):
        return (plane.astype(jnp.float32) - low_of(wl_ref, plane, turn)).astype(jnp.bfloat16)

    planes = jnp.concatenate(
        [remainder_of(xb_ref[...]), rem_ref[...], remainder_of(xa_ref[...])], axis=0
    )
    mixed = jnp.dot(wz_ref[...], planes, preferred_element_type=jnp.float32)
    filtered = mixed[:frames] + turn(mixed[frames:])
    square = filtered * filtered
    magnitude = jnp.sqrt(square + pair(square))
    scale = jnp.maximum(magnitude - cut, 0.0) / jnp.maximum(magnitude, cut)
    out_ref[...] = (low_ref[...] + filtered * scale).astype(out_ref.dtype)


def post_of(plane, before, after, low_t, filter_t):
    frames, width = plane.shape
    nb = 4096 if width % 4096 == 0 else width
    lane_spec = pl.BlockSpec((frames, nb), lambda i: (0, i))
    whole2 = lambda shape: pl.BlockSpec(shape, lambda i: (0, 0))
    params = pltpu.CompilerParams(dimension_semantics=("arbitrary",))
    low, rem = pl.pallas_call(
        own_kernel,
        out_shape=(
            jax.ShapeDtypeStruct(plane.shape, jnp.float32),
            jax.ShapeDtypeStruct(plane.shape, jnp.bfloat16),
        ),
        grid=(width // nb,),
        in_specs=[lane_spec, whole2(low_t.shape)],
        out_specs=(lane_spec, lane_spec),
        compiler_params=params,
        cost_estimate=pl.CostEstimate(
            flops=2 * width * frames * (2 * frames), transcendentals=0,
            bytes_accessed=plane.size * 8,
        ),
    )(plane, low_t)
    return pl.pallas_call(
        functools.partial(post_kernel, cut=SOFT_CUT),
        out_shape=jax.ShapeDtypeStruct(plane.shape, jnp.bfloat16),
        grid=(width // nb,),
        in_specs=[lane_spec] * 4 + [whole2(low_t.shape), whole2(filter_t.shape)],
        out_specs=lane_spec,
        compiler_params=params,
        cost_estimate=pl.CostEstimate(
            flops=2 * width * frames * (2 * frames) * 5, transcendentals=width * frames,
            bytes_accessed=plane.size * 12,
        ),
    )(low, rem, before, after, low_t, filter_t)


def solve_kernel(a_ref, x0_ref, s_ref, out_ref, *, steps):
    size = a_ref.shape[0]
    rows = lax.broadcasted_iota(jnp.int32, (size, size), 0)
    cols = lax.broadcasted_iota(jnp.int32, (size, size), 1)
    twice = jnp.where(rows == cols, 2.0, 0.0).astype(jnp.float32)
    a = a_ref[...]
    high = lax.Precision.HIGHEST

    def step(i, x):
        t = jnp.dot(a, x, precision=high, preferred_element_type=jnp.float32)
        return jnp.dot(x, twice - t, precision=high, preferred_element_type=jnp.float32)

    x = x0_ref[...]
    for i in range(steps):
        x = step(i, x)
    out_ref[...] = jnp.dot(x, s_ref[...], precision=high, preferred_element_type=jnp.float32)


def shrink_of(stacked, threshold_sq, rank_value):
    size = stacked.shape[0]
    unit_matrix = jnp.eye(size, dtype=jnp.float32)
    system = stacked + threshold_sq * unit_matrix
    start = unit_matrix * (2.0 / (threshold_sq * (2.0 + rank_value)))
    whole = pl.BlockSpec(memory_space=pltpu.VMEM)
    return pl.pallas_call(
        functools.partial(solve_kernel, steps=10),
        out_shape=jax.ShapeDtypeStruct((size, size), jnp.float32),
        in_specs=[whole, whole, whole],
        out_specs=whole,
    )(system, start, stacked)


def apply_frames(mix_real, mix_imag, field_values):
    direct = jnp.einsum("fg,zftw->zgtw", mix_real, field_values, preferred_element_type=jnp.float32)
    turned = jnp.einsum(
        "fg,zftw->zgtw", mix_imag, rotate(field_values), preferred_element_type=jnp.float32
    )
    return direct + turned


def soft_shrink(filtered):
    half_width = filtered.shape[-1] // 2
    real_part, imag_part = (filtered[..., :half_width], filtered[..., half_width:])
    magnitude = jnp.sqrt(real_part * real_part + imag_part * imag_part)
    scale_values = jnp.maximum(magnitude - SOFT_CUT, 0.0) / jnp.maximum(magnitude, SOFT_CUT)
    return filtered * jnp.concatenate([scale_values, scale_values], axis=-1)


def tree_sum(value, axis):
    count = lax.axis_size(axis)
    if count & (count - 1):
        return lax.psum(value, axis)
    step = 1
    while step < count:
        pairs = [(i, i ^ step) for i in range(count)]
        value = value + lax.ppermute(value, axis, pairs)
        step *= 2
    return value


def mix_frames(weights, field_values):
    half = weights.shape[1] // 2
    mixed = jnp.einsum("kh,ktw->htw", weights, field_values, preferred_element_type=jnp.float32)
    return mixed[:half] + rotate(mixed[half:])


def local(image, adjoint_data, coil_maps, spoke_counts, tile_map, blocks, z_kernel, rank_cap):
    frame_count = image.shape[1]
    fresh = fresh_image_of(
        image[0], adjoint_data[0], coil_maps[0], spoke_counts[0], tile_map[0], blocks
    )
    count = lax.axis_size("dom")
    forward = [(i, i + 1) for i in range(count - 1)]
    backward = [(target, source) for source, target in forward]
    flat = fresh.reshape(frame_count, -1)
    rows_real = flat
    rows_turned = rotate(fresh).reshape(frame_count, -1)
    gram_real = jnp.einsum("fn,gn->fg", rows_real, rows_real, preferred_element_type=jnp.float32)
    gram_imag = jnp.einsum("fn,gn->fg", rows_turned, rows_real, preferred_element_type=jnp.float32)
    gram_real, gram_imag = tree_sum(jnp.stack([gram_real, gram_imag]), "dom")
    flat, gram_real, gram_imag = lax.optimization_barrier((flat, gram_real, gram_imag))
    fresh_before = lax.ppermute(flat, "dom", forward)
    fresh_after = lax.ppermute(flat, "dom", backward)
    stacked = jnp.block([[gram_real, -gram_imag], [gram_imag, gram_real]])
    rank_value = rank_cap[0].astype(jnp.float32)
    threshold_sq = jnp.trace(gram_real) / rank_value
    shrink = shrink_of(stacked, threshold_sq, rank_value)
    shrink_real = shrink[:frame_count, :frame_count].astype(jnp.bfloat16)
    shrink_imag = shrink[frame_count:, :frame_count].astype(jnp.bfloat16)
    low_t = jnp.concatenate([shrink_real, shrink_imag], axis=1).T
    taps = z_kernel.shape[0]
    filter_weights = jnp.concatenate([z_kernel[:, 0], z_kernel[:, 1]], axis=-1)
    filter_t = filter_weights.reshape(taps * frame_count, 2 * frame_count).T
    out = post_of(flat, fresh_before, fresh_after, low_t, filter_t)
    return out.reshape(image.shape)


def solution(mesh):
    return jax.shard_map(
        local,
        mesh=mesh,
        in_specs=(
            P(("groups", "dom"), None, None, None),
            P(("groups", "dom"), None, None, None),
            P(("groups", "dom"), None, None, None),
            P(("groups", "dom"), None),
            P(("groups", "dom"), None, None, None, None),
            P(),
            P(),
            P(),
        ),
        out_specs=P(("groups", "dom"), None, None, None),
        check_vma=False,
    )
```

```python
import jax
import jax.numpy as jnp
from jax import lax
from jax.sharding import PartitionSpec as P
import functools
from jax.experimental import pallas as pl
from jax.experimental.pallas import tpu as pltpu

SOFT_CUT = 0.25


def padded_2(block, sides, width):
    for axis, dim in sides:
        count = lax.axis_size(axis)
        forward = [(i, i + 1) for i in range(count - 1)]
        backward = [(target, source) for source, target in forward]
        low = lax.ppermute(
            lax.slice_in_dim(block, block.shape[dim] - width, None, axis=dim), axis, forward
        )
        high = lax.ppermute(lax.slice_in_dim(block, 0, width, axis=dim), axis, backward)
        block = jnp.concatenate([low, block, high], axis=dim)
    return block


def rotate(field_values):
    half_width = field_values.shape[-1] // 2
    return jnp.concatenate(
        [-field_values[..., half_width:], field_values[..., :half_width]], axis=-1
    )


def complex_times(left_value, right_value):
    half_width = left_value.shape[-1] // 2
    left_real, left_imag = (left_value[..., :half_width], left_value[..., half_width:])
    right_real, right_imag = (right_value[..., :half_width], right_value[..., half_width:])
    return jnp.concatenate(
        [
            left_real * right_real - left_imag * right_imag,
            left_real * right_imag + left_imag * right_real,
        ],
        axis=-1,
    )


def conj_times(left_value, right_value):
    half_width = left_value.shape[-1] // 2
    left_real, left_imag = (left_value[..., :half_width], left_value[..., half_width:])
    right_real, right_imag = (right_value[..., :half_width], right_value[..., half_width:])
    return jnp.concatenate(
        [
            left_real * right_real + left_imag * right_imag,
            left_real * right_imag - left_imag * right_real,
        ],
        axis=-1,
    )


def grid_gradient(image_plane, plane_maps, counts, plane_map, blocks):
    frame_count, tile_count, lane_width = image_plane.shape
    read_tiles, link_count = (plane_map.shape[2], plane_map.shape[3])
    coil_count = plane_maps.shape[0]
    tile_ids = jnp.arange(tile_count, dtype=jnp.int32)

    def one_slot(spoke_slot, accum):
        tile_index = lax.dynamic_index_in_dim(plane_map, spoke_slot, axis=1, keepdims=False)
        flat_index = tile_index.reshape(frame_count, read_tiles * link_count)
        image_picked = jnp.take_along_axis(image_plane, flat_index[:, :, None], axis=1)
        image_picked = image_picked.reshape(frame_count, read_tiles, link_count, lane_width)
        maps_picked = jnp.take(plane_maps, flat_index.reshape(-1), axis=1)
        maps_picked = maps_picked.reshape(
            coil_count, frame_count, read_tiles, link_count, lane_width
        ).astype(jnp.float32)
        coil_tiles = complex_times(maps_picked, image_picked.astype(jnp.float32)[None]).astype(
            jnp.bfloat16
        )
        samples = jnp.einsum(
            "ctqji,qjio->ctqo", coil_tiles, blocks, preferred_element_type=jnp.float32
        )
        live_mask = (counts > spoke_slot).astype(jnp.float32)[None, :, None, None]
        samples = (samples * live_mask).astype(jnp.bfloat16)
        spread = jnp.einsum("ctqo,qjio->ctqji", samples, blocks, preferred_element_type=jnp.float32)
        back_sum = jnp.sum(conj_times(maps_picked, spread), axis=0)
        back_sum = back_sum.reshape(frame_count, read_tiles * link_count, lane_width)
        onehot = (flat_index[:, :, None] == tile_ids).astype(jnp.float32)
        return accum + jnp.einsum("tkn,tkw->tnw", onehot, back_sum, precision=lax.Precision.HIGHEST)

    most_spokes = jnp.max(counts)
    start_value = jnp.zeros((frame_count, tile_count, lane_width), jnp.float32)
    return lax.fori_loop(0, most_spokes, one_slot, start_value)


def gradient_kernel(idx_ref, cnt_ref, nsl_ref, img_ref, adj_ref, maps_ref,
                    bf_ref, bt_ref, btr_ref, out_ref, x_scr, rx_scr, g_scr, g2_scr,
                    lhs_a, y_a, ry_a, lhs_b, y_b, ry_b, mrr_ref, mii_ref, *, fb, slots, links,
                    coils):
    b = pl.program_id(0)
    reads = links // 2
    img = img_ref[...].astype(jnp.float32)
    x_scr[...] = img
    half = img.shape[-1] // 2
    lane = lax.broadcasted_iota(jnp.int32, img.shape, 2)
    sign = jnp.where(lane < half, -1.0, 1.0).astype(jnp.float32)
    rx_scr[...] = pltpu.roll(img, half, 2) * sign

    @pl.when(b == 0)
    def _():
        maps = maps_ref[...].astype(jnp.float32)
        map_lane = lax.broadcasted_iota(jnp.int32, maps.shape, 2) < half
        swapped = pltpu.roll(maps, half, 2)
        mrr_ref[...] = jnp.where(map_lane, maps, swapped)
        mii_ref[...] = jnp.where(map_lane, swapped, maps)
    g_scr[...] = jnp.zeros_like(g_scr)
    g2_scr[...] = jnp.zeros_like(g2_scr)
    lhs_a[...] = jnp.zeros_like(lhs_a)
    lhs_b[...] = jnp.zeros_like(lhs_b)
    accums = (g_scr, g2_scr)

    def slot_body(s, carry):
        for q in range(reads):
            lhs_scr, y_scr, ry_scr = (lhs_a, y_a, ry_a) if q % 2 == 0 else (lhs_b, y_b, ry_b)

            def gather_t(t, c):
                frame = b * fb + t
                base = (frame * slots + s) * links + q * 2
                row = pl.multiple_of(t * coils, coils)
                for j in range(2):
                    p = idx_ref[base + j]
                    xv = x_scr[t, pl.ds(p, 1), :]
                    rxv = rx_scr[t, pl.ds(p, 1), :]
                    ct = mrr_ref[p] * xv + mii_ref[p] * rxv
                    lhs_scr[pl.ds(row, coils), pl.ds(j * 128, 128)] = ct.astype(jnp.bfloat16)
                return c

            lax.fori_loop(0, fb, gather_t, 0, unroll=True)
            samples = jnp.dot(lhs_scr[...], bf_ref[q], preferred_element_type=jnp.float32)
            samples = samples.astype(jnp.bfloat16)
            y_scr[...] = jnp.dot(samples, bt_ref[q], preferred_element_type=jnp.float32)
            ry_scr[...] = jnp.dot(samples, btr_ref[q], preferred_element_type=jnp.float32)

            def scatter_t(t, c):
                frame = b * fb + t
                live = cnt_ref[frame] > s
                base = (frame * slots + s) * links + q * 2
                row = pl.multiple_of(t * coils, coils)

                keep = live.astype(jnp.float32)
                for j in range(2):
                    p = idx_ref[base + j]
                    yv = y_scr[pl.ds(row, coils), pl.ds(j * 128, 128)]
                    ryv = ry_scr[pl.ds(row, coils), pl.ds(j * 128, 128)]
                    v = mrr_ref[p] * yv - mii_ref[p] * ryv
                    back = jnp.sum(v, axis=0, keepdims=True) * keep
                    acc = accums[j]
                    acc[t, pl.ds(p, 1), :] = acc[t, pl.ds(p, 1), :] + back
                return c

            lax.fori_loop(0, fb, scatter_t, 0, unroll=True)
        return carry

    lax.fori_loop(0, nsl_ref[b], slot_body, 0)
    grad = g_scr[...] + g2_scr[...]
    out_ref[...] = (x_scr[...] - (grad - adj_ref[...].astype(jnp.float32))).astype(out_ref.dtype)


def fresh_image_of(image_plane, adjoint_plane, plane_maps, counts, plane_map, blocks):
    frame_count, tile_count, lane_width = image_plane.shape
    slots, reads, links = plane_map.shape[1], plane_map.shape[2], plane_map.shape[3]
    coils = plane_maps.shape[0]
    fb = 32 if frame_count % 32 == 0 else frame_count
    nblocks = frame_count // fb
    half = lane_width // 2
    maps_t = jnp.swapaxes(plane_maps, 0, 1)
    bf = blocks.reshape(reads, links * lane_width, lane_width)
    bt4 = jnp.transpose(blocks, (0, 3, 1, 2))
    bt = bt4.reshape(reads, lane_width, links * lane_width)
    btr = rotate(bt4).reshape(reads, lane_width, links * lane_width)
    idx = plane_map.reshape(-1).astype(jnp.int32)
    cnt = counts.astype(jnp.int32)
    nsl = jnp.minimum(jnp.max(cnt.reshape(nblocks, fb), axis=1), slots).astype(jnp.int32)
    kernel = functools.partial(
        gradient_kernel, fb=fb, slots=slots, links=reads * links, coils=coils
    )
    plane_spec = pl.BlockSpec((fb, tile_count, lane_width), lambda b, *_: (b, 0, 0))
    whole3 = lambda shape: pl.BlockSpec(shape, lambda b, *_: (0, 0, 0))
    flops = 2 * frame_count * slots * reads * coils * (links * lane_width) * lane_width * 3
    return pl.pallas_call(
        kernel,
        out_shape=jax.ShapeDtypeStruct(image_plane.shape, jnp.bfloat16),
        grid_spec=pltpu.PrefetchScalarGridSpec(
            num_scalar_prefetch=3,
            grid=(nblocks,),
            in_specs=[
                plane_spec,
                plane_spec,
                whole3(maps_t.shape),
                whole3(bf.shape),
                whole3(bt.shape),
                whole3(btr.shape),
            ],
            out_specs=plane_spec,
            scratch_shapes=[
                pltpu.VMEM((fb, tile_count, lane_width), jnp.float32),
                pltpu.VMEM((fb, tile_count, lane_width), jnp.float32),
                pltpu.VMEM((fb, tile_count, lane_width), jnp.float32),
                pltpu.VMEM((fb, tile_count, lane_width), jnp.float32),
                pltpu.VMEM((fb * coils, links * lane_width), jnp.bfloat16),
                pltpu.VMEM((fb * coils, links * lane_width), jnp.float32),
                pltpu.VMEM((fb * coils, links * lane_width), jnp.float32),
                pltpu.VMEM((fb * coils, links * lane_width), jnp.bfloat16),
                pltpu.VMEM((fb * coils, links * lane_width), jnp.float32),
                pltpu.VMEM((fb * coils, links * lane_width), jnp.float32),
                pltpu.VMEM(maps_t.shape, jnp.float32),
                pltpu.VMEM(maps_t.shape, jnp.float32),
            ],
        ),
        compiler_params=pltpu.CompilerParams(dimension_semantics=("arbitrary",)),
        cost_estimate=pl.CostEstimate(
            flops=flops, transcendentals=0, bytes_accessed=image_plane.size * 6 + maps_t.size * 2
        ),
    )(idx, cnt, nsl, image_plane, adjoint_plane, maps_t, bf, bt, btr)


def lane_tools(frames, width):
    lane = lax.broadcasted_iota(jnp.int32, (frames, width), 1) % 128
    low_lane = lane < 64

    def turn(v):
        return jnp.where(low_lane, -pltpu.roll(v, width - 64, 1), pltpu.roll(v, 64, 1))

    def pair(v):
        return jnp.where(low_lane, pltpu.roll(v, width - 64, 1), pltpu.roll(v, 64, 1))

    return turn, pair


def low_of(wl_ref, plane, turn):
    frames = plane.shape[0]
    mixed = jnp.dot(wl_ref[...], plane, preferred_element_type=jnp.float32)
    return mixed[:frames] + turn(mixed[frames:])


def own_kernel(x_ref, wl_ref, low_ref, rem_ref):
    frames, width = x_ref.shape
    turn, _ = lane_tools(frames, width)
    x = x_ref[...]
    low = low_of(wl_ref, x, turn)
    low_ref[...] = low
    rem_ref[...] = (x.astype(jnp.float32) - low).astype(jnp.bfloat16)


def post_kernel(low_ref, rem_ref, xb_ref, xa_ref, wl_ref, wz_ref, out_ref, *, cut):
    frames, width = rem_ref.shape
    turn, pair = lane_tools(frames, width)

    def remainder_of(plane):
        return (plane.astype(jnp.float32) - low_of(wl_ref, plane, turn)).astype(jnp.bfloat16)

    planes = jnp.concatenate(
        [remainder_of(xb_ref[...]), rem_ref[...], remainder_of(xa_ref[...])], axis=0
    )
    mixed = jnp.dot(wz_ref[...], planes, preferred_element_type=jnp.float32)
    filtered = mixed[:frames] + turn(mixed[frames:])
    square = filtered * filtered
    magnitude = jnp.sqrt(square + pair(square))
    scale = jnp.maximum(magnitude - cut, 0.0) / jnp.maximum(magnitude, cut)
    result = low_ref[...] + filtered * scale
    out_ref[...] = result.reshape(out_ref.shape).astype(out_ref.dtype)


def post_of(plane, before, after, low_t, filter_t):
    frames, width = plane.shape
    nb = 4096 if width % 4096 == 0 else width
    lane_spec = pl.BlockSpec((frames, nb), lambda i: (0, i))
    whole2 = lambda shape: pl.BlockSpec(shape, lambda i: (0, 0))
    params = pltpu.CompilerParams(dimension_semantics=("arbitrary",))
    low, rem = pl.pallas_call(
        own_kernel,
        out_shape=(
            jax.ShapeDtypeStruct(plane.shape, jnp.float32),
            jax.ShapeDtypeStruct(plane.shape, jnp.bfloat16),
        ),
        grid=(width // nb,),
        in_specs=[lane_spec, whole2(low_t.shape)],
        out_specs=(lane_spec, lane_spec),
        compiler_params=params,
        cost_estimate=pl.CostEstimate(
            flops=2 * width * frames * (2 * frames), transcendentals=0,
            bytes_accessed=plane.size * 8,
        ),
    )(plane, low_t)
    tile_spec = pl.BlockSpec((frames, nb // 128, 128), lambda i: (0, i, 0))
    return pl.pallas_call(
        functools.partial(post_kernel, cut=SOFT_CUT),
        out_shape=jax.ShapeDtypeStruct((frames, width // 128, 128), jnp.bfloat16),
        grid=(width // nb,),
        in_specs=[lane_spec] * 4 + [whole2(low_t.shape), whole2(filter_t.shape)],
        out_specs=tile_spec,
        compiler_params=params,
        cost_estimate=pl.CostEstimate(
            flops=2 * width * frames * (2 * frames) * 5, transcendentals=width * frames,
            bytes_accessed=plane.size * 12,
        ),
    )(low, rem, before, after, low_t, filter_t)


def solve_kernel(a_ref, x0_ref, s_ref, out_ref, *, steps):
    size = a_ref.shape[0]
    rows = lax.broadcasted_iota(jnp.int32, (size, size), 0)
    cols = lax.broadcasted_iota(jnp.int32, (size, size), 1)
    twice = jnp.where(rows == cols, 2.0, 0.0).astype(jnp.float32)
    a = a_ref[...]
    high = lax.Precision.HIGHEST

    def step(i, x):
        t = jnp.dot(a, x, precision=high, preferred_element_type=jnp.float32)
        return jnp.dot(x, twice - t, precision=high, preferred_element_type=jnp.float32)

    x = x0_ref[...]
    for i in range(steps):
        x = step(i, x)
    out_ref[...] = jnp.dot(x, s_ref[...], precision=high, preferred_element_type=jnp.float32)


def shrink_of(stacked, threshold_sq, rank_value):
    size = stacked.shape[0]
    unit_matrix = jnp.eye(size, dtype=jnp.float32)
    system = stacked + threshold_sq * unit_matrix
    start = unit_matrix * (2.0 / (threshold_sq * (2.0 + rank_value)))
    whole = pl.BlockSpec(memory_space=pltpu.VMEM)
    return pl.pallas_call(
        functools.partial(solve_kernel, steps=10),
        out_shape=jax.ShapeDtypeStruct((size, size), jnp.float32),
        in_specs=[whole, whole, whole],
        out_specs=whole,
    )(system, start, stacked)


def apply_frames(mix_real, mix_imag, field_values):
    direct = jnp.einsum("fg,zftw->zgtw", mix_real, field_values, preferred_element_type=jnp.float32)
    turned = jnp.einsum(
        "fg,zftw->zgtw", mix_imag, rotate(field_values), preferred_element_type=jnp.float32
    )
    return direct + turned


def soft_shrink(filtered):
    half_width = filtered.shape[-1] // 2
    real_part, imag_part = (filtered[..., :half_width], filtered[..., half_width:])
    magnitude = jnp.sqrt(real_part * real_part + imag_part * imag_part)
    scale_values = jnp.maximum(magnitude - SOFT_CUT, 0.0) / jnp.maximum(magnitude, SOFT_CUT)
    return filtered * jnp.concatenate([scale_values, scale_values], axis=-1)


def tree_sum(value, axis):
    count = lax.axis_size(axis)
    if count & (count - 1):
        return lax.psum(value, axis)
    step = 1
    while step < count:
        pairs = [(i, i ^ step) for i in range(count)]
        value = value + lax.ppermute(value, axis, pairs)
        step *= 2
    return value


def mix_frames(weights, field_values):
    half = weights.shape[1] // 2
    mixed = jnp.einsum("kh,ktw->htw", weights, field_values, preferred_element_type=jnp.float32)
    return mixed[:half] + rotate(mixed[half:])


def local(image, adjoint_data, coil_maps, spoke_counts, tile_map, blocks, z_kernel, rank_cap):
    frame_count = image.shape[1]
    fresh = fresh_image_of(
        image[0], adjoint_data[0], coil_maps[0], spoke_counts[0], tile_map[0], blocks
    )
    count = lax.axis_size("dom")
    forward = [(i, i + 1) for i in range(count - 1)]
    backward = [(target, source) for source, target in forward]
    flat = fresh.reshape(frame_count, -1)
    rows_real = flat
    rows_turned = rotate(fresh).reshape(frame_count, -1)
    gram_real = jnp.einsum("fn,gn->fg", rows_real, rows_real, preferred_element_type=jnp.float32)
    gram_imag = jnp.einsum("fn,gn->fg", rows_turned, rows_real, preferred_element_type=jnp.float32)
    gram_real, gram_imag = tree_sum(jnp.stack([gram_real, gram_imag]), "dom")
    flat, gram_real, gram_imag = lax.optimization_barrier((flat, gram_real, gram_imag))
    fresh_before = lax.ppermute(flat, "dom", forward)
    fresh_after = lax.ppermute(flat, "dom", backward)
    stacked = jnp.block([[gram_real, -gram_imag], [gram_imag, gram_real]])
    rank_value = rank_cap[0].astype(jnp.float32)
    threshold_sq = jnp.trace(gram_real) / rank_value
    shrink = shrink_of(stacked, threshold_sq, rank_value)
    shrink_real = shrink[:frame_count, :frame_count].astype(jnp.bfloat16)
    shrink_imag = shrink[frame_count:, :frame_count].astype(jnp.bfloat16)
    low_t = jnp.concatenate([shrink_real, shrink_imag], axis=1).T
    taps = z_kernel.shape[0]
    filter_weights = jnp.concatenate([z_kernel[:, 0], z_kernel[:, 1]], axis=-1)
    filter_t = filter_weights.reshape(taps * frame_count, 2 * frame_count).T
    out = post_of(flat, fresh_before, fresh_after, low_t, filter_t)
    return out.reshape(image.shape)


def solution(mesh):
    return jax.shard_map(
        local,
        mesh=mesh,
        in_specs=(
            P(("groups", "dom"), None, None, None),
            P(("groups", "dom"), None, None, None),
            P(("groups", "dom"), None, None, None),
            P(("groups", "dom"), None),
            P(("groups", "dom"), None, None, None, None),
            P(),
            P(),
            P(),
        ),
        out_specs=P(("groups", "dom"), None, None, None),
        check_vma=False,
    )
```

```python
import jax
import jax.numpy as jnp
from jax import lax
from jax.sharding import PartitionSpec as P
import functools
from jax.experimental import pallas as pl
from jax.experimental.pallas import tpu as pltpu

SOFT_CUT = 0.25


def padded_2(block, sides, width):
    for axis, dim in sides:
        count = lax.axis_size(axis)
        forward = [(i, i + 1) for i in range(count - 1)]
        backward = [(target, source) for source, target in forward]
        low = lax.ppermute(
            lax.slice_in_dim(block, block.shape[dim] - width, None, axis=dim), axis, forward
        )
        high = lax.ppermute(lax.slice_in_dim(block, 0, width, axis=dim), axis, backward)
        block = jnp.concatenate([low, block, high], axis=dim)
    return block


def rotate(field_values):
    half_width = field_values.shape[-1] // 2
    return jnp.concatenate(
        [-field_values[..., half_width:], field_values[..., :half_width]], axis=-1
    )


def complex_times(left_value, right_value):
    half_width = left_value.shape[-1] // 2
    left_real, left_imag = (left_value[..., :half_width], left_value[..., half_width:])
    right_real, right_imag = (right_value[..., :half_width], right_value[..., half_width:])
    return jnp.concatenate(
        [
            left_real * right_real - left_imag * right_imag,
            left_real * right_imag + left_imag * right_real,
        ],
        axis=-1,
    )


def conj_times(left_value, right_value):
    half_width = left_value.shape[-1] // 2
    left_real, left_imag = (left_value[..., :half_width], left_value[..., half_width:])
    right_real, right_imag = (right_value[..., :half_width], right_value[..., half_width:])
    return jnp.concatenate(
        [
            left_real * right_real + left_imag * right_imag,
            left_real * right_imag - left_imag * right_real,
        ],
        axis=-1,
    )


def grid_gradient(image_plane, plane_maps, counts, plane_map, blocks):
    frame_count, tile_count, lane_width = image_plane.shape
    read_tiles, link_count = (plane_map.shape[2], plane_map.shape[3])
    coil_count = plane_maps.shape[0]
    tile_ids = jnp.arange(tile_count, dtype=jnp.int32)

    def one_slot(spoke_slot, accum):
        tile_index = lax.dynamic_index_in_dim(plane_map, spoke_slot, axis=1, keepdims=False)
        flat_index = tile_index.reshape(frame_count, read_tiles * link_count)
        image_picked = jnp.take_along_axis(image_plane, flat_index[:, :, None], axis=1)
        image_picked = image_picked.reshape(frame_count, read_tiles, link_count, lane_width)
        maps_picked = jnp.take(plane_maps, flat_index.reshape(-1), axis=1)
        maps_picked = maps_picked.reshape(
            coil_count, frame_count, read_tiles, link_count, lane_width
        ).astype(jnp.float32)
        coil_tiles = complex_times(maps_picked, image_picked.astype(jnp.float32)[None]).astype(
            jnp.bfloat16
        )
        samples = jnp.einsum(
            "ctqji,qjio->ctqo", coil_tiles, blocks, preferred_element_type=jnp.float32
        )
        live_mask = (counts > spoke_slot).astype(jnp.float32)[None, :, None, None]
        samples = (samples * live_mask).astype(jnp.bfloat16)
        spread = jnp.einsum("ctqo,qjio->ctqji", samples, blocks, preferred_element_type=jnp.float32)
        back_sum = jnp.sum(conj_times(maps_picked, spread), axis=0)
        back_sum = back_sum.reshape(frame_count, read_tiles * link_count, lane_width)
        onehot = (flat_index[:, :, None] == tile_ids).astype(jnp.float32)
        return accum + jnp.einsum("tkn,tkw->tnw", onehot, back_sum, precision=lax.Precision.HIGHEST)

    most_spokes = jnp.max(counts)
    start_value = jnp.zeros((frame_count, tile_count, lane_width), jnp.float32)
    return lax.fori_loop(0, most_spokes, one_slot, start_value)


def gradient_kernel(idx_ref, cnt_ref, nsl_ref, img_ref, adj_ref, maps_ref,
                    bf_ref, out_ref, x_scr, rx_scr, g_scr, g2_scr,
                    lhs_a, y_a, ry_a, lhs_b, y_b, ry_b, mrr_ref, mii_ref, *, fb, slots, links,
                    coils):
    b = pl.program_id(0)
    reads = links // 2
    img = img_ref[...].astype(jnp.float32)
    x_scr[...] = img
    half = img.shape[-1] // 2
    lane = lax.broadcasted_iota(jnp.int32, img.shape, 2)
    sign = jnp.where(lane < half, -1.0, 1.0).astype(jnp.float32)
    rx_scr[...] = pltpu.roll(img, half, 2) * sign

    @pl.when(b == 0)
    def _():
        maps = maps_ref[...].astype(jnp.float32)
        map_lane = lax.broadcasted_iota(jnp.int32, maps.shape, 2) < half
        swapped = pltpu.roll(maps, half, 2)
        mrr_ref[...] = jnp.where(map_lane, maps, swapped)
        mii_ref[...] = jnp.where(map_lane, swapped, maps)
    g_scr[...] = jnp.zeros_like(g_scr)
    g2_scr[...] = jnp.zeros_like(g2_scr)
    lhs_a[...] = jnp.zeros_like(lhs_a)
    lhs_b[...] = jnp.zeros_like(lhs_b)
    accums = (g_scr, g2_scr)

    def slot_body(s, carry):
        for q in range(reads):
            lhs_scr, y_scr, ry_scr = (lhs_a, y_a, ry_a) if q % 2 == 0 else (lhs_b, y_b, ry_b)

            def gather_t(t, c):
                frame = b * fb + t
                base = (frame * slots + s) * links + q * 2
                row = pl.multiple_of(t * coils, coils)
                for j in range(2):
                    p = idx_ref[base + j]
                    xv = x_scr[t, pl.ds(p, 1), :]
                    rxv = rx_scr[t, pl.ds(p, 1), :]
                    ct = mrr_ref[p] * xv + mii_ref[p] * rxv
                    lhs_scr[pl.ds(row, coils), pl.ds(j * 128, 128)] = ct.astype(jnp.bfloat16)
                return c

            lax.fori_loop(0, fb, gather_t, 0, unroll=True)
            samples = jnp.dot(lhs_scr[...], bf_ref[q], preferred_element_type=jnp.float32)
            samples = samples.astype(jnp.bfloat16)
            pairs = (((1,), (1,)), ((), ()))
            for j in range(2):
                block = bf_ref[q, pl.ds(j * 128, 128), :]
                turned = jnp.concatenate([-block[64:], block[:64]], axis=0)
                y_scr[:, pl.ds(j * 128, 128)] = lax.dot_general(
                    samples, block, pairs, preferred_element_type=jnp.float32)
                ry_scr[:, pl.ds(j * 128, 128)] = lax.dot_general(
                    samples, turned, pairs, preferred_element_type=jnp.float32)

            def scatter_t(t, c):
                frame = b * fb + t
                live = cnt_ref[frame] > s
                base = (frame * slots + s) * links + q * 2
                row = pl.multiple_of(t * coils, coils)

                keep = live.astype(jnp.float32)
                for j in range(2):
                    p = idx_ref[base + j]
                    yv = y_scr[pl.ds(row, coils), pl.ds(j * 128, 128)]
                    ryv = ry_scr[pl.ds(row, coils), pl.ds(j * 128, 128)]
                    v = mrr_ref[p] * yv - mii_ref[p] * ryv
                    back = jnp.sum(v, axis=0, keepdims=True) * keep
                    acc = accums[j]
                    acc[t, pl.ds(p, 1), :] = acc[t, pl.ds(p, 1), :] + back
                return c

            lax.fori_loop(0, fb, scatter_t, 0, unroll=True)
        return carry

    lax.fori_loop(0, nsl_ref[b], slot_body, 0)
    grad = g_scr[...] + g2_scr[...]
    out_ref[...] = (x_scr[...] - (grad - adj_ref[...].astype(jnp.float32))).astype(out_ref.dtype)


def fresh_image_of(image_plane, adjoint_plane, plane_maps, counts, plane_map, blocks):
    frame_count, tile_count, lane_width = image_plane.shape
    slots, reads, links = plane_map.shape[1], plane_map.shape[2], plane_map.shape[3]
    coils = plane_maps.shape[0]
    fb = 32 if frame_count % 32 == 0 else frame_count
    nblocks = frame_count // fb
    half = lane_width // 2
    maps_t = jnp.swapaxes(plane_maps, 0, 1)
    bf = blocks.reshape(reads, links * lane_width, lane_width)
    idx = plane_map.reshape(-1).astype(jnp.int32)
    cnt = counts.astype(jnp.int32)
    nsl = jnp.minimum(jnp.max(cnt.reshape(nblocks, fb), axis=1), slots).astype(jnp.int32)
    kernel = functools.partial(
        gradient_kernel, fb=fb, slots=slots, links=reads * links, coils=coils
    )
    plane_spec = pl.BlockSpec((fb, tile_count, lane_width), lambda b, *_: (b, 0, 0))
    whole3 = lambda shape: pl.BlockSpec(shape, lambda b, *_: (0, 0, 0))
    flops = 2 * frame_count * slots * reads * coils * (links * lane_width) * lane_width * 3
    return pl.pallas_call(
        kernel,
        out_shape=jax.ShapeDtypeStruct(image_plane.shape, jnp.bfloat16),
        grid_spec=pltpu.PrefetchScalarGridSpec(
            num_scalar_prefetch=3,
            grid=(nblocks,),
            in_specs=[
                plane_spec,
                plane_spec,
                whole3(maps_t.shape),
                whole3(bf.shape),
            ],
            out_specs=plane_spec,
            scratch_shapes=[
                pltpu.VMEM((fb, tile_count, lane_width), jnp.float32),
                pltpu.VMEM((fb, tile_count, lane_width), jnp.float32),
                pltpu.VMEM((fb, tile_count, lane_width), jnp.float32),
                pltpu.VMEM((fb, tile_count, lane_width), jnp.float32),
                pltpu.VMEM((fb * coils, links * lane_width), jnp.bfloat16),
                pltpu.VMEM((fb * coils, links * lane_width), jnp.float32),
                pltpu.VMEM((fb * coils, links * lane_width), jnp.float32),
                pltpu.VMEM((fb * coils, links * lane_width), jnp.bfloat16),
                pltpu.VMEM((fb * coils, links * lane_width), jnp.float32),
                pltpu.VMEM((fb * coils, links * lane_width), jnp.float32),
                pltpu.VMEM(maps_t.shape, jnp.float32),
                pltpu.VMEM(maps_t.shape, jnp.float32),
            ],
        ),
        compiler_params=pltpu.CompilerParams(dimension_semantics=("arbitrary",)),
        cost_estimate=pl.CostEstimate(
            flops=flops, transcendentals=0, bytes_accessed=image_plane.size * 6 + maps_t.size * 2
        ),
    )(idx, cnt, nsl, image_plane, adjoint_plane, maps_t, bf)


def lane_tools(frames, width):
    lane = lax.broadcasted_iota(jnp.int32, (frames, width), 1) % 128
    low_lane = lane < 64

    def turn(v):
        return jnp.where(low_lane, -pltpu.roll(v, width - 64, 1), pltpu.roll(v, 64, 1))

    def pair(v):
        return jnp.where(low_lane, pltpu.roll(v, width - 64, 1), pltpu.roll(v, 64, 1))

    return turn, pair


def low_of(wl_ref, plane, turn):
    frames = plane.shape[0]
    mixed = jnp.dot(wl_ref[...], plane, preferred_element_type=jnp.float32)
    return mixed[:frames] + turn(mixed[frames:])


def own_kernel(x_ref, wl_ref, low_ref, rem_ref):
    frames, width = x_ref.shape
    turn, _ = lane_tools(frames, width)
    x = x_ref[...]
    low = low_of(wl_ref, x, turn)
    low_ref[...] = low
    rem_ref[...] = (x.astype(jnp.float32) - low).astype(jnp.bfloat16)


def post_kernel(low_ref, rem_ref, xb_ref, xa_ref, wl_ref, wz_ref, out_ref, *, cut):
    frames, width = rem_ref.shape
    turn, pair = lane_tools(frames, width)

    def remainder_of(plane):
        return (plane.astype(jnp.float32) - low_of(wl_ref, plane, turn)).astype(jnp.bfloat16)

    planes = jnp.concatenate(
        [remainder_of(xb_ref[...]), rem_ref[...], remainder_of(xa_ref[...])], axis=0
    )
    mixed = jnp.dot(wz_ref[...], planes, preferred_element_type=jnp.float32)
    filtered = mixed[:frames] + turn(mixed[frames:])
    square = filtered * filtered
    magnitude = jnp.sqrt(square + pair(square))
    scale = jnp.maximum(magnitude - cut, 0.0) / jnp.maximum(magnitude, cut)
    result = low_ref[...] + filtered * scale
    out_ref[...] = result.reshape(out_ref.shape).astype(out_ref.dtype)


def post_of(plane, before, after, low_t, filter_t):
    frames, width = plane.shape
    nb = 4096 if width % 4096 == 0 else width
    lane_spec = pl.BlockSpec((frames, nb), lambda i: (0, i))
    whole2 = lambda shape: pl.BlockSpec(shape, lambda i: (0, 0))
    params = pltpu.CompilerParams(dimension_semantics=("arbitrary",))
    low, rem = pl.pallas_call(
        own_kernel,
        out_shape=(
            jax.ShapeDtypeStruct(plane.shape, jnp.float32),
            jax.ShapeDtypeStruct(plane.shape, jnp.bfloat16),
        ),
        grid=(width // nb,),
        in_specs=[lane_spec, whole2(low_t.shape)],
        out_specs=(lane_spec, lane_spec),
        compiler_params=params,
        cost_estimate=pl.CostEstimate(
            flops=2 * width * frames * (2 * frames), transcendentals=0,
            bytes_accessed=plane.size * 8,
        ),
    )(plane, low_t)
    tile_spec = pl.BlockSpec((frames, nb // 128, 128), lambda i: (0, i, 0))
    return pl.pallas_call(
        functools.partial(post_kernel, cut=SOFT_CUT),
        out_shape=jax.ShapeDtypeStruct((frames, width // 128, 128), jnp.bfloat16),
        grid=(width // nb,),
        in_specs=[lane_spec] * 4 + [whole2(low_t.shape), whole2(filter_t.shape)],
        out_specs=tile_spec,
        compiler_params=params,
        cost_estimate=pl.CostEstimate(
            flops=2 * width * frames * (2 * frames) * 5, transcendentals=width * frames,
            bytes_accessed=plane.size * 12,
        ),
    )(low, rem, before, after, low_t, filter_t)


def solve_kernel(a_ref, x0_ref, s_ref, out_ref, *, steps):
    size = a_ref.shape[0]
    rows = lax.broadcasted_iota(jnp.int32, (size, size), 0)
    cols = lax.broadcasted_iota(jnp.int32, (size, size), 1)
    twice = jnp.where(rows == cols, 2.0, 0.0).astype(jnp.float32)
    a = a_ref[...]
    high = lax.Precision.HIGHEST

    def step(i, x):
        t = jnp.dot(a, x, precision=high, preferred_element_type=jnp.float32)
        return jnp.dot(x, twice - t, precision=high, preferred_element_type=jnp.float32)

    x = x0_ref[...]
    for i in range(steps):
        x = step(i, x)
    out_ref[...] = jnp.dot(x, s_ref[...], precision=high, preferred_element_type=jnp.float32)


def shrink_of(stacked, threshold_sq, rank_value):
    size = stacked.shape[0]
    unit_matrix = jnp.eye(size, dtype=jnp.float32)
    system = stacked + threshold_sq * unit_matrix
    start = unit_matrix * (2.0 / (threshold_sq * (2.0 + rank_value)))
    whole = pl.BlockSpec(memory_space=pltpu.VMEM)
    return pl.pallas_call(
        functools.partial(solve_kernel, steps=10),
        out_shape=jax.ShapeDtypeStruct((size, size), jnp.float32),
        in_specs=[whole, whole, whole],
        out_specs=whole,
    )(system, start, stacked)


def apply_frames(mix_real, mix_imag, field_values):
    direct = jnp.einsum("fg,zftw->zgtw", mix_real, field_values, preferred_element_type=jnp.float32)
    turned = jnp.einsum(
        "fg,zftw->zgtw", mix_imag, rotate(field_values), preferred_element_type=jnp.float32
    )
    return direct + turned


def soft_shrink(filtered):
    half_width = filtered.shape[-1] // 2
    real_part, imag_part = (filtered[..., :half_width], filtered[..., half_width:])
    magnitude = jnp.sqrt(real_part * real_part + imag_part * imag_part)
    scale_values = jnp.maximum(magnitude - SOFT_CUT, 0.0) / jnp.maximum(magnitude, SOFT_CUT)
    return filtered * jnp.concatenate([scale_values, scale_values], axis=-1)


def tree_sum(value, axis):
    count = lax.axis_size(axis)
    if count & (count - 1):
        return lax.psum(value, axis)
    step = 1
    while step < count:
        pairs = [(i, i ^ step) for i in range(count)]
        value = value + lax.ppermute(value, axis, pairs)
        step *= 2
    return value


def mix_frames(weights, field_values):
    half = weights.shape[1] // 2
    mixed = jnp.einsum("kh,ktw->htw", weights, field_values, preferred_element_type=jnp.float32)
    return mixed[:half] + rotate(mixed[half:])


def local(image, adjoint_data, coil_maps, spoke_counts, tile_map, blocks, z_kernel, rank_cap):
    frame_count = image.shape[1]
    fresh = fresh_image_of(
        image[0], adjoint_data[0], coil_maps[0], spoke_counts[0], tile_map[0], blocks
    )
    count = lax.axis_size("dom")
    forward = [(i, i + 1) for i in range(count - 1)]
    backward = [(target, source) for source, target in forward]
    flat = fresh.reshape(frame_count, -1)
    rows_real = flat
    rows_turned = rotate(fresh).reshape(frame_count, -1)
    gram_real = jnp.einsum("fn,gn->fg", rows_real, rows_real, preferred_element_type=jnp.float32)
    gram_imag = jnp.einsum("fn,gn->fg", rows_turned, rows_real, preferred_element_type=jnp.float32)
    gram_real, gram_imag = tree_sum(jnp.stack([gram_real, gram_imag]), "dom")
    flat, gram_real, gram_imag = lax.optimization_barrier((flat, gram_real, gram_imag))
    fresh_before = lax.ppermute(flat, "dom", forward)
    fresh_after = lax.ppermute(flat, "dom", backward)
    stacked = jnp.block([[gram_real, -gram_imag], [gram_imag, gram_real]])
    rank_value = rank_cap[0].astype(jnp.float32)
    threshold_sq = jnp.trace(gram_real) / rank_value
    shrink = shrink_of(stacked, threshold_sq, rank_value)
    shrink_real = shrink[:frame_count, :frame_count].astype(jnp.bfloat16)
    shrink_imag = shrink[frame_count:, :frame_count].astype(jnp.bfloat16)
    low_t = jnp.concatenate([shrink_real, shrink_imag], axis=1).T
    taps = z_kernel.shape[0]
    filter_weights = jnp.concatenate([z_kernel[:, 0], z_kernel[:, 1]], axis=-1)
    filter_t = filter_weights.reshape(taps * frame_count, 2 * frame_count).T
    out = post_of(flat, fresh_before, fresh_after, low_t, filter_t)
    return out.reshape(image.shape)


def solution(mesh):
    return jax.shard_map(
        local,
        mesh=mesh,
        in_specs=(
            P(("groups", "dom"), None, None, None),
            P(("groups", "dom"), None, None, None),
            P(("groups", "dom"), None, None, None),
            P(("groups", "dom"), None),
            P(("groups", "dom"), None, None, None, None),
            P(),
            P(),
            P(),
        ),
        out_specs=P(("groups", "dom"), None, None, None),
        check_vma=False,
    )
```

```python
import jax
import jax.numpy as jnp
from jax import lax
from jax.sharding import PartitionSpec as P
import functools
from jax.experimental import pallas as pl
from jax.experimental.pallas import tpu as pltpu

SOFT_CUT = 0.25


def padded_2(block, sides, width):
    for axis, dim in sides:
        count = lax.axis_size(axis)
        forward = [(i, i + 1) for i in range(count - 1)]
        backward = [(target, source) for source, target in forward]
        low = lax.ppermute(
            lax.slice_in_dim(block, block.shape[dim] - width, None, axis=dim), axis, forward
        )
        high = lax.ppermute(lax.slice_in_dim(block, 0, width, axis=dim), axis, backward)
        block = jnp.concatenate([low, block, high], axis=dim)
    return block


def rotate(field_values):
    half_width = field_values.shape[-1] // 2
    return jnp.concatenate(
        [-field_values[..., half_width:], field_values[..., :half_width]], axis=-1
    )


def complex_times(left_value, right_value):
    half_width = left_value.shape[-1] // 2
    left_real, left_imag = (left_value[..., :half_width], left_value[..., half_width:])
    right_real, right_imag = (right_value[..., :half_width], right_value[..., half_width:])
    return jnp.concatenate(
        [
            left_real * right_real - left_imag * right_imag,
            left_real * right_imag + left_imag * right_real,
        ],
        axis=-1,
    )


def conj_times(left_value, right_value):
    half_width = left_value.shape[-1] // 2
    left_real, left_imag = (left_value[..., :half_width], left_value[..., half_width:])
    right_real, right_imag = (right_value[..., :half_width], right_value[..., half_width:])
    return jnp.concatenate(
        [
            left_real * right_real + left_imag * right_imag,
            left_real * right_imag - left_imag * right_real,
        ],
        axis=-1,
    )


def grid_gradient(image_plane, plane_maps, counts, plane_map, blocks):
    frame_count, tile_count, lane_width = image_plane.shape
    read_tiles, link_count = (plane_map.shape[2], plane_map.shape[3])
    coil_count = plane_maps.shape[0]
    tile_ids = jnp.arange(tile_count, dtype=jnp.int32)

    def one_slot(spoke_slot, accum):
        tile_index = lax.dynamic_index_in_dim(plane_map, spoke_slot, axis=1, keepdims=False)
        flat_index = tile_index.reshape(frame_count, read_tiles * link_count)
        image_picked = jnp.take_along_axis(image_plane, flat_index[:, :, None], axis=1)
        image_picked = image_picked.reshape(frame_count, read_tiles, link_count, lane_width)
        maps_picked = jnp.take(plane_maps, flat_index.reshape(-1), axis=1)
        maps_picked = maps_picked.reshape(
            coil_count, frame_count, read_tiles, link_count, lane_width
        ).astype(jnp.float32)
        coil_tiles = complex_times(maps_picked, image_picked.astype(jnp.float32)[None]).astype(
            jnp.bfloat16
        )
        samples = jnp.einsum(
            "ctqji,qjio->ctqo", coil_tiles, blocks, preferred_element_type=jnp.float32
        )
        live_mask = (counts > spoke_slot).astype(jnp.float32)[None, :, None, None]
        samples = (samples * live_mask).astype(jnp.bfloat16)
        spread = jnp.einsum("ctqo,qjio->ctqji", samples, blocks, preferred_element_type=jnp.float32)
        back_sum = jnp.sum(conj_times(maps_picked, spread), axis=0)
        back_sum = back_sum.reshape(frame_count, read_tiles * link_count, lane_width)
        onehot = (flat_index[:, :, None] == tile_ids).astype(jnp.float32)
        return accum + jnp.einsum("tkn,tkw->tnw", onehot, back_sum, precision=lax.Precision.HIGHEST)

    most_spokes = jnp.max(counts)
    start_value = jnp.zeros((frame_count, tile_count, lane_width), jnp.float32)
    return lax.fori_loop(0, most_spokes, one_slot, start_value)


def gradient_kernel(idx_ref, cnt_ref, nsl_ref, img_ref, adj_ref, maps_ref,
                    bf_ref, out_ref, x_scr, rx_scr, g_scr, g2_scr,
                    lhs_a, y_a, ry_a, lhs_b, y_b, ry_b, mrr_ref, mii_ref, *, fb, slots, links,
                    coils):
    b = pl.program_id(0)
    reads = links // 2
    img = img_ref[...].astype(jnp.float32)
    x_scr[...] = img
    half = img.shape[-1] // 2
    lane = lax.broadcasted_iota(jnp.int32, img.shape, 2)
    sign = jnp.where(lane < half, -1.0, 1.0).astype(jnp.float32)
    rx_scr[...] = pltpu.roll(img, half, 2) * sign

    @pl.when(b == 0)
    def _():
        maps = maps_ref[...].astype(jnp.float32)
        map_lane = lax.broadcasted_iota(jnp.int32, maps.shape, 2) < half
        swapped = pltpu.roll(maps, half, 2)
        mrr_ref[...] = jnp.where(map_lane, maps, swapped)
        mii_ref[...] = jnp.where(map_lane, swapped, maps)
    g_scr[...] = jnp.zeros_like(g_scr)
    g2_scr[...] = jnp.zeros_like(g2_scr)
    lhs_a[...] = jnp.zeros_like(lhs_a)
    lhs_b[...] = jnp.zeros_like(lhs_b)
    accums = (g_scr, g2_scr)

    def slot_body(s, carry):
        for q in range(reads):
            lhs_scr, y_scr, ry_scr = (lhs_a, y_a, ry_a) if q % 2 == 0 else (lhs_b, y_b, ry_b)

            def gather_t(t, c):
                frame = b * fb + t
                base = (frame * slots + s) * links + q * 2
                row = pl.multiple_of(t * coils, coils)
                for j in range(2):
                    p = idx_ref[base + j]
                    xv = x_scr[t, pl.ds(p, 1), :]
                    rxv = rx_scr[t, pl.ds(p, 1), :]
                    ct = mrr_ref[p] * xv + mii_ref[p] * rxv
                    lhs_scr[pl.ds(row, coils), pl.ds(j * 128, 128)] = ct.astype(jnp.bfloat16)
                return c

            lax.fori_loop(0, fb, gather_t, 0, unroll=True)
            samples = jnp.dot(lhs_scr[...], bf_ref[q], preferred_element_type=jnp.float32)
            samples = samples.astype(jnp.bfloat16)
            pairs = (((1,), (1,)), ((), ()))
            for j in range(2):
                block = bf_ref[q, pl.ds(j * 128, 128), :]
                turned = jnp.concatenate([-block[64:], block[:64]], axis=0)
                y_scr[:, pl.ds(j * 128, 128)] = lax.dot_general(
                    samples, block, pairs, preferred_element_type=jnp.float32)
                ry_scr[:, pl.ds(j * 128, 128)] = lax.dot_general(
                    samples, turned, pairs, preferred_element_type=jnp.float32)

            def scatter_t(t, c):
                frame = b * fb + t
                live = cnt_ref[frame] > s
                base = (frame * slots + s) * links + q * 2
                row = pl.multiple_of(t * coils, coils)

                keep = live.astype(jnp.float32)
                for j in range(2):
                    p = idx_ref[base + j]
                    yv = y_scr[pl.ds(row, coils), pl.ds(j * 128, 128)]
                    ryv = ry_scr[pl.ds(row, coils), pl.ds(j * 128, 128)]
                    v = mrr_ref[p] * yv - mii_ref[p] * ryv
                    back = jnp.sum(v, axis=0, keepdims=True) * keep
                    acc = accums[j]
                    acc[t, pl.ds(p, 1), :] = acc[t, pl.ds(p, 1), :] + back
                return c

            lax.fori_loop(0, fb, scatter_t, 0, unroll=True)
        return carry

    lax.fori_loop(0, nsl_ref[b], slot_body, 0)
    grad = g_scr[...] + g2_scr[...]
    out_ref[...] = (x_scr[...] - (grad - adj_ref[...].astype(jnp.float32))).astype(out_ref.dtype)


def fresh_image_of(image_plane, adjoint_plane, plane_maps, counts, plane_map, blocks):
    frame_count, tile_count, lane_width = image_plane.shape
    slots, reads, links = plane_map.shape[1], plane_map.shape[2], plane_map.shape[3]
    coils = plane_maps.shape[0]
    fb = 64 if frame_count % 64 == 0 else frame_count
    nblocks = frame_count // fb
    half = lane_width // 2
    maps_t = jnp.swapaxes(plane_maps, 0, 1)
    bf = blocks.reshape(reads, links * lane_width, lane_width)
    idx = plane_map.reshape(-1).astype(jnp.int32)
    cnt = counts.astype(jnp.int32)
    nsl = jnp.minimum(jnp.max(cnt.reshape(nblocks, fb), axis=1), slots).astype(jnp.int32)
    kernel = functools.partial(
        gradient_kernel, fb=fb, slots=slots, links=reads * links, coils=coils
    )
    plane_spec = pl.BlockSpec((fb, tile_count, lane_width), lambda b, *_: (b, 0, 0))
    whole3 = lambda shape: pl.BlockSpec(shape, lambda b, *_: (0, 0, 0))
    flops = 2 * frame_count * slots * reads * coils * (links * lane_width) * lane_width * 3
    return pl.pallas_call(
        kernel,
        out_shape=jax.ShapeDtypeStruct(image_plane.shape, jnp.bfloat16),
        grid_spec=pltpu.PrefetchScalarGridSpec(
            num_scalar_prefetch=3,
            grid=(nblocks,),
            in_specs=[
                plane_spec,
                plane_spec,
                whole3(maps_t.shape),
                whole3(bf.shape),
            ],
            out_specs=plane_spec,
            scratch_shapes=[
                pltpu.VMEM((fb, tile_count, lane_width), jnp.float32),
                pltpu.VMEM((fb, tile_count, lane_width), jnp.float32),
                pltpu.VMEM((fb, tile_count, lane_width), jnp.float32),
                pltpu.VMEM((fb, tile_count, lane_width), jnp.float32),
                pltpu.VMEM((fb * coils, links * lane_width), jnp.bfloat16),
                pltpu.VMEM((fb * coils, links * lane_width), jnp.float32),
                pltpu.VMEM((fb * coils, links * lane_width), jnp.float32),
                pltpu.VMEM((fb * coils, links * lane_width), jnp.bfloat16),
                pltpu.VMEM((fb * coils, links * lane_width), jnp.float32),
                pltpu.VMEM((fb * coils, links * lane_width), jnp.float32),
                pltpu.VMEM(maps_t.shape, jnp.float32),
                pltpu.VMEM(maps_t.shape, jnp.float32),
            ],
        ),
        compiler_params=pltpu.CompilerParams(dimension_semantics=("arbitrary",)),
        cost_estimate=pl.CostEstimate(
            flops=flops, transcendentals=0, bytes_accessed=image_plane.size * 6 + maps_t.size * 2
        ),
    )(idx, cnt, nsl, image_plane, adjoint_plane, maps_t, bf)


def lane_tools(frames, width):
    lane = lax.broadcasted_iota(jnp.int32, (frames, width), 1) % 128
    low_lane = lane < 64

    def turn(v):
        return jnp.where(low_lane, -pltpu.roll(v, width - 64, 1), pltpu.roll(v, 64, 1))

    def pair(v):
        return jnp.where(low_lane, pltpu.roll(v, width - 64, 1), pltpu.roll(v, 64, 1))

    return turn, pair


def low_of(wl_ref, plane, turn):
    frames = plane.shape[0]
    mixed = jnp.dot(wl_ref[...], plane, preferred_element_type=jnp.float32)
    return mixed[:frames] + turn(mixed[frames:])


def own_kernel(x_ref, wl_ref, low_ref, rem_ref):
    frames, width = x_ref.shape
    turn, _ = lane_tools(frames, width)
    x = x_ref[...]
    low = low_of(wl_ref, x, turn)
    low_ref[...] = low
    rem_ref[...] = (x.astype(jnp.float32) - low).astype(jnp.bfloat16)


def post_kernel(low_ref, rem_ref, xb_ref, xa_ref, wl_ref, wz_ref, out_ref, *, cut):
    frames, width = rem_ref.shape
    turn, pair = lane_tools(frames, width)

    def remainder_of(plane):
        return (plane.astype(jnp.float32) - low_of(wl_ref, plane, turn)).astype(jnp.bfloat16)

    planes = jnp.concatenate(
        [remainder_of(xb_ref[...]), rem_ref[...], remainder_of(xa_ref[...])], axis=0
    )
    mixed = jnp.dot(wz_ref[...], planes, preferred_element_type=jnp.float32)
    filtered = mixed[:frames] + turn(mixed[frames:])
    square = filtered * filtered
    magnitude = jnp.sqrt(square + pair(square))
    scale = jnp.maximum(magnitude - cut, 0.0) / jnp.maximum(magnitude, cut)
    result = low_ref[...] + filtered * scale
    out_ref[...] = result.reshape(out_ref.shape).astype(out_ref.dtype)


def post_of(plane, before, after, low_t, filter_t):
    frames, width = plane.shape
    nb = 4096 if width % 4096 == 0 else width
    lane_spec = pl.BlockSpec((frames, nb), lambda i: (0, i))
    whole2 = lambda shape: pl.BlockSpec(shape, lambda i: (0, 0))
    params = pltpu.CompilerParams(dimension_semantics=("arbitrary",))
    low, rem = pl.pallas_call(
        own_kernel,
        out_shape=(
            jax.ShapeDtypeStruct(plane.shape, jnp.float32),
            jax.ShapeDtypeStruct(plane.shape, jnp.bfloat16),
        ),
        grid=(width // nb,),
        in_specs=[lane_spec, whole2(low_t.shape)],
        out_specs=(lane_spec, lane_spec),
        compiler_params=params,
        cost_estimate=pl.CostEstimate(
            flops=2 * width * frames * (2 * frames), transcendentals=0,
            bytes_accessed=plane.size * 8,
        ),
    )(plane, low_t)
    tile_spec = pl.BlockSpec((frames, nb // 128, 128), lambda i: (0, i, 0))
    return pl.pallas_call(
        functools.partial(post_kernel, cut=SOFT_CUT),
        out_shape=jax.ShapeDtypeStruct((frames, width // 128, 128), jnp.bfloat16),
        grid=(width // nb,),
        in_specs=[lane_spec] * 4 + [whole2(low_t.shape), whole2(filter_t.shape)],
        out_specs=tile_spec,
        compiler_params=params,
        cost_estimate=pl.CostEstimate(
            flops=2 * width * frames * (2 * frames) * 5, transcendentals=width * frames,
            bytes_accessed=plane.size * 12,
        ),
    )(low, rem, before, after, low_t, filter_t)


def solve_kernel(a_ref, x0_ref, s_ref, out_ref, *, steps):
    size = a_ref.shape[0]
    rows = lax.broadcasted_iota(jnp.int32, (size, size), 0)
    cols = lax.broadcasted_iota(jnp.int32, (size, size), 1)
    twice = jnp.where(rows == cols, 2.0, 0.0).astype(jnp.float32)
    a = a_ref[...]
    high = lax.Precision.HIGHEST

    def step(i, x):
        t = jnp.dot(a, x, precision=high, preferred_element_type=jnp.float32)
        return jnp.dot(x, twice - t, precision=high, preferred_element_type=jnp.float32)

    x = x0_ref[...]
    for i in range(steps):
        x = step(i, x)
    out_ref[...] = jnp.dot(x, s_ref[...], precision=high, preferred_element_type=jnp.float32)


def shrink_of(stacked, threshold_sq, rank_value):
    size = stacked.shape[0]
    unit_matrix = jnp.eye(size, dtype=jnp.float32)
    system = stacked + threshold_sq * unit_matrix
    start = unit_matrix * (2.0 / (threshold_sq * (2.0 + rank_value)))
    whole = pl.BlockSpec(memory_space=pltpu.VMEM)
    return pl.pallas_call(
        functools.partial(solve_kernel, steps=9),
        out_shape=jax.ShapeDtypeStruct((size, size), jnp.float32),
        in_specs=[whole, whole, whole],
        out_specs=whole,
    )(system, start, stacked)


def apply_frames(mix_real, mix_imag, field_values):
    direct = jnp.einsum("fg,zftw->zgtw", mix_real, field_values, preferred_element_type=jnp.float32)
    turned = jnp.einsum(
        "fg,zftw->zgtw", mix_imag, rotate(field_values), preferred_element_type=jnp.float32
    )
    return direct + turned


def soft_shrink(filtered):
    half_width = filtered.shape[-1] // 2
    real_part, imag_part = (filtered[..., :half_width], filtered[..., half_width:])
    magnitude = jnp.sqrt(real_part * real_part + imag_part * imag_part)
    scale_values = jnp.maximum(magnitude - SOFT_CUT, 0.0) / jnp.maximum(magnitude, SOFT_CUT)
    return filtered * jnp.concatenate([scale_values, scale_values], axis=-1)


def tree_sum(value, axis):
    count = lax.axis_size(axis)
    if count & (count - 1):
        return lax.psum(value, axis)
    step = 1
    while step < count:
        pairs = [(i, i ^ step) for i in range(count)]
        value = value + lax.ppermute(value, axis, pairs)
        step *= 2
    return value


def mix_frames(weights, field_values):
    half = weights.shape[1] // 2
    mixed = jnp.einsum("kh,ktw->htw", weights, field_values, preferred_element_type=jnp.float32)
    return mixed[:half] + rotate(mixed[half:])


def local(image, adjoint_data, coil_maps, spoke_counts, tile_map, blocks, z_kernel, rank_cap):
    frame_count = image.shape[1]
    fresh = fresh_image_of(
        image[0], adjoint_data[0], coil_maps[0], spoke_counts[0], tile_map[0], blocks
    )
    count = lax.axis_size("dom")
    forward = [(i, i + 1) for i in range(count - 1)]
    backward = [(target, source) for source, target in forward]
    flat = fresh.reshape(frame_count, -1)
    rows_real = flat
    rows_turned = rotate(fresh).reshape(frame_count, -1)
    gram_real = jnp.einsum("fn,gn->fg", rows_real, rows_real, preferred_element_type=jnp.float32)
    gram_imag = jnp.einsum("fn,gn->fg", rows_turned, rows_real, preferred_element_type=jnp.float32)
    gram_real, gram_imag = tree_sum(jnp.stack([gram_real, gram_imag]), "dom")
    flat, gram_real, gram_imag = lax.optimization_barrier((flat, gram_real, gram_imag))
    fresh_before = lax.ppermute(flat, "dom", forward)
    fresh_after = lax.ppermute(flat, "dom", backward)
    stacked = jnp.block([[gram_real, -gram_imag], [gram_imag, gram_real]])
    rank_value = rank_cap[0].astype(jnp.float32)
    threshold_sq = jnp.trace(gram_real) / rank_value
    shrink = shrink_of(stacked, threshold_sq, rank_value)
    shrink_real = shrink[:frame_count, :frame_count].astype(jnp.bfloat16)
    shrink_imag = shrink[frame_count:, :frame_count].astype(jnp.bfloat16)
    low_t = jnp.concatenate([shrink_real, shrink_imag], axis=1).T
    taps = z_kernel.shape[0]
    filter_weights = jnp.concatenate([z_kernel[:, 0], z_kernel[:, 1]], axis=-1)
    filter_t = filter_weights.reshape(taps * frame_count, 2 * frame_count).T
    out = post_of(flat, fresh_before, fresh_after, low_t, filter_t)
    return out.reshape(image.shape)


def solution(mesh):
    return jax.shard_map(
        local,
        mesh=mesh,
        in_specs=(
            P(("groups", "dom"), None, None, None),
            P(("groups", "dom"), None, None, None),
            P(("groups", "dom"), None, None, None),
            P(("groups", "dom"), None),
            P(("groups", "dom"), None, None, None, None),
            P(),
            P(),
            P(),
        ),
        out_specs=P(("groups", "dom"), None, None, None),
        check_vma=False,
    )
```
